512 devices in a mesh: tm: 16 (over z_hi, y), space: 32 (over z_lo, x, core).
Axes of the slice: x: 4, y: 4, z: 16 (z_hi: 4, z_lo: 4; z = z_hi * 4 + z_lo), core: 2. Of those that a mesh axis runs over, the one named last changes fastest.
Arguments:
- queries: bfloat16 [128, 2048, 256], P('tm', 'space'), as said below
- keys: bfloat16 [128, 2048, 256], P('tm', 'space'), as said below
- label_values: bfloat16 [128, 2048, 64], P('tm', 'space'), may hold values from -6 to 6
- class_ids: int32 [128, 2048], P(None, 'space'), may hold values from 0 to 63
- valid_pixels: int32 [128], replicated, may hold values from 1024 to 2048
- keyframe_index: int32 [2, 2], replicated, may hold values from 0 to 127, as said below
Outputs:
- readout: bfloat16 [128, 2048, 64], P('tm', 'space')
- confidence: float32 [2, 2, 2048], P(None, None, 'space')
The draws below stay inside these ranges and needn't reach their ends.
Inputs may be any that keep to these rules, and one draw needn't show every extreme that they name: `queries`: queries and keys are real-valued embeddings. `keys`: Real-valued embeddings. `keyframe_index`: all 4 entries are different frames.
All inputs are finite; a program needn't handle non-finite values.
Results may differ from the reference program's by a relative error of at most 0.0053.
Values may be sent and summed in bfloat16 or wider, within the bound.
No kernel may reach another device: no remote copies, remote signals or barrier semaphores. Data moves between devices by JAX's collectives and lax.ppermute only.
A program may use at most 192 MiB of HBM per device.

```python
import math
import jax
import jax.numpy as jnp
import numpy as np
from jax import lax

D = 256
VAL = 64
KEYS_N = 2
STEPS = 2
FRAMES = 128
PIX = 2048


def shared_keys(key):
    base = jax.random.truncated_normal(jax.random.fold_in(key, 11), -6.0, 6.0, (FRAMES, PIX, D), jnp.float32)
    return base


def draw_keys(key, part):
    return shared_keys(key).astype(jnp.bfloat16)


def draw_queries(key, part):
    base = jax.random.truncated_normal(jax.random.fold_in(key, 23), -6.0, 6.0, (FRAMES, PIX, D), jnp.float32)
    return base.astype(jnp.bfloat16)


def draw_valid_pixels(key, part):
    lengths = jax.random.randint(jax.random.fold_in(key, 3), (FRAMES,), PIX // 2, PIX + 1, jnp.int32)
    spots = jax.random.permutation(jax.random.fold_in(key, 4), FRAMES)
    lengths = lengths.at[spots[0]].set(PIX)
    lengths = lengths.at[spots[1]].set(PIX // 2)
    return lengths.astype(jnp.int32)


def draw_keyframe_index(key, part):
    total = STEPS * KEYS_N
    middle = jax.random.permutation(jax.random.fold_in(key, 5), FRAMES - 2)[:total - 2].astype(jnp.int32) + 1
    chosen = jnp.concatenate([jnp.array([0, FRAMES - 1], jnp.int32), middle])
    order = jax.random.permutation(jax.random.fold_in(key, 7), total)
    return chosen[order].reshape(STEPS, KEYS_N).astype(jnp.int32)


def with_ends(drawn, stream_key, low, largest):
    dims = drawn.shape
    index_at = [jax.random.randint(jax.random.fold_in(stream_key, axis), (), 0, dims[axis]) for axis in range(len(dims))]
    drawn = drawn.at[tuple(index_at)].set(low)
    longest = dims.index(max(dims))
    index_at[longest] = (index_at[longest] + 1) % dims[longest]
    return drawn.at[tuple(index_at)].set(largest)


def steps_of(stream_key, shape, cuts, low, largest):
    def one(position, parts):
        heights = jax.random.uniform(jax.random.fold_in(jax.random.fold_in(stream_key, 6), position), (parts,), jnp.float32, low / len(cuts), largest / len(cuts))
        return jnp.repeat(jnp.exp(heights), shape[position] // parts).reshape((-1,) + (1,) * (len(shape) - position - 1))

    loudness = one(*cuts[0])
    for cut in cuts[1:]:
        loudness = loudness * one(*cut)
    return loudness


def cumulative_ranks(amount, lean):
    weights = [(1 << 20) // math.isqrt(rank ** lean) + 1 for rank in range(1, amount + 1)]
    scale = 1 + sum(weights) // (1 << 30)
    return np.cumsum(np.array([max(1, weight // scale) for weight in weights]))


def ranked(rng, extent, amount, slope):
    grid = cumulative_ranks(amount, slope)
    pick = jax.random.randint(jax.random.fold_in(rng, 1), extent, 0, int(grid[amount - 1]))
    rank = jnp.searchsorted(jnp.asarray(grid, jnp.int32), pick, side="right")
    return jax.random.permutation(jax.random.fold_in(rng, 2), amount)[rank].astype(jnp.int32)


def normal_values(own_key, extent, width, reach, shards=(), held_as=jnp.bfloat16):
    result = jax.random.normal(own_key, extent, jnp.float32) * width
    if len(shards) > 0:
        result = steps_of(own_key, extent, shards, -0.22, 0.18) * result
    return jnp.clip(result, min=-reach, max=reach).astype(held_as)


def setup_inputs(seed: int = 0) -> dict:
    key_list = jax.random.split(jax.random.key(seed), 7)
    return {
        "queries": draw_queries(jax.random.fold_in(key_list[6], 71), 0),
        "keys": draw_keys(jax.random.fold_in(key_list[6], 71), 0),
        "label_values": normal_values(key_list[2], (FRAMES, PIX, VAL), 1.0, 6.0, ((0, 16), (1, 32))),
        "class_ids": with_ends(ranked(key_list[3], (FRAMES, PIX), VAL, 1), jax.random.fold_in(key_list[3], 3), 0, VAL - 1).astype(jnp.int32),
        "valid_pixels": draw_valid_pixels(jax.random.fold_in(key_list[6], 71), 0),
        "keyframe_index": draw_keyframe_index(jax.random.fold_in(key_list[6], 71), 0),
    }


def step_pass(queries, memory_keys, memory_values, memory_ids, memory_valid, valid_pixels):
    scale = 3.0 / math.sqrt(D)
    width_mem = KEYS_N * PIX
    onehot = (memory_ids[None, :] == jnp.arange(VAL, dtype=jnp.int32)[:, None]).astype(jnp.bfloat16)

    def frame(carry, inputs):
        query, length = inputs
        col_max, col_total, col_num = carry
        row_valid = jnp.arange(PIX, dtype=jnp.int32) < length
        scores = jnp.dot(query, memory_keys.T, preferred_element_type=jnp.float32) * scale
        masked = jnp.where(memory_valid[None, :], scores, -1e+30)
        row_max = lax.optimization_barrier(jnp.max(masked, axis=1, keepdims=True))
        weights = jnp.where(memory_valid[None, :], jnp.exp(scores - row_max), 0.0)
        total = lax.optimization_barrier(jnp.sum(weights, axis=1, keepdims=True))
        mixed = jnp.dot(weights.astype(jnp.bfloat16), memory_values, preferred_element_type=jnp.float32) / total
        readout = jnp.where(row_valid[:, None], mixed, 0.0).astype(jnp.bfloat16)
        picked = jnp.dot(readout, onehot, preferred_element_type=jnp.float32)
        local_max = lax.optimization_barrier(jnp.max(jnp.where(row_valid[:, None], scores, -1e+30), axis=0))
        new_max = jnp.maximum(col_max, local_max)
        expo = jnp.where(row_valid[:, None], jnp.exp(scores - new_max[None, :]), 0.0)
        keep = jnp.exp(col_max - new_max)
        col_total = col_total * keep + lax.optimization_barrier(jnp.sum(expo, axis=0))
        col_num = col_num * keep + lax.optimization_barrier(jnp.sum(expo * picked, axis=0))
        return ((new_max, col_total, col_num), readout)
    init = (jnp.full((width_mem,), -1e+30, jnp.float32), jnp.zeros((width_mem,), jnp.float32), jnp.zeros((width_mem,), jnp.float32))
    (col_max, col_total, col_num), readout = lax.scan(frame, init, (queries, valid_pixels))
    hits = (memory_ids[None, :] == jnp.arange(VAL, dtype=jnp.int32)[:, None]) & memory_valid[None, :]
    counts = lax.optimization_barrier(jnp.sum(hits.astype(jnp.int32), axis=1))
    all_count = jnp.sum(counts)
    own = lax.optimization_barrier(jnp.sum(jnp.where(memory_ids[None, :] == jnp.arange(VAL, dtype=jnp.int32)[:, None], counts[:, None], 0), axis=0))
    own_safe = jnp.where(memory_valid, own, 1)
    factor = jnp.sqrt(all_count.astype(jnp.float32) / (VAL * own_safe.astype(jnp.float32)))
    confidence = jnp.where(memory_valid, col_num / col_total * factor, 0.0)
    return (readout, confidence)

def reference(queries, keys, label_values, class_ids, valid_pixels, keyframe_index):
    current = label_values
    confidences = []
    readout = label_values
    for step in range(STEPS):
        chosen = keyframe_index[step]
        memory_keys = keys[chosen].reshape(KEYS_N * PIX, D)
        memory_values = current[chosen].reshape(KEYS_N * PIX, VAL)
        memory_ids = class_ids[chosen].reshape(KEYS_N * PIX)
        memory_valid = (jnp.arange(PIX, dtype=jnp.int32)[None, :] < valid_pixels[chosen][:, None]).reshape(KEYS_N * PIX)
        readout, confidence = step_pass(queries, memory_keys, memory_values, memory_ids, memory_valid, valid_pixels)
        current = readout
        confidences.append(confidence.reshape(KEYS_N, PIX))
    return (readout, jnp.stack(confidences))
```

```python
import math

import jax
import jax.numpy as jnp
from jax import lax
from jax.sharding import PartitionSpec as P

LOWEST = -1e30


def broadcast_tm(values, owners, axis):
    size = lax.axis_size(axis)
    me = lax.axis_index(axis)
    rounds = size.bit_length() - 1
    assert (1 << rounds) == size
    for r in range(rounds):
        bit = 1 << r
        pairs = [(i, i ^ bit) for i in range(size)]
        received = lax.ppermute(values, axis, pairs)
        out = []
        for value, owner, got in zip(values, owners, received):
            take = ((me ^ owner) >> r) == 1
            take = take.reshape(take.shape + (1,) * (value.ndim - take.ndim))
            out.append(jnp.where(take, got, value))
        values = tuple(out)
    return values


def merge_stats(col_max, col_total, col_num, axis):
    top = jnp.max(col_max, axis=axis, keepdims=True)
    keep = jnp.exp(col_max - top)
    total = jnp.sum(col_total * keep, axis=axis)
    num = jnp.sum(col_num * keep, axis=axis)
    return jnp.squeeze(top, axis), total, num


def body(queries, keys, label_values, class_ids, valid_pixels, keyframe_index):
    fr_dev, pix_dev, width = queries.shape
    channels = label_values.shape[2]
    total_steps, keyframes = keyframe_index.shape
    n_space = lax.axis_size("space")
    pix_all = pix_dev * n_space
    mem_width = keyframes * pix_all
    time_pos = lax.axis_index("tm")
    space_pos = lax.axis_index("space")
    rows = fr_dev * pix_dev
    scale = 3.0 / math.sqrt(width)
    class_range = jnp.arange(channels, dtype=jnp.int32)

    frame_valid = lax.dynamic_slice_in_dim(valid_pixels, time_pos * fr_dev, fr_dev)
    pixel_ids = space_pos * pix_dev + jnp.arange(pix_dev, dtype=jnp.int32)
    row_valid = (pixel_ids[None, :] < frame_valid[:, None]).reshape(rows)
    query_rows = queries.reshape(rows, width)

    flat_kf = keyframe_index.reshape(-1)
    owners = flat_kf // fr_dev
    slots = flat_kf % fr_dev
    later = keyframes * (total_steps - 1)

    kf_keys = jnp.take(keys, slots, axis=0)
    kf_values = jnp.take(label_values, slots[:keyframes], axis=0)
    kf_queries = jnp.take(queries, slots[keyframes:], axis=0)
    kf_keys, kf_values, kf_queries = broadcast_tm(
        (kf_keys, kf_values, kf_queries),
        (owners, owners[:keyframes], owners[keyframes:]),
        "tm",
    )

    kf_ids = jnp.take(class_ids, flat_kf, axis=0).astype(jnp.bfloat16)
    kf_ids = kf_ids.reshape(total_steps, keyframes, pix_dev).transpose(1, 2, 0)
    step_keys = kf_keys.reshape(total_steps, keyframes, pix_dev, width)
    packed = jnp.concatenate(
        [step_keys[s] for s in range(total_steps)] + [kf_values, kf_ids], axis=2
    )
    gathered = lax.all_gather(packed, "space", axis=1, tiled=True)
    mem_keys = [
        gathered[:, :, s * width:(s + 1) * width].reshape(mem_width, width)
        for s in range(total_steps)
    ]
    base = total_steps * width
    mem_values = gathered[:, :, base:base + channels].reshape(mem_width, channels)
    mem_ids = [
        gathered[:, :, base + channels + s].reshape(mem_width).astype(jnp.int32)
        for s in range(total_steps)
    ]

    extra_queries = kf_queries.reshape(later, pix_dev, width)
    extra_valid = pixel_ids[None, :] < jnp.take(valid_pixels, flat_kf[keyframes:])[:, None]

    stats = []
    readout = None
    for step in range(total_steps):
        chosen = keyframe_index[step]
        key_valid = (
            jnp.arange(pix_all, dtype=jnp.int32)[None, :]
            < jnp.take(valid_pixels, chosen)[:, None]
        ).reshape(mem_width)
        ids = mem_ids[step]
        onehot_t = (ids[None, :] == class_range[:, None]).astype(jnp.bfloat16)
        if step + 1 < total_steps:
            extra = extra_queries[step * keyframes:(step + 1) * keyframes].reshape(-1, width)
            extra_ok = extra_valid[step * keyframes:(step + 1) * keyframes].reshape(-1)
            q = jnp.concatenate([query_rows, extra], axis=0)
            q_valid = jnp.concatenate([row_valid, extra_ok], axis=0)
        else:
            q = query_rows
            q_valid = row_valid
        scores = lax.dot_general(
            q, mem_keys[step], (((1,), (1,)), ((), ())), preferred_element_type=jnp.float32
        ) * scale
        masked = jnp.where(key_valid[None, :], scores, LOWEST)
        row_max = jnp.max(masked, axis=1, keepdims=True)
        weights = jnp.where(key_valid[None, :], jnp.exp(scores - row_max), 0.0)
        total = jnp.sum(weights, axis=1, keepdims=True)
        mixed = (
            jnp.dot(weights.astype(jnp.bfloat16), mem_values, preferred_element_type=jnp.float32)
            / total
        )
        out = jnp.where(q_valid[:, None], mixed, 0.0).astype(jnp.bfloat16)
        readout = out[:rows]
        own_scores = scores[:rows]
        picked = jnp.dot(readout, onehot_t, preferred_element_type=jnp.float32)
        col_max = jnp.max(jnp.where(row_valid[:, None], own_scores, LOWEST), axis=0)
        expo = jnp.where(row_valid[:, None], jnp.exp(own_scores - col_max[None, :]), 0.0)
        col_total = jnp.sum(expo, axis=0)
        col_num = jnp.sum(expo * picked, axis=0)
        stats.append(jnp.stack([col_max, col_total, col_num]))
        if step + 1 < total_steps:
            part = out[rows:].reshape(keyframes, pix_dev, channels)
            mem_values = lax.all_gather(part, "space", axis=1, tiled=True).reshape(
                mem_width, channels
            )

    local = jnp.stack(stats).reshape(total_steps, 3, keyframes, n_space, pix_dev)
    local = local.transpose(3, 1, 0, 2, 4)
    spread = lax.all_to_all(local, "space", 0, 0, tiled=True)
    m, t, n = merge_stats(spread[:, 0], spread[:, 1], spread[:, 2], 0)
    joined = lax.all_gather(jnp.stack([m, t, n]), "tm", axis=0, tiled=False)
    m, col_total, col_num = merge_stats(joined[:, 0], joined[:, 1], joined[:, 2], 0)

    confidences = []
    for step in range(total_steps):
        chosen = keyframe_index[step]
        key_valid = (
            jnp.arange(pix_all, dtype=jnp.int32)[None, :]
            < jnp.take(valid_pixels, chosen)[:, None]
        ).reshape(mem_width)
        class_match = mem_ids[step][None, :] == class_range[:, None]
        hits = (class_match & key_valid[None, :]).astype(jnp.int32)
        counts = jnp.sum(hits, axis=1)
        all_count = jnp.sum(counts)
        own_ids = lax.dynamic_slice_in_dim(
            mem_ids[step].reshape(keyframes, pix_all), space_pos * pix_dev, pix_dev, 1
        )
        own_valid = pixel_ids[None, :] < jnp.take(valid_pixels, chosen)[:, None]
        own = jnp.take(counts, own_ids)
        own_safe = jnp.where(own_valid, own, 1)
        factor = jnp.sqrt(all_count.astype(jnp.float32) / (channels * own_safe.astype(jnp.float32)))
        conf = jnp.where(own_valid, col_num[step] / col_total[step] * factor, 0.0)
        confidences.append(conf)
    return (readout.reshape(fr_dev, pix_dev, channels), jnp.stack(confidences))


def solution(mesh):
    placed = (
        P("tm", "space", None),
        P("tm", "space", None),
        P("tm", "space", None),
        P(None, "space"),
        P(),
        P(),
    )
    return jax.shard_map(
        body,
        mesh=mesh,
        in_specs=placed,
        out_specs=(P("tm", "space", None), P(None, None, "space")),
        check_vma=False,
    )
```

```python
import math

import jax
import jax.numpy as jnp
from jax import lax
from jax.sharding import PartitionSpec as P

LOWEST = -1e30


def broadcast_tm(value, owner, axis):
    size = lax.axis_size(axis)
    me = lax.axis_index(axis)
    rounds = size.bit_length() - 1
    assert (1 << rounds) == size
    for r in range(rounds):
        bit = 1 << r
        pairs = [(i, i ^ bit) for i in range(size)]
        got = lax.ppermute(value, axis, pairs)
        take = ((me ^ owner) >> r) == 1
        value = jnp.where(take[:, None], got, value)
    return value


def gather_all(value, axis):
    size = lax.axis_size(axis)
    spread = jnp.broadcast_to(value[None], (size,) + value.shape)
    return lax.all_to_all(spread, axis, 0, 0, tiled=True)


def merge_stats(col_max, col_total, col_num, axis):
    top = jnp.max(col_max, axis=axis, keepdims=True)
    keep = jnp.exp(col_max - top)
    total = jnp.sum(col_total * keep, axis=axis)
    num = jnp.sum(col_num * keep, axis=axis)
    return jnp.squeeze(top, axis), total, num


def body(queries, keys, label_values, class_ids, valid_pixels, keyframe_index):
    fr_dev, pix_dev, width = queries.shape
    channels = label_values.shape[2]
    total_steps, keyframes = keyframe_index.shape
    n_space = lax.axis_size("space")
    pix_all = pix_dev * n_space
    mem_width = keyframes * pix_all
    time_pos = lax.axis_index("tm")
    space_pos = lax.axis_index("space")
    rows = fr_dev * pix_dev
    scale = 3.0 / math.sqrt(width)
    class_range = jnp.arange(channels, dtype=jnp.int32)

    frame_valid = lax.dynamic_slice_in_dim(valid_pixels, time_pos * fr_dev, fr_dev)
    pixel_ids = space_pos * pix_dev + jnp.arange(pix_dev, dtype=jnp.int32)
    row_valid = (pixel_ids[None, :] < frame_valid[:, None]).reshape(rows)
    query_rows = queries.reshape(rows, width)

    flat_kf = keyframe_index.reshape(-1)
    owners = flat_kf // fr_dev
    slots = flat_kf % fr_dev
    later = keyframes * (total_steps - 1)

    kf_keys = jnp.take(keys, slots, axis=0)
    kf_values = jnp.take(label_values, slots[:keyframes], axis=0)
    kf_queries = jnp.take(queries, slots[keyframes:], axis=0)
    parts = [kf_keys, kf_queries, kf_values]
    part_owners = [owners, owners[keyframes:], owners[:keyframes]]
    flat = jnp.concatenate([p.reshape(-1, width) for p in parts], axis=0)
    row_owner = jnp.concatenate(
        [jnp.repeat(o, p[0].size // width) for p, o in zip(parts, part_owners)]
    )
    flat = broadcast_tm(flat, row_owner, "tm")
    sizes = [p.size // width for p in parts]
    kf_keys = flat[:sizes[0]].reshape(kf_keys.shape)
    kf_queries = flat[sizes[0]:sizes[0] + sizes[1]].reshape(kf_queries.shape)
    kf_values = flat[sizes[0] + sizes[1]:].reshape(kf_values.shape)

    kf_ids = jnp.take(class_ids, flat_kf, axis=0).astype(jnp.bfloat16)
    kf_ids = kf_ids.reshape(total_steps, keyframes, pix_dev).transpose(1, 2, 0)
    step_keys = kf_keys.reshape(total_steps, keyframes, pix_dev, width)
    packed = jnp.concatenate(
        [step_keys[s] for s in range(total_steps)] + [kf_values, kf_ids], axis=2
    )
    gathered = lax.all_gather(packed, "space", axis=1, tiled=True)
    mem_keys = [
        gathered[:, :, s * width:(s + 1) * width].reshape(mem_width, width)
        for s in range(total_steps)
    ]
    base = total_steps * width
    mem_values = gathered[:, :, base:base + channels].reshape(mem_width, channels)
    mem_ids = [
        gathered[:, :, base + channels + s].reshape(mem_width).astype(jnp.int32)
        for s in range(total_steps)
    ]

    extra_queries = kf_queries.reshape(later, pix_dev, width)
    extra_valid = pixel_ids[None, :] < jnp.take(valid_pixels, flat_kf[keyframes:])[:, None]

    stats = []
    readout = None
    for step in range(total_steps):
        chosen = keyframe_index[step]
        key_valid = (
            jnp.arange(pix_all, dtype=jnp.int32)[None, :]
            < jnp.take(valid_pixels, chosen)[:, None]
        ).reshape(mem_width)
        ids = mem_ids[step]
        onehot_t = (ids[None, :] == class_range[:, None]).astype(jnp.bfloat16)
        if step + 1 < total_steps:
            extra = extra_queries[step * keyframes:(step + 1) * keyframes].reshape(-1, width)
            extra_ok = extra_valid[step * keyframes:(step + 1) * keyframes].reshape(-1)
            q = jnp.concatenate([query_rows, extra], axis=0)
            q_valid = jnp.concatenate([row_valid, extra_ok], axis=0)
        else:
            q = query_rows
            q_valid = row_valid
        scores = lax.dot_general(
            q, mem_keys[step], (((1,), (1,)), ((), ())), preferred_element_type=jnp.float32
        ) * scale
        masked = jnp.where(key_valid[None, :], scores, LOWEST)
        row_max = jnp.max(masked, axis=1, keepdims=True)
        weights = jnp.where(key_valid[None, :], jnp.exp(scores - row_max), 0.0)
        total = jnp.sum(weights, axis=1, keepdims=True)
        mixed = (
            jnp.dot(weights.astype(jnp.bfloat16), mem_values, preferred_element_type=jnp.float32)
            / total
        )
        out = jnp.where(q_valid[:, None], mixed, 0.0).astype(jnp.bfloat16)
        readout = out[:rows]
        own_scores = scores[:rows]
        picked = jnp.dot(readout, onehot_t, preferred_element_type=jnp.float32)
        col_max = jnp.max(jnp.where(row_valid[:, None], own_scores, LOWEST), axis=0)
        expo = jnp.where(row_valid[:, None], jnp.exp(own_scores - col_max[None, :]), 0.0)
        col_total = jnp.sum(expo, axis=0)
        col_num = jnp.sum(expo * picked, axis=0)
        stats.append(jnp.stack([col_max, col_total, col_num]))
        if step + 1 < total_steps:
            part = out[rows:].reshape(keyframes, pix_dev, channels)
            mem_values = gather_all(part, "space").transpose(1, 0, 2, 3).reshape(
                mem_width, channels
            )

    local = jnp.stack(stats).reshape(total_steps, 3, keyframes, n_space, pix_dev)
    local = local.transpose(3, 1, 0, 2, 4)
    spread = lax.all_to_all(local, "space", 0, 0, tiled=True)
    m, t, n = merge_stats(spread[:, 0], spread[:, 1], spread[:, 2], 0)
    joined = gather_all(jnp.stack([m, t, n]), "tm")
    m, col_total, col_num = merge_stats(joined[:, 0], joined[:, 1], joined[:, 2], 0)

    confidences = []
    for step in range(total_steps):
        chosen = keyframe_index[step]
        key_valid = (
            jnp.arange(pix_all, dtype=jnp.int32)[None, :]
            < jnp.take(valid_pixels, chosen)[:, None]
        ).reshape(mem_width)
        class_match = mem_ids[step][None, :] == class_range[:, None]
        hits = (class_match & key_valid[None, :]).astype(jnp.int32)
        counts = jnp.sum(hits, axis=1)
        all_count = jnp.sum(counts)
        own_ids = lax.dynamic_slice_in_dim(
            mem_ids[step].reshape(keyframes, pix_all), space_pos * pix_dev, pix_dev, 1
        )
        own_valid = pixel_ids[None, :] < jnp.take(valid_pixels, chosen)[:, None]
        own = jnp.take(counts, own_ids)
        own_safe = jnp.where(own_valid, own, 1)
        factor = jnp.sqrt(all_count.astype(jnp.float32) / (channels * own_safe.astype(jnp.float32)))
        conf = jnp.where(own_valid, col_num[step] / col_total[step] * factor, 0.0)
        confidences.append(conf)
    return (readout.reshape(fr_dev, pix_dev, channels), jnp.stack(confidences))


def solution(mesh):
    placed = (
        P("tm", "space", None),
        P("tm", "space", None),
        P("tm", "space", None),
        P(None, "space"),
        P(),
        P(),
    )
    return jax.shard_map(
        body,
        mesh=mesh,
        in_specs=placed,
        out_specs=(P("tm", "space", None), P(None, None, "space")),
        check_vma=False,
    )
```

```python
import math

import jax
import jax.numpy as jnp
from jax import lax
from jax.sharding import PartitionSpec as P

LOWEST = -1e30
NEAR_TM = 4


def broadcast_tm(value, owner, axis, inner):
    size = lax.axis_size(axis)
    me = lax.axis_index(axis)
    rounds = inner.bit_length() - 1
    assert (1 << rounds) == inner and size % inner == 0
    for r in range(rounds):
        bit = 1 << r
        pairs = [(i, i ^ bit) for i in range(size)]
        got = lax.ppermute(value, axis, pairs)
        take = ((me ^ owner) % inner >> r) == 1
        value = jnp.where(take[:, None], got, value)
    groups = size // inner
    rel = (me // inner - owner // inner) % groups
    ahead = [(i, (i + inner) % size) for i in range(size)]
    behind = [(i, (i - inner) % size) for i in range(size)]
    half = value.shape[0] // 2
    for k in range(1, groups // 2 + 1):
        if 2 * k == groups:
            got_a = lax.ppermute(value[:half], axis, ahead)
            got_b = lax.ppermute(value[half:], axis, behind)
            got = jnp.concatenate([got_a, got_b], axis=0)
            value = jnp.where((rel == k)[:, None], got, value)
        else:
            got_a = lax.ppermute(value, axis, ahead)
            got_b = lax.ppermute(value, axis, behind)
            value = jnp.where((rel == k)[:, None], got_a, value)
            value = jnp.where((rel == groups - k)[:, None], got_b, value)
    return value


def gather_all(value, axis):
    size = lax.axis_size(axis)
    spread = jnp.broadcast_to(value[None], (size,) + value.shape)
    return lax.all_to_all(spread, axis, 0, 0, tiled=True)


def merge_stats(col_max, col_total, col_num, axis):
    top = jnp.max(col_max, axis=axis, keepdims=True)
    keep = jnp.exp(col_max - top)
    total = jnp.sum(col_total * keep, axis=axis)
    num = jnp.sum(col_num * keep, axis=axis)
    return jnp.squeeze(top, axis), total, num


def body(queries, keys, label_values, class_ids, valid_pixels, keyframe_index):
    fr_dev, pix_dev, width = queries.shape
    channels = label_values.shape[2]
    total_steps, keyframes = keyframe_index.shape
    n_space = lax.axis_size("space")
    pix_all = pix_dev * n_space
    mem_width = keyframes * pix_all
    time_pos = lax.axis_index("tm")
    space_pos = lax.axis_index("space")
    rows = fr_dev * pix_dev
    scale = 3.0 / math.sqrt(width)
    class_range = jnp.arange(channels, dtype=jnp.int32)

    frame_valid = lax.dynamic_slice_in_dim(valid_pixels, time_pos * fr_dev, fr_dev)
    pixel_ids = space_pos * pix_dev + jnp.arange(pix_dev, dtype=jnp.int32)
    row_valid = (pixel_ids[None, :] < frame_valid[:, None]).reshape(rows)
    query_rows = queries.reshape(rows, width)

    flat_kf = keyframe_index.reshape(-1)
    owners = flat_kf // fr_dev
    slots = flat_kf % fr_dev
    later = keyframes * (total_steps - 1)

    kf_keys = jnp.take(keys, slots, axis=0)
    kf_values = jnp.take(label_values, slots[:keyframes], axis=0)
    kf_queries = jnp.take(queries, slots[keyframes:], axis=0)
    parts = [kf_keys, kf_queries, kf_values]
    part_owners = [owners, owners[keyframes:], owners[:keyframes]]
    flat = jnp.concatenate([p.reshape(-1, width) for p in parts], axis=0)
    row_owner = jnp.concatenate(
        [jnp.repeat(o, p[0].size // width) for p, o in zip(parts, part_owners)]
    )
    flat = broadcast_tm(flat, row_owner, "tm", NEAR_TM)
    sizes = [p.size // width for p in parts]
    kf_keys = flat[:sizes[0]].reshape(kf_keys.shape)
    kf_queries = flat[sizes[0]:sizes[0] + sizes[1]].reshape(kf_queries.shape)
    kf_values = flat[sizes[0] + sizes[1]:].reshape(kf_values.shape)

    kf_ids = jnp.take(class_ids, flat_kf, axis=0).astype(jnp.bfloat16)
    kf_ids = kf_ids.reshape(total_steps, keyframes, pix_dev).transpose(1, 2, 0)
    step_keys = kf_keys.reshape(total_steps, keyframes, pix_dev, width)
    packed = jnp.concatenate([step_keys[0], kf_values, kf_ids], axis=2)
    gathered = lax.all_gather(packed, "space", axis=1, tiled=True)
    mem_keys = [gathered[:, :, :width].reshape(mem_width, width)]
    mem_values = gathered[:, :, width:width + channels].reshape(mem_width, channels)
    mem_ids = [
        gathered[:, :, width + channels + s].reshape(mem_width).astype(jnp.int32)
        for s in range(total_steps)
    ]
    rest_keys, unused = lax.optimization_barrier((step_keys[1:], gathered))
    rest_keys = lax.all_gather(rest_keys, "space", axis=2, tiled=True)
    mem_keys += [rest_keys[s].reshape(mem_width, width) for s in range(total_steps - 1)]

    extra_queries = kf_queries.reshape(later, pix_dev, width)
    extra_valid = pixel_ids[None, :] < jnp.take(valid_pixels, flat_kf[keyframes:])[:, None]

    stats = []
    readout = None
    for step in range(total_steps):
        chosen = keyframe_index[step]
        key_valid = (
            jnp.arange(pix_all, dtype=jnp.int32)[None, :]
            < jnp.take(valid_pixels, chosen)[:, None]
        ).reshape(mem_width)
        ids = mem_ids[step]
        onehot_t = (ids[None, :] == class_range[:, None]).astype(jnp.bfloat16)
        if step + 1 < total_steps:
            extra = extra_queries[step * keyframes:(step + 1) * keyframes].reshape(-1, width)
            extra_ok = extra_valid[step * keyframes:(step + 1) * keyframes].reshape(-1)
            q = jnp.concatenate([query_rows, extra], axis=0)
            q_valid = jnp.concatenate([row_valid, extra_ok], axis=0)
        else:
            q = query_rows
            q_valid = row_valid
        scores = lax.dot_general(
            q, mem_keys[step], (((1,), (1,)), ((), ())), preferred_element_type=jnp.float32
        ) * scale
        masked = jnp.where(key_valid[None, :], scores, LOWEST)
        row_max = jnp.max(masked, axis=1, keepdims=True)
        weights = jnp.where(key_valid[None, :], jnp.exp(scores - row_max), 0.0)
        total = jnp.sum(weights, axis=1, keepdims=True)
        mixed = (
            jnp.dot(weights.astype(jnp.bfloat16), mem_values, preferred_element_type=jnp.float32)
            / total
        )
        out = jnp.where(q_valid[:, None], mixed, 0.0).astype(jnp.bfloat16)
        readout = out[:rows]
        own_scores = scores[:rows]
        picked = jnp.dot(readout, onehot_t, preferred_element_type=jnp.float32)
        col_max = jnp.max(jnp.where(row_valid[:, None], own_scores, LOWEST), axis=0)
        expo = jnp.where(row_valid[:, None], jnp.exp(own_scores - col_max[None, :]), 0.0)
        col_total = jnp.sum(expo, axis=0)
        col_num = jnp.sum(expo * picked, axis=0)
        stats.append(jnp.stack([col_max, col_total, col_num]))
        if step + 1 < total_steps:
            part = out[rows:].reshape(keyframes, pix_dev, channels)
            mem_values = gather_all(part, "space").transpose(1, 0, 2, 3).reshape(
                mem_width, channels
            )

    local = jnp.stack(stats).reshape(total_steps, 3, keyframes, n_space, pix_dev)
    local = local.transpose(3, 1, 0, 2, 4)
    spread = lax.all_to_all(local, "space", 0, 0, tiled=True)
    m, t, n = merge_stats(spread[:, 0], spread[:, 1], spread[:, 2], 0)
    joined = gather_all(jnp.stack([m, t, n]), "tm")
    m, col_total, col_num = merge_stats(joined[:, 0], joined[:, 1], joined[:, 2], 0)

    confidences = []
    for step in range(total_steps):
        chosen = keyframe_index[step]
        key_valid = (
            jnp.arange(pix_all, dtype=jnp.int32)[None, :]
            < jnp.take(valid_pixels, chosen)[:, None]
        ).reshape(mem_width)
        class_match = mem_ids[step][None, :] == class_range[:, None]
        hits = (class_match & key_valid[None, :]).astype(jnp.int32)
        counts = jnp.sum(hits, axis=1)
        all_count = jnp.sum(counts)
        own_ids = lax.dynamic_slice_in_dim(
            mem_ids[step].reshape(keyframes, pix_all), space_pos * pix_dev, pix_dev, 1
        )
        own_valid = pixel_ids[None, :] < jnp.take(valid_pixels, chosen)[:, None]
        own = jnp.take(counts, own_ids)
        own_safe = jnp.where(own_valid, own, 1)
        factor = jnp.sqrt(all_count.astype(jnp.float32) / (channels * own_safe.astype(jnp.float32)))
        conf = jnp.where(own_valid, col_num[step] / col_total[step] * factor, 0.0)
        confidences.append(conf)
    return (readout.reshape(fr_dev, pix_dev, channels), jnp.stack(confidences))


def solution(mesh):
    placed = (
        P("tm", "space", None),
        P("tm", "space", None),
        P("tm", "space", None),
        P(None, "space"),
        P(),
        P(),
    )
    return jax.shard_map(
        body,
        mesh=mesh,
        in_specs=placed,
        out_specs=(P("tm", "space", None), P(None, None, "space")),
        check_vma=False,
    )
```

```python
import math

import jax
import jax.numpy as jnp
from jax import lax
from jax.sharding import PartitionSpec as P

LOWEST = -1e30
NEAR_TM = 4


def broadcast_tm(value, owner, axis, inner):
    size = lax.axis_size(axis)
    me = lax.axis_index(axis)
    rounds = inner.bit_length() - 1
    assert (1 << rounds) == inner and size % inner == 0
    for r in range(rounds):
        bit = 1 << r
        pairs = [(i, i ^ bit) for i in range(size)]
        got = lax.ppermute(value, axis, pairs)
        take = ((me ^ owner) % inner >> r) == 1
        value = jnp.where(take[:, None], got, value)
    groups = size // inner
    rel = (me // inner - owner // inner) % groups
    ahead = [(i, (i + inner) % size) for i in range(size)]
    behind = [(i, (i - inner) % size) for i in range(size)]
    half = value.shape[0] // 2
    for k in range(1, groups // 2 + 1):
        if 2 * k == groups:
            got_a = lax.ppermute(value[:half], axis, ahead)
            got_b = lax.ppermute(value[half:], axis, behind)
            got = jnp.concatenate([got_a, got_b], axis=0)
            value = jnp.where((rel == k)[:, None], got, value)
        else:
            got_a = lax.ppermute(value, axis, ahead)
            got_b = lax.ppermute(value, axis, behind)
            value = jnp.where((rel == k)[:, None], got_a, value)
            value = jnp.where((rel == groups - k)[:, None], got_b, value)
    return value


def gather_all(value, axis):
    size = lax.axis_size(axis)
    spread = jnp.broadcast_to(value[None], (size,) + value.shape)
    return lax.all_to_all(spread, axis, 0, 0, tiled=True)


def merge_stats(col_max, col_total, col_num, axis):
    top = jnp.max(col_max, axis=axis, keepdims=True)
    keep = jnp.exp(col_max - top)
    total = jnp.sum(col_total * keep, axis=axis)
    num = jnp.sum(col_num * keep, axis=axis)
    return jnp.squeeze(top, axis), total, num


def body(queries, keys, label_values, class_ids, valid_pixels, keyframe_index):
    fr_dev, pix_dev, width = queries.shape
    channels = label_values.shape[2]
    total_steps, keyframes = keyframe_index.shape
    n_space = lax.axis_size("space")
    pix_all = pix_dev * n_space
    mem_width = keyframes * pix_all
    time_pos = lax.axis_index("tm")
    space_pos = lax.axis_index("space")
    rows = fr_dev * pix_dev
    scale = 3.0 / math.sqrt(width)
    class_range = jnp.arange(channels, dtype=jnp.int32)

    frame_valid = lax.dynamic_slice_in_dim(valid_pixels, time_pos * fr_dev, fr_dev)
    pixel_ids = space_pos * pix_dev + jnp.arange(pix_dev, dtype=jnp.int32)
    row_valid = (pixel_ids[None, :] < frame_valid[:, None]).reshape(rows)
    query_rows = queries.reshape(rows, width)

    flat_kf = keyframe_index.reshape(-1)
    owners = flat_kf // fr_dev
    slots = flat_kf % fr_dev
    later = keyframes * (total_steps - 1)

    kf_keys = jnp.take(keys, slots, axis=0)
    kf_values = jnp.take(label_values, slots[:keyframes], axis=0)
    kf_queries = jnp.take(queries, slots[keyframes:], axis=0)
    parts = [kf_keys, kf_queries, kf_values]
    part_owners = [owners, owners[keyframes:], owners[:keyframes]]
    flat = jnp.concatenate([p.reshape(-1, width) for p in parts], axis=0)
    row_owner = jnp.concatenate(
        [jnp.repeat(o, p[0].size // width) for p, o in zip(parts, part_owners)]
    )
    flat = broadcast_tm(flat, row_owner, "tm", NEAR_TM)
    sizes = [p.size // width for p in parts]
    kf_keys = flat[:sizes[0]].reshape(kf_keys.shape)
    kf_queries = flat[sizes[0]:sizes[0] + sizes[1]].reshape(kf_queries.shape)
    kf_values = flat[sizes[0] + sizes[1]:].reshape(kf_values.shape)

    kf_ids = jnp.take(class_ids, flat_kf, axis=0).astype(jnp.bfloat16)
    kf_ids = kf_ids.reshape(total_steps, keyframes, pix_dev).transpose(1, 2, 0)
    step_keys = kf_keys.reshape(total_steps, keyframes, pix_dev, width)
    packed = jnp.concatenate(
        [step_keys[s] for s in range(total_steps)] + [kf_values, kf_ids], axis=2
    )
    gathered = gather_all(packed, "space").transpose(1, 0, 2, 3)
    gathered = gathered.reshape(keyframes, pix_all, packed.shape[2])
    mem_keys = [
        gathered[:, :, s * width:(s + 1) * width].reshape(mem_width, width)
        for s in range(total_steps)
    ]
    base = total_steps * width
    mem_values = gathered[:, :, base:base + channels].reshape(mem_width, channels)
    mem_ids = [
        gathered[:, :, base + channels + s].reshape(mem_width).astype(jnp.int32)
        for s in range(total_steps)
    ]

    extra_queries = kf_queries.reshape(later, pix_dev, width)
    extra_valid = pixel_ids[None, :] < jnp.take(valid_pixels, flat_kf[keyframes:])[:, None]

    stats = []
    readout = None
    for step in range(total_steps):
        chosen = keyframe_index[step]
        key_valid = (
            jnp.arange(pix_all, dtype=jnp.int32)[None, :]
            < jnp.take(valid_pixels, chosen)[:, None]
        ).reshape(mem_width)
        ids = mem_ids[step]
        onehot_t = (ids[None, :] == class_range[:, None]).astype(jnp.bfloat16)
        if step + 1 < total_steps:
            extra = extra_queries[step * keyframes:(step + 1) * keyframes].reshape(-1, width)
            extra_ok = extra_valid[step * keyframes:(step + 1) * keyframes].reshape(-1)
            q = jnp.concatenate([query_rows, extra], axis=0)
            q_valid = jnp.concatenate([row_valid, extra_ok], axis=0)
        else:
            q = query_rows
            q_valid = row_valid
        scores = lax.dot_general(
            q, mem_keys[step], (((1,), (1,)), ((), ())), preferred_element_type=jnp.float32
        ) * scale
        masked = jnp.where(key_valid[None, :], scores, LOWEST)
        row_max = jnp.max(masked, axis=1, keepdims=True)
        weights = jnp.where(key_valid[None, :], jnp.exp(scores - row_max), 0.0)
        total = jnp.sum(weights, axis=1, keepdims=True)
        mixed = (
            jnp.dot(weights.astype(jnp.bfloat16), mem_values, preferred_element_type=jnp.float32)
            / total
        )
        out = jnp.where(q_valid[:, None], mixed, 0.0).astype(jnp.bfloat16)
        readout = out[:rows]
        own_scores = scores[:rows]
        picked = jnp.dot(readout, onehot_t, preferred_element_type=jnp.float32)
        col_max = jnp.max(jnp.where(row_valid[:, None], own_scores, LOWEST), axis=0)
        expo = jnp.where(row_valid[:, None], jnp.exp(own_scores - col_max[None, :]), 0.0)
        col_total = jnp.sum(expo, axis=0)
        col_num = jnp.sum(expo * picked, axis=0)
        stats.append(jnp.stack([col_max, col_total, col_num]))
        if step + 1 < total_steps:
            part = out[rows:].reshape(keyframes, pix_dev, channels)
            mem_values = gather_all(part, "space").transpose(1, 0, 2, 3).reshape(
                mem_width, channels
            )

    local = jnp.stack(stats).reshape(total_steps, 3, keyframes, n_space, pix_dev)
    local = local.transpose(3, 1, 0, 2, 4)
    spread = lax.all_to_all(local, "space", 0, 0, tiled=True)
    m, t, n = merge_stats(spread[:, 0], spread[:, 1], spread[:, 2], 0)
    joined = gather_all(jnp.stack([m, t, n]), "tm")
    m, col_total, col_num = merge_stats(joined[:, 0], joined[:, 1], joined[:, 2], 0)

    confidences = []
    for step in range(total_steps):
        chosen = keyframe_index[step]
        key_valid = (
            jnp.arange(pix_all, dtype=jnp.int32)[None, :]
            < jnp.take(valid_pixels, chosen)[:, None]
        ).reshape(mem_width)
        class_match = mem_ids[step][None, :] == class_range[:, None]
        hits = (class_match & key_valid[None, :]).astype(jnp.int32)
        counts = jnp.sum(hits, axis=1)
        all_count = jnp.sum(counts)
        own_ids = lax.dynamic_slice_in_dim(
            mem_ids[step].reshape(keyframes, pix_all), space_pos * pix_dev, pix_dev, 1
        )
        own_valid = pixel_ids[None, :] < jnp.take(valid_pixels, chosen)[:, None]
        own = jnp.take(counts, own_ids)
        own_safe = jnp.where(own_valid, own, 1)
        factor = jnp.sqrt(all_count.astype(jnp.float32) / (channels * own_safe.astype(jnp.float32)))
        conf = jnp.where(own_valid, col_num[step] / col_total[step] * factor, 0.0)
        confidences.append(conf)
    return (readout.reshape(fr_dev, pix_dev, channels), jnp.stack(confidences))


def solution(mesh):
    placed = (
        P("tm", "space", None),
        P("tm", "space", None),
        P("tm", "space", None),
        P(None, "space"),
        P(),
        P(),
    )
    return jax.shard_map(
        body,
        mesh=mesh,
        in_specs=placed,
        out_specs=(P("tm", "space", None), P(None, None, "space")),
        check_vma=False,
    )
```

```python
import math

import jax
import jax.numpy as jnp
from jax import lax
from jax.sharding import PartitionSpec as P

LOWEST = -1e30
NEAR_TM = 4


def broadcast_tm(value, owner, axis, inner):
    size = lax.axis_size(axis)
    me = lax.axis_index(axis)
    rounds = inner.bit_length() - 1
    assert (1 << rounds) == inner and size % inner == 0
    for r in range(rounds):
        bit = 1 << r
        pairs = [(i, i ^ bit) for i in range(size)]
        got = lax.ppermute(value, axis, pairs)
        take = ((me ^ owner) % inner >> r) == 1
        value = jnp.where(take[:, None], got, value)
    groups = size // inner
    rel = (me // inner - owner // inner) % groups
    ahead = [(i, (i + inner) % size) for i in range(size)]
    behind = [(i, (i - inner) % size) for i in range(size)]
    half = value.shape[0] // 2
    for k in range(1, groups // 2 + 1):
        if 2 * k == groups:
            got_a = lax.ppermute(value[:half], axis, ahead)
            got_b = lax.ppermute(value[half:], axis, behind)
            got = jnp.concatenate([got_a, got_b], axis=0)
            value = jnp.where((rel == k)[:, None], got, value)
        else:
            got_a = lax.ppermute(value, axis, ahead)
            got_b = lax.ppermute(value, axis, behind)
            value = jnp.where((rel == k)[:, None], got_a, value)
            value = jnp.where((rel == groups - k)[:, None], got_b, value)
    return value


def gather_all(value, axis):
    size = lax.axis_size(axis)
    spread = jnp.broadcast_to(value[None], (size,) + value.shape)
    return lax.all_to_all(spread, axis, 0, 0, tiled=True)


def merge_stats(col_max, col_total, col_num, axis):
    top = jnp.max(col_max, axis=axis, keepdims=True)
    keep = jnp.exp(col_max - top)
    total = jnp.sum(col_total * keep, axis=axis)
    num = jnp.sum(col_num * keep, axis=axis)
    return jnp.squeeze(top, axis), total, num


def body(queries, keys, label_values, class_ids, valid_pixels, keyframe_index):
    fr_dev, pix_dev, width = queries.shape
    channels = label_values.shape[2]
    total_steps, keyframes = keyframe_index.shape
    n_space = lax.axis_size("space")
    pix_all = pix_dev * n_space
    mem_width = keyframes * pix_all
    time_pos = lax.axis_index("tm")
    space_pos = lax.axis_index("space")
    rows = fr_dev * pix_dev
    scale = 3.0 / math.sqrt(width)
    class_range = jnp.arange(channels, dtype=jnp.int32)

    frame_valid = lax.dynamic_slice_in_dim(valid_pixels, time_pos * fr_dev, fr_dev)
    pixel_ids = space_pos * pix_dev + jnp.arange(pix_dev, dtype=jnp.int32)
    row_valid = (pixel_ids[None, :] < frame_valid[:, None]).reshape(rows)
    query_rows = queries.reshape(rows, width)

    flat_kf = keyframe_index.reshape(-1)
    owners = flat_kf // fr_dev
    slots = flat_kf % fr_dev
    later = keyframes * (total_steps - 1)

    kf_keys = jnp.take(keys, slots, axis=0)
    kf_values = jnp.take(label_values, slots[:keyframes], axis=0)
    kf_queries = jnp.take(queries, slots[keyframes:], axis=0)
    parts = [kf_keys, kf_queries, kf_values]
    part_owners = [owners, owners[keyframes:], owners[:keyframes]]
    flat = jnp.concatenate([p.reshape(-1, width) for p in parts], axis=0)
    row_owner = jnp.concatenate(
        [jnp.repeat(o, p[0].size // width) for p, o in zip(parts, part_owners)]
    )
    flat = broadcast_tm(flat, row_owner, "tm", NEAR_TM)
    sizes = [p.size // width for p in parts]
    kf_keys = flat[:sizes[0]].reshape(kf_keys.shape)
    kf_queries = flat[sizes[0]:sizes[0] + sizes[1]].reshape(kf_queries.shape)
    kf_values = flat[sizes[0] + sizes[1]:].reshape(kf_values.shape)

    kf_ids = jnp.take(class_ids, flat_kf, axis=0).astype(jnp.bfloat16)
    kf_ids = kf_ids.reshape(total_steps, keyframes, pix_dev).transpose(1, 2, 0)
    step_keys = kf_keys.reshape(total_steps, keyframes, pix_dev, width)
    packed = jnp.concatenate(
        [step_keys[s] for s in range(total_steps)] + [kf_values, kf_ids], axis=2
    )
    gathered = lax.all_gather(packed, "space", axis=1, tiled=True)
    mem_keys = [
        gathered[:, :, s * width:(s + 1) * width].reshape(mem_width, width)
        for s in range(total_steps)
    ]
    base = total_steps * width
    mem_values = gathered[:, :, base:base + channels].reshape(mem_width, channels)
    mem_ids = [
        gathered[:, :, base + channels + s].reshape(mem_width).astype(jnp.int32)
        for s in range(total_steps)
    ]

    extra_queries = kf_queries.reshape(later, pix_dev, width)
    extra_valid = pixel_ids[None, :] < jnp.take(valid_pixels, flat_kf[keyframes:])[:, None]

    stats = []
    readout = None
    for step in range(total_steps):
        chosen = keyframe_index[step]
        key_valid = (
            jnp.arange(pix_all, dtype=jnp.int32)[None, :]
            < jnp.take(valid_pixels, chosen)[:, None]
        ).reshape(mem_width)
        ids = mem_ids[step]
        onehot_t = (ids[None, :] == class_range[:, None]).astype(jnp.bfloat16)
        if step + 1 < total_steps:
            extra = extra_queries[step * keyframes:(step + 1) * keyframes].reshape(-1, width)
            extra_ok = extra_valid[step * keyframes:(step + 1) * keyframes].reshape(-1)
            q = jnp.concatenate([query_rows, extra], axis=0)
            q_valid = jnp.concatenate([row_valid, extra_ok], axis=0)
        else:
            q = query_rows
            q_valid = row_valid
        scores = lax.dot_general(
            q, mem_keys[step], (((1,), (1,)), ((), ())), preferred_element_type=jnp.float32
        ) * scale
        masked = jnp.where(key_valid[None, :], scores, LOWEST)
        row_max = jnp.max(masked, axis=1, keepdims=True)
        weights = jnp.where(key_valid[None, :], jnp.exp(scores - row_max), 0.0)
        total = jnp.sum(weights, axis=1, keepdims=True)
        mixed = (
            jnp.dot(weights.astype(jnp.bfloat16), mem_values, preferred_element_type=jnp.float32)
            / total
        )
        out = jnp.where(q_valid[:, None], mixed, 0.0).astype(jnp.bfloat16)
        readout = out[:rows]
        own_scores = scores[:rows]
        picked = jnp.dot(readout, onehot_t, preferred_element_type=jnp.float32)
        col_max = jnp.max(jnp.where(row_valid[:, None], own_scores, LOWEST), axis=0)
        expo = jnp.where(row_valid[:, None], jnp.exp(own_scores - col_max[None, :]), 0.0)
        col_total = jnp.sum(expo, axis=0)
        col_num = jnp.sum(expo * picked, axis=0)
        stats.append(jnp.stack([col_max, col_total, col_num]))
        if step + 1 < total_steps:
            part = out[rows:].reshape(keyframes, pix_dev, channels)
            mem_values = gather_all(part, "space").transpose(1, 0, 2, 3).reshape(
                mem_width, channels
            )

    local = jnp.stack(stats).reshape(total_steps, 3, keyframes, n_space, pix_dev)
    local = local.transpose(3, 1, 0, 2, 4)
    spread = lax.all_to_all(local, "space", 0, 0, tiled=True)
    m, t, n = merge_stats(spread[:, 0], spread[:, 1], spread[:, 2], 0)
    joined = gather_all(jnp.stack([m, t, n]), "tm")
    m, col_total, col_num = merge_stats(joined[:, 0], joined[:, 1], joined[:, 2], 0)

    confidences = []
    for step in range(total_steps):
        chosen = keyframe_index[step]
        key_valid = (
            jnp.arange(pix_all, dtype=jnp.int32)[None, :]
            < jnp.take(valid_pixels, chosen)[:, None]
        ).reshape(mem_width)
        class_match = mem_ids[step][None, :] == class_range[:, None]
        hits = (class_match & key_valid[None, :]).astype(jnp.int32)
        counts = jnp.sum(hits, axis=1)
        all_count = jnp.sum(counts)
        own_ids = lax.dynamic_slice_in_dim(
            mem_ids[step].reshape(keyframes, pix_all), space_pos * pix_dev, pix_dev, 1
        )
        own_valid = pixel_ids[None, :] < jnp.take(valid_pixels, chosen)[:, None]
        own = jnp.take(counts, own_ids)
        own_safe = jnp.where(own_valid, own, 1)
        factor = jnp.sqrt(all_count.astype(jnp.float32) / (channels * own_safe.astype(jnp.float32)))
        conf = jnp.where(own_valid, col_num[step] / col_total[step] * factor, 0.0)
        confidences.append(conf)
    return (readout.reshape(fr_dev, pix_dev, channels), jnp.stack(confidences))


def solution(mesh):
    placed = (
        P("tm", "space", None),
        P("tm", "space", None),
        P("tm", "space", None),
        P(None, "space"),
        P(),
        P(),
    )
    return jax.shard_map(
        body,
        mesh=mesh,
        in_specs=placed,
        out_specs=(P("tm", "space", None), P(None, None, "space")),
        check_vma=False,
    )
```

```python
import math

import jax
import jax.numpy as jnp
from jax import lax
from jax.experimental import pallas as pl
from jax.experimental.pallas import tpu as pltpu
from jax.sharding import PartitionSpec as P

LOWEST = -1e30
NEAR_TM = 4


def broadcast_tm(value, owner, axis, inner):
    size = lax.axis_size(axis)
    me = lax.axis_index(axis)
    rounds = inner.bit_length() - 1
    assert (1 << rounds) == inner and size % inner == 0
    for r in range(rounds):
        bit = 1 << r
        pairs = [(i, i ^ bit) for i in range(size)]
        got = lax.ppermute(value, axis, pairs)
        take = ((me ^ owner) % inner >> r) == 1
        value = jnp.where(take[:, None], got, value)
    groups = size // inner
    rel = (me // inner - owner // inner) % groups
    ahead = [(i, (i + inner) % size) for i in range(size)]
    behind = [(i, (i - inner) % size) for i in range(size)]
    half = value.shape[0] // 2
    for k in range(1, groups // 2 + 1):
        if 2 * k == groups:
            got_a = lax.ppermute(value[:half], axis, ahead)
            got_b = lax.ppermute(value[half:], axis, behind)
            got = jnp.concatenate([got_a, got_b], axis=0)
            value = jnp.where((rel == k)[:, None], got, value)
        else:
            got_a = lax.ppermute(value, axis, ahead)
            got_b = lax.ppermute(value, axis, behind)
            value = jnp.where((rel == k)[:, None], got_a, value)
            value = jnp.where((rel == groups - k)[:, None], got_b, value)
    return value


def gather_all(value, axis):
    size = lax.axis_size(axis)
    spread = jnp.broadcast_to(value[None], (size,) + value.shape)
    return lax.all_to_all(spread, axis, 0, 0, tiled=True)


def merge_stats(col_max, col_total, col_num, axis):
    top = jnp.max(col_max, axis=axis, keepdims=True)
    keep = jnp.exp(col_max - top)
    total = jnp.sum(col_total * keep, axis=axis)
    num = jnp.sum(col_num * keep, axis=axis)
    return jnp.squeeze(top, axis), total, num


BLOCK_ROWS = 128


def step_kernel(q_ref, row_ok_ref, col_ok_ref, keys_ref, key_ok_ref, values_ref, onehot_ref,
                out_ref, cmax_ref, ctot_ref, cnum_ref, *, scale):
    @pl.when(pl.program_id(0) == 0)
    def _():
        cmax_ref[...] = jnp.full_like(cmax_ref, LOWEST)
        ctot_ref[...] = jnp.zeros_like(ctot_ref)
        cnum_ref[...] = jnp.zeros_like(cnum_ref)

    scores = lax.dot_general(
        q_ref[...], keys_ref[...], (((1,), (1,)), ((), ())), preferred_element_type=jnp.float32
    ) * scale
    key_ok = key_ok_ref[...] != 0
    row_ok = row_ok_ref[...] != 0
    col_ok = col_ok_ref[...] != 0
    masked = jnp.where(key_ok, scores, LOWEST)
    row_max = jnp.max(masked, axis=1, keepdims=True)
    weights = jnp.where(key_ok, jnp.exp(scores - row_max), 0.0)
    total = jnp.sum(weights, axis=1, keepdims=True)
    mixed = jnp.dot(
        weights.astype(jnp.bfloat16), values_ref[...], preferred_element_type=jnp.float32
    ) / total
    out = jnp.where(row_ok, mixed, 0.0).astype(jnp.bfloat16)
    out_ref[...] = out
    picked = jnp.dot(out, onehot_ref[...], preferred_element_type=jnp.float32)
    old_max = cmax_ref[...]
    local = jnp.max(jnp.where(col_ok, scores, LOWEST), axis=0, keepdims=True)
    new_max = jnp.maximum(old_max, local)
    keep = jnp.exp(old_max - new_max)
    expo = jnp.where(col_ok, jnp.exp(scores - new_max), 0.0)
    ctot_ref[...] = ctot_ref[...] * keep + jnp.sum(expo, axis=0, keepdims=True)
    cnum_ref[...] = cnum_ref[...] * keep + jnp.sum(expo * picked, axis=0, keepdims=True)
    cmax_ref[...] = new_max


def step_pass(q, row_ok, col_ok, mem_keys, key_ok, mem_values, onehot_t, scale):
    rows, width = q.shape
    mem, channels = mem_values.shape
    blocks = rows // BLOCK_ROWS
    whole = lambda shape: pl.BlockSpec(shape, lambda i: (0, 0))
    by_row = lambda cols: pl.BlockSpec((BLOCK_ROWS, cols), lambda i: (i, 0))
    stat = jax.ShapeDtypeStruct((1, mem), jnp.float32)
    return pl.pallas_call(
        lambda *refs: step_kernel(*refs, scale=scale),
        grid=(blocks,),
        in_specs=[
            by_row(width), by_row(1), by_row(1),
            whole((mem, width)), whole((1, mem)), whole((mem, channels)), whole((channels, mem)),
        ],
        out_specs=[by_row(channels), whole((1, mem)), whole((1, mem)), whole((1, mem))],
        out_shape=[jax.ShapeDtypeStruct((rows, channels), jnp.bfloat16), stat, stat, stat],
        compiler_params=pltpu.CompilerParams(dimension_semantics=("arbitrary",)),
    )(q, row_ok, col_ok, mem_keys, key_ok, mem_values, onehot_t)


def body(queries, keys, label_values, class_ids, valid_pixels, keyframe_index):
    fr_dev, pix_dev, width = queries.shape
    channels = label_values.shape[2]
    total_steps, keyframes = keyframe_index.shape
    n_space = lax.axis_size("space")
    pix_all = pix_dev * n_space
    mem_width = keyframes * pix_all
    time_pos = lax.axis_index("tm")
    space_pos = lax.axis_index("space")
    rows = fr_dev * pix_dev
    scale = 3.0 / math.sqrt(width)
    class_range = jnp.arange(channels, dtype=jnp.int32)

    frame_valid = lax.dynamic_slice_in_dim(valid_pixels, time_pos * fr_dev, fr_dev)
    pixel_ids = space_pos * pix_dev + jnp.arange(pix_dev, dtype=jnp.int32)
    row_valid = (pixel_ids[None, :] < frame_valid[:, None]).reshape(rows)
    query_rows = queries.reshape(rows, width)

    flat_kf = keyframe_index.reshape(-1)
    owners = flat_kf // fr_dev
    slots = flat_kf % fr_dev
    later = keyframes * (total_steps - 1)

    kf_keys = jnp.take(keys, slots, axis=0)
    kf_values = jnp.take(label_values, slots[:keyframes], axis=0)
    kf_queries = jnp.take(queries, slots[keyframes:], axis=0)
    parts = [kf_keys, kf_queries, kf_values]
    part_owners = [owners, owners[keyframes:], owners[:keyframes]]
    flat = jnp.concatenate([p.reshape(-1, width) for p in parts], axis=0)
    row_owner = jnp.concatenate(
        [jnp.repeat(o, p[0].size // width) for p, o in zip(parts, part_owners)]
    )
    flat = broadcast_tm(flat, row_owner, "tm", NEAR_TM)
    sizes = [p.size // width for p in parts]
    kf_keys = flat[:sizes[0]].reshape(kf_keys.shape)
    kf_queries = flat[sizes[0]:sizes[0] + sizes[1]].reshape(kf_queries.shape)
    kf_values = flat[sizes[0] + sizes[1]:].reshape(kf_values.shape)

    kf_ids = jnp.take(class_ids, flat_kf, axis=0).astype(jnp.bfloat16)
    kf_ids = kf_ids.reshape(total_steps, keyframes, pix_dev).transpose(1, 2, 0)
    step_keys = kf_keys.reshape(total_steps, keyframes, pix_dev, width)
    packed = jnp.concatenate(
        [step_keys[s] for s in range(total_steps)] + [kf_values, kf_ids], axis=2
    )
    gathered = lax.all_gather(packed, "space", axis=1, tiled=True)
    mem_keys = [
        gathered[:, :, s * width:(s + 1) * width].reshape(mem_width, width)
        for s in range(total_steps)
    ]
    base = total_steps * width
    mem_values = gathered[:, :, base:base + channels].reshape(mem_width, channels)
    mem_ids = [
        gathered[:, :, base + channels + s].reshape(mem_width).astype(jnp.int32)
        for s in range(total_steps)
    ]

    extra_queries = kf_queries.reshape(later, pix_dev, width)
    extra_valid = pixel_ids[None, :] < jnp.take(valid_pixels, flat_kf[keyframes:])[:, None]

    stats = []
    readout = None
    for step in range(total_steps):
        chosen = keyframe_index[step]
        key_valid = (
            jnp.arange(pix_all, dtype=jnp.int32)[None, :]
            < jnp.take(valid_pixels, chosen)[:, None]
        ).reshape(mem_width)
        ids = mem_ids[step]
        onehot_t = (ids[None, :] == class_range[:, None]).astype(jnp.bfloat16)
        if step + 1 < total_steps:
            extra = extra_queries[step * keyframes:(step + 1) * keyframes].reshape(-1, width)
            extra_ok = extra_valid[step * keyframes:(step + 1) * keyframes].reshape(-1)
            q = jnp.concatenate([query_rows, extra], axis=0)
            q_valid = jnp.concatenate([row_valid, extra_ok], axis=0)
        else:
            q = query_rows
            q_valid = row_valid
        col_ok = jnp.concatenate(
            [row_valid, jnp.zeros((q.shape[0] - rows,), jnp.bool_)], axis=0
        )
        out, col_max, col_total, col_num = step_pass(
            q,
            q_valid.astype(jnp.int32)[:, None],
            col_ok.astype(jnp.int32)[:, None],
            mem_keys[step],
            key_valid.astype(jnp.int32)[None, :],
            mem_values,
            onehot_t,
            scale,
        )
        readout = out[:rows]
        stats.append(jnp.stack([col_max[0], col_total[0], col_num[0]]))
        if step + 1 < total_steps:
            part = out[rows:].reshape(keyframes, pix_dev, channels)
            mem_values = gather_all(part, "space").transpose(1, 0, 2, 3).reshape(
                mem_width, channels
            )

    local = jnp.stack(stats).reshape(total_steps, 3, keyframes, n_space, pix_dev)
    local = local.transpose(3, 1, 0, 2, 4)
    spread = lax.all_to_all(local, "space", 0, 0, tiled=True)
    m, t, n = merge_stats(spread[:, 0], spread[:, 1], spread[:, 2], 0)
    joined = gather_all(jnp.stack([m, t, n]), "tm")
    m, col_total, col_num = merge_stats(joined[:, 0], joined[:, 1], joined[:, 2], 0)

    confidences = []
    for step in range(total_steps):
        chosen = keyframe_index[step]
        key_valid = (
            jnp.arange(pix_all, dtype=jnp.int32)[None, :]
            < jnp.take(valid_pixels, chosen)[:, None]
        ).reshape(mem_width)
        class_match = mem_ids[step][None, :] == class_range[:, None]
        hits = (class_match & key_valid[None, :]).astype(jnp.int32)
        counts = jnp.sum(hits, axis=1)
        all_count = jnp.sum(counts)
        own_ids = lax.dynamic_slice_in_dim(
            mem_ids[step].reshape(keyframes, pix_all), space_pos * pix_dev, pix_dev, 1
        )
        own_valid = pixel_ids[None, :] < jnp.take(valid_pixels, chosen)[:, None]
        own = jnp.take(counts, own_ids)
        own_safe = jnp.where(own_valid, own, 1)
        factor = jnp.sqrt(all_count.astype(jnp.float32) / (channels * own_safe.astype(jnp.float32)))
        conf = jnp.where(own_valid, col_num[step] / col_total[step] * factor, 0.0)
        confidences.append(conf)
    return (readout.reshape(fr_dev, pix_dev, channels), jnp.stack(confidences))


def solution(mesh):
    placed = (
        P("tm", "space", None),
        P("tm", "space", None),
        P("tm", "space", None),
        P(None, "space"),
        P(),
        P(),
    )
    return jax.shard_map(
        body,
        mesh=mesh,
        in_specs=placed,
        out_specs=(P("tm", "space", None), P(None, None, "space")),
        check_vma=False,
    )
```

```python
import math

import jax
import jax.numpy as jnp
from jax import lax
from jax.experimental import pallas as pl
from jax.experimental.pallas import tpu as pltpu
from jax.sharding import PartitionSpec as P

LOWEST = -1e30
NEAR_TM = 4


def broadcast_tm(value, owner, axis, inner):
    size = lax.axis_size(axis)
    me = lax.axis_index(axis)
    rounds = inner.bit_length() - 1
    assert (1 << rounds) == inner and size % inner == 0
    for r in range(rounds):
        bit = 1 << r
        pairs = [(i, i ^ bit) for i in range(size)]
        got = lax.ppermute(value, axis, pairs)
        take = ((me ^ owner) % inner >> r) == 1
        value = jnp.where(take[:, None], got, value)
    groups = size // inner
    rel = (me // inner - owner // inner) % groups
    ahead = [(i, (i + inner) % size) for i in range(size)]
    behind = [(i, (i - inner) % size) for i in range(size)]
    half = value.shape[0] // 2
    for k in range(1, groups // 2 + 1):
        if 2 * k == groups:
            got_a = lax.ppermute(value[:half], axis, ahead)
            got_b = lax.ppermute(value[half:], axis, behind)
            got = jnp.concatenate([got_a, got_b], axis=0)
            value = jnp.where((rel == k)[:, None], got, value)
        else:
            got_a = lax.ppermute(value, axis, ahead)
            got_b = lax.ppermute(value, axis, behind)
            value = jnp.where((rel == k)[:, None], got_a, value)
            value = jnp.where((rel == groups - k)[:, None], got_b, value)
    return value


def gather_all(value, axis):
    size = lax.axis_size(axis)
    spread = jnp.broadcast_to(value[None], (size,) + value.shape)
    return lax.all_to_all(spread, axis, 0, 0, tiled=True)


def merge_stats(col_max, col_total, col_num, axis):
    top = jnp.max(col_max, axis=axis, keepdims=True)
    keep = jnp.exp(col_max - top)
    total = jnp.sum(col_total * keep, axis=axis)
    num = jnp.sum(col_num * keep, axis=axis)
    return jnp.squeeze(top, axis), total, num


BLOCK_ROWS = 128


def step_kernel(q_ref, row_ok_ref, col_ok_ref, keys_ref, key_ok_ref, values_ref, aux_ref,
                *out_refs, scale, step, with_stats):
    scores = lax.dot_general(
        q_ref[...], keys_ref[...], (((1,), (1,)), ((), ())), preferred_element_type=jnp.float32
    ) * scale
    key_ok = key_ok_ref[...] != 0
    row_ok = row_ok_ref[...] != 0
    masked = jnp.where(key_ok, scores, LOWEST)
    row_max = jnp.max(masked, axis=1, keepdims=True)
    weights = jnp.where(key_ok, jnp.exp(scores - row_max), 0.0)
    total = jnp.sum(weights, axis=1, keepdims=True)
    mixed = jnp.dot(
        weights.astype(jnp.bfloat16), values_ref[...], preferred_element_type=jnp.float32
    ) / total
    out = jnp.where(row_ok, mixed, 0.0).astype(jnp.bfloat16)
    out_refs[0][...] = out
    if not with_stats:
        return
    cmax_ref, ctot_ref, cnum_ref = out_refs[1:]

    @pl.when(pl.program_id(0) == 0)
    def _():
        cmax_ref[...] = jnp.full_like(cmax_ref, LOWEST)
        ctot_ref[...] = jnp.zeros_like(ctot_ref)
        cnum_ref[...] = jnp.zeros_like(cnum_ref)

    channels = values_ref.shape[1]
    ids = aux_ref[:, channels + step:channels + step + 1].astype(jnp.float32)
    classes = lax.broadcasted_iota(jnp.int32, (1, channels), 1).astype(jnp.float32)
    onehot = (ids == classes).astype(jnp.bfloat16)
    picked = lax.dot_general(
        out, onehot, (((1,), (1,)), ((), ())), preferred_element_type=jnp.float32
    )
    col_ok = col_ok_ref[...] != 0
    old_max = cmax_ref[...]
    local = jnp.max(jnp.where(col_ok, scores, LOWEST), axis=0, keepdims=True)
    new_max = jnp.maximum(old_max, local)
    keep = jnp.exp(old_max - new_max)
    expo = jnp.where(col_ok, jnp.exp(scores - new_max), 0.0)
    ctot_ref[...] = ctot_ref[...] * keep + jnp.sum(expo, axis=0, keepdims=True)
    cnum_ref[...] = cnum_ref[...] * keep + jnp.sum(expo * picked, axis=0, keepdims=True)
    cmax_ref[...] = new_max


def step_pass(q, row_ok, col_ok, gathered, step, key_ok, mem_values, scale, with_stats):
    rows, width = q.shape
    parts, mem, _ = gathered.shape
    channels = mem_values.shape[1]
    blocks = rows // BLOCK_ROWS
    whole = lambda shape: pl.BlockSpec(shape, lambda i: (0, 0))
    by_row = lambda cols: pl.BlockSpec((BLOCK_ROWS, cols), lambda i: (i, 0))
    stat = jax.ShapeDtypeStruct((1, mem), jnp.float32)
    out_specs = [by_row(channels)]
    out_shape = [jax.ShapeDtypeStruct((rows, channels), jnp.bfloat16)]
    if with_stats:
        out_specs += [whole((1, mem))] * 3
        out_shape += [stat] * 3
    return pl.pallas_call(
        lambda *refs: step_kernel(*refs, scale=scale, step=step, with_stats=with_stats),
        grid=(blocks,),
        in_specs=[
            by_row(width), by_row(1), by_row(1),
            pl.BlockSpec((None, mem, width), lambda i: (step, 0, 0)),
            whole((1, mem)),
            whole((mem, channels)),
            pl.BlockSpec((None, mem, 128), lambda i: (parts - 1, 0, 0)),
        ],
        out_specs=out_specs,
        out_shape=out_shape,
        compiler_params=pltpu.CompilerParams(dimension_semantics=("arbitrary",)),
    )(q, row_ok, col_ok, gathered, key_ok, mem_values, gathered)


def body(queries, keys, label_values, class_ids, valid_pixels, keyframe_index):
    fr_dev, pix_dev, width = queries.shape
    channels = label_values.shape[2]
    total_steps, keyframes = keyframe_index.shape
    n_space = lax.axis_size("space")
    pix_all = pix_dev * n_space
    mem_width = keyframes * pix_all
    time_pos = lax.axis_index("tm")
    space_pos = lax.axis_index("space")
    rows = fr_dev * pix_dev
    scale = 3.0 / math.sqrt(width)
    class_range = jnp.arange(channels, dtype=jnp.int32)

    frame_valid = lax.dynamic_slice_in_dim(valid_pixels, time_pos * fr_dev, fr_dev)
    pixel_ids = space_pos * pix_dev + jnp.arange(pix_dev, dtype=jnp.int32)
    row_valid = (pixel_ids[None, :] < frame_valid[:, None]).reshape(rows)
    query_rows = queries.reshape(rows, width)

    flat_kf = keyframe_index.reshape(-1)
    owners = flat_kf // fr_dev
    slots = flat_kf % fr_dev
    later = keyframes * (total_steps - 1)

    kf_keys = jnp.take(keys, slots, axis=0)
    kf_values = jnp.take(label_values, slots[:keyframes], axis=0)
    kf_queries = jnp.take(queries, slots[keyframes:], axis=0)
    parts = [kf_keys, kf_queries, kf_values]
    part_owners = [owners, owners[keyframes:], owners[:keyframes]]
    flat = jnp.concatenate([p.reshape(-1, width) for p in parts], axis=0)
    row_owner = jnp.concatenate(
        [jnp.repeat(o, p[0].size // width) for p, o in zip(parts, part_owners)]
    )
    flat = broadcast_tm(flat, row_owner, "tm", NEAR_TM)
    sizes = [p.size // width for p in parts]
    kf_keys = flat[:sizes[0]].reshape(kf_keys.shape)
    kf_queries = flat[sizes[0]:sizes[0] + sizes[1]].reshape(kf_queries.shape)
    kf_values = flat[sizes[0] + sizes[1]:].reshape(kf_values.shape)

    kf_ids = jnp.take(class_ids, flat_kf, axis=0).astype(jnp.bfloat16)
    kf_ids = kf_ids.reshape(total_steps, keyframes, pix_dev).transpose(1, 2, 0)
    step_keys = kf_keys.reshape(total_steps, keyframes, pix_dev, width)
    aux = jnp.concatenate([kf_values, kf_ids], axis=2)
    aux = jnp.pad(aux, ((0, 0), (0, 0), (0, width - aux.shape[2])))
    packed = jnp.concatenate([step_keys, aux[None]], axis=0)
    gathered = lax.all_gather(packed, "space", axis=2, tiled=True)
    gathered = gathered.reshape(total_steps + 1, mem_width, width)
    mem_values = gathered[total_steps, :, :channels]
    mem_ids = [
        gathered[total_steps, :, channels + s].astype(jnp.int32) for s in range(total_steps)
    ]

    extra_queries = kf_queries.reshape(later, pix_dev, width)
    extra_valid = pixel_ids[None, :] < jnp.take(valid_pixels, flat_kf[keyframes:])[:, None]

    stats = []
    readout = None
    for step in range(total_steps):
        chosen = keyframe_index[step]
        key_valid = (
            jnp.arange(pix_all, dtype=jnp.int32)[None, :]
            < jnp.take(valid_pixels, chosen)[:, None]
        ).reshape(mem_width)
        key_ok = key_valid.astype(jnp.int32)[None, :]
        if step + 1 < total_steps:
            extra = extra_queries[step * keyframes:(step + 1) * keyframes].reshape(-1, width)
            extra_ok = extra_valid[step * keyframes:(step + 1) * keyframes].reshape(-1, 1)
            extra_ok = extra_ok.astype(jnp.int32)
            (part,) = step_pass(
                extra, extra_ok, extra_ok, gathered, step, key_ok, mem_values, scale, False
            )
            part = part.reshape(keyframes, pix_dev, channels)
            next_values = gather_all(part, "space").transpose(1, 0, 2, 3).reshape(
                mem_width, channels
            )
        ok = row_valid.astype(jnp.int32)[:, None]
        readout, col_max, col_total, col_num = step_pass(
            query_rows, ok, ok, gathered, step, key_ok, mem_values, scale, True
        )
        stats.append(jnp.stack([col_max[0], col_total[0], col_num[0]]))
        if step + 1 < total_steps:
            mem_values = next_values

    local = jnp.stack(stats).reshape(total_steps, 3, keyframes, n_space, pix_dev)
    local = local.transpose(3, 1, 0, 2, 4)
    spread = lax.all_to_all(local, "space", 0, 0, tiled=True)
    m, t, n = merge_stats(spread[:, 0], spread[:, 1], spread[:, 2], 0)
    joined = gather_all(jnp.stack([m, t, n]), "tm")
    m, col_total, col_num = merge_stats(joined[:, 0], joined[:, 1], joined[:, 2], 0)

    confidences = []
    for step in range(total_steps):
        chosen = keyframe_index[step]
        key_valid = (
            jnp.arange(pix_all, dtype=jnp.int32)[None, :]
            < jnp.take(valid_pixels, chosen)[:, None]
        ).reshape(mem_width)
        class_match = mem_ids[step][None, :] == class_range[:, None]
        hits = (class_match & key_valid[None, :]).astype(jnp.int32)
        counts = jnp.sum(hits, axis=1)
        all_count = jnp.sum(counts)
        own_ids = lax.dynamic_slice_in_dim(
            mem_ids[step].reshape(keyframes, pix_all), space_pos * pix_dev, pix_dev, 1
        )
        own_valid = pixel_ids[None, :] < jnp.take(valid_pixels, chosen)[:, None]
        own = jnp.take(counts, own_ids)
        own_safe = jnp.where(own_valid, own, 1)
        factor = jnp.sqrt(all_count.astype(jnp.float32) / (channels * own_safe.astype(jnp.float32)))
        conf = jnp.where(own_valid, col_num[step] / col_total[step] * factor, 0.0)
        confidences.append(conf)
    return (readout.reshape(fr_dev, pix_dev, channels), jnp.stack(confidences))


def solution(mesh):
    placed = (
        P("tm", "space", None),
        P("tm", "space", None),
        P("tm", "space", None),
        P(None, "space"),
        P(),
        P(),
    )
    return jax.shard_map(
        body,
        mesh=mesh,
        in_specs=placed,
        out_specs=(P("tm", "space", None), P(None, None, "space")),
        check_vma=False,
    )
```

```python
import math

import jax
import jax.numpy as jnp
from jax import lax
from jax.experimental import pallas as pl
from jax.experimental.pallas import tpu as pltpu
from jax.sharding import PartitionSpec as P

LOWEST = -1e30
NEAR_TM = 4


def broadcast_tm(value, owner, axis, inner):
    size = lax.axis_size(axis)
    me = lax.axis_index(axis)
    rounds = inner.bit_length() - 1
    assert (1 << rounds) == inner and size % inner == 0
    for r in range(rounds):
        bit = 1 << r
        pairs = [(i, i ^ bit) for i in range(size)]
        got = lax.ppermute(value, axis, pairs)
        take = ((me ^ owner) % inner >> r) == 1
        value = jnp.where(take[:, None], got, value)
    groups = size // inner
    rel = (me // inner - owner // inner) % groups
    ahead = [(i, (i + inner) % size) for i in range(size)]
    behind = [(i, (i - inner) % size) for i in range(size)]
    half = value.shape[0] // 2
    for k in range(1, groups // 2 + 1):
        if 2 * k == groups:
            got_a = lax.ppermute(value[:half], axis, ahead)
            got_b = lax.ppermute(value[half:], axis, behind)
            got = jnp.concatenate([got_a, got_b], axis=0)
            value = jnp.where((rel == k)[:, None], got, value)
        else:
            got_a = lax.ppermute(value, axis, ahead)
            got_b = lax.ppermute(value, axis, behind)
            value = jnp.where((rel == k)[:, None], got_a, value)
            value = jnp.where((rel == groups - k)[:, None], got_b, value)
    return value


def gather_all(value, axis):
    size = lax.axis_size(axis)
    spread = jnp.broadcast_to(value[None], (size,) + value.shape)
    return lax.all_to_all(spread, axis, 0, 0, tiled=True)


def merge_stats(col_max, col_total, col_num, axis):
    top = jnp.max(col_max, axis=axis, keepdims=True)
    keep = jnp.exp(col_max - top)
    total = jnp.sum(col_total * keep, axis=axis)
    num = jnp.sum(col_num * keep, axis=axis)
    return jnp.squeeze(top, axis), total, num


BLOCK_ROWS = 128


def step_kernel(q_ref, row_ok_ref, col_ok_ref, keys_ref, key_ok_ref, values_ref, aux_ref,
                *out_refs, scale, step, with_stats):
    scores = lax.dot_general(
        q_ref[...], keys_ref[...], (((1,), (1,)), ((), ())), preferred_element_type=jnp.float32
    ) * scale
    key_ok = key_ok_ref[...] != 0
    row_ok = row_ok_ref[...] != 0
    masked = jnp.where(key_ok, scores, LOWEST)
    row_max = jnp.max(masked, axis=1, keepdims=True)
    weights = jnp.where(key_ok, jnp.exp(scores - row_max), 0.0)
    total = jnp.sum(weights, axis=1, keepdims=True)
    mixed = jnp.dot(
        weights.astype(jnp.bfloat16), values_ref[...], preferred_element_type=jnp.float32
    ) / total
    out = jnp.where(row_ok, mixed, 0.0).astype(jnp.bfloat16)
    out_refs[0][...] = out
    if not with_stats:
        return
    cmax_ref, ctot_ref, cnum_ref, onehot_ref = out_refs[1:]

    @pl.when(pl.program_id(0) == 0)
    def _():
        cmax_ref[...] = jnp.full_like(cmax_ref, LOWEST)
        ctot_ref[...] = jnp.zeros_like(ctot_ref)
        cnum_ref[...] = jnp.zeros_like(cnum_ref)
        channels = values_ref.shape[1]
        ids = aux_ref[:, channels + step:channels + step + 1].astype(jnp.float32)
        classes = lax.broadcasted_iota(jnp.int32, (1, channels), 1).astype(jnp.float32)
        onehot = (ids == classes).astype(jnp.float32)
        onehot_ref[...] = jnp.transpose(onehot).astype(jnp.bfloat16)

    picked = jnp.dot(out, onehot_ref[...], preferred_element_type=jnp.float32)
    col_ok = col_ok_ref[...] != 0
    old_max = cmax_ref[...]
    local = jnp.max(jnp.where(col_ok, scores, LOWEST), axis=0, keepdims=True)
    new_max = jnp.maximum(old_max, local)
    keep = jnp.exp(old_max - new_max)
    expo = jnp.where(col_ok, jnp.exp(scores - new_max), 0.0)
    ctot_ref[...] = ctot_ref[...] * keep + jnp.sum(expo, axis=0, keepdims=True)
    cnum_ref[...] = cnum_ref[...] * keep + jnp.sum(expo * picked, axis=0, keepdims=True)
    cmax_ref[...] = new_max


def step_pass(q, row_ok, col_ok, gathered, step, key_ok, mem_values, scale, with_stats):
    rows, width = q.shape
    parts, mem, _ = gathered.shape
    channels = mem_values.shape[1]
    blocks = rows // BLOCK_ROWS
    whole = lambda shape: pl.BlockSpec(shape, lambda i: (0, 0))
    by_row = lambda cols: pl.BlockSpec((BLOCK_ROWS, cols), lambda i: (i, 0))
    stat = jax.ShapeDtypeStruct((1, mem), jnp.float32)
    out_specs = [by_row(channels)]
    out_shape = [jax.ShapeDtypeStruct((rows, channels), jnp.bfloat16)]
    if with_stats:
        out_specs += [whole((1, mem))] * 3
        out_shape += [stat] * 3
    return pl.pallas_call(
        lambda *refs: step_kernel(*refs, scale=scale, step=step, with_stats=with_stats),
        grid=(blocks,),
        in_specs=[
            by_row(width), by_row(1), by_row(1),
            pl.BlockSpec((None, mem, width), lambda i: (step, 0, 0)),
            whole((1, mem)),
            whole((mem, channels)),
            pl.BlockSpec((None, mem, 128), lambda i: (parts - 1, 0, 0)),
        ],
        out_specs=out_specs,
        out_shape=out_shape,
        scratch_shapes=[pltpu.VMEM((channels, mem), jnp.bfloat16)] if with_stats else [],
        compiler_params=pltpu.CompilerParams(dimension_semantics=("arbitrary",)),
    )(q, row_ok, col_ok, gathered, key_ok, mem_values, gathered)


def body(queries, keys, label_values, class_ids, valid_pixels, keyframe_index):
    fr_dev, pix_dev, width = queries.shape
    channels = label_values.shape[2]
    total_steps, keyframes = keyframe_index.shape
    n_space = lax.axis_size("space")
    pix_all = pix_dev * n_space
    mem_width = keyframes * pix_all
    time_pos = lax.axis_index("tm")
    space_pos = lax.axis_index("space")
    rows = fr_dev * pix_dev
    scale = 3.0 / math.sqrt(width)
    class_range = jnp.arange(channels, dtype=jnp.int32)

    frame_valid = lax.dynamic_slice_in_dim(valid_pixels, time_pos * fr_dev, fr_dev)
    pixel_ids = space_pos * pix_dev + jnp.arange(pix_dev, dtype=jnp.int32)
    row_valid = (pixel_ids[None, :] < frame_valid[:, None]).reshape(rows)
    query_rows = queries.reshape(rows, width)

    flat_kf = keyframe_index.reshape(-1)
    owners = flat_kf // fr_dev
    slots = flat_kf % fr_dev
    later = keyframes * (total_steps - 1)

    kf_keys = jnp.take(keys, slots, axis=0)
    kf_values = jnp.take(label_values, slots[:keyframes], axis=0)
    kf_queries = jnp.take(queries, slots[keyframes:], axis=0)
    parts = [kf_keys, kf_queries, kf_values]
    part_owners = [owners, owners[keyframes:], owners[:keyframes]]
    flat = jnp.concatenate([p.reshape(-1, width) for p in parts], axis=0)
    row_owner = jnp.concatenate(
        [jnp.repeat(o, p[0].size // width) for p, o in zip(parts, part_owners)]
    )
    flat = broadcast_tm(flat, row_owner, "tm", NEAR_TM)
    sizes = [p.size // width for p in parts]
    kf_keys = flat[:sizes[0]].reshape(kf_keys.shape)
    kf_queries = flat[sizes[0]:sizes[0] + sizes[1]].reshape(kf_queries.shape)
    kf_values = flat[sizes[0] + sizes[1]:].reshape(kf_values.shape)

    kf_ids = jnp.take(class_ids, flat_kf, axis=0).astype(jnp.bfloat16)
    kf_ids = kf_ids.reshape(total_steps, keyframes, pix_dev).transpose(1, 2, 0)
    step_keys = kf_keys.reshape(total_steps, keyframes, pix_dev, width)
    aux = jnp.concatenate([kf_values, kf_ids], axis=2)
    aux = jnp.pad(aux, ((0, 0), (0, 0), (0, width - aux.shape[2])))
    packed = jnp.concatenate([step_keys, aux[None]], axis=0)
    gathered = lax.all_gather(packed, "space", axis=2, tiled=True)
    gathered = gathered.reshape(total_steps + 1, mem_width, width)
    mem_values = gathered[total_steps, :, :channels]
    mem_ids = [
        gathered[total_steps, :, channels + s].astype(jnp.int32) for s in range(total_steps)
    ]

    extra_queries = kf_queries.reshape(later, pix_dev, width)
    extra_valid = pixel_ids[None, :] < jnp.take(valid_pixels, flat_kf[keyframes:])[:, None]

    stats = []
    readout = None
    for step in range(total_steps):
        chosen = keyframe_index[step]
        key_valid = (
            jnp.arange(pix_all, dtype=jnp.int32)[None, :]
            < jnp.take(valid_pixels, chosen)[:, None]
        ).reshape(mem_width)
        key_ok = key_valid.astype(jnp.int32)[None, :]
        if step + 1 < total_steps:
            extra = extra_queries[step * keyframes:(step + 1) * keyframes].reshape(-1, width)
            extra_ok = extra_valid[step * keyframes:(step + 1) * keyframes].reshape(-1, 1)
            extra_ok = extra_ok.astype(jnp.int32)
            (part,) = step_pass(
                extra, extra_ok, extra_ok, gathered, step, key_ok, mem_values, scale, False
            )
            part = part.reshape(keyframes, pix_dev, channels)
            next_values = gather_all(part, "space").transpose(1, 0, 2, 3).reshape(
                mem_width, channels
            )
        ok = row_valid.astype(jnp.int32)[:, None]
        readout, col_max, col_total, col_num = step_pass(
            query_rows, ok, ok, gathered, step, key_ok, mem_values, scale, True
        )
        stats.append(jnp.stack([col_max[0], col_total[0], col_num[0]]))
        if step + 1 < total_steps:
            mem_values = next_values

    local = jnp.stack(stats).reshape(total_steps, 3, keyframes, n_space, pix_dev)
    local = local.transpose(3, 1, 0, 2, 4)
    spread = lax.all_to_all(local, "space", 0, 0, tiled=True)
    m, t, n = merge_stats(spread[:, 0], spread[:, 1], spread[:, 2], 0)
    joined = gather_all(jnp.stack([m, t, n]), "tm")
    m, col_total, col_num = merge_stats(joined[:, 0], joined[:, 1], joined[:, 2], 0)

    confidences = []
    for step in range(total_steps):
        chosen = keyframe_index[step]
        key_valid = (
            jnp.arange(pix_all, dtype=jnp.int32)[None, :]
            < jnp.take(valid_pixels, chosen)[:, None]
        ).reshape(mem_width)
        class_match = mem_ids[step][None, :] == class_range[:, None]
        hits = (class_match & key_valid[None, :]).astype(jnp.int32)
        counts = jnp.sum(hits, axis=1)
        all_count = jnp.sum(counts)
        own_ids = lax.dynamic_slice_in_dim(
            mem_ids[step].reshape(keyframes, pix_all), space_pos * pix_dev, pix_dev, 1
        )
        own_valid = pixel_ids[None, :] < jnp.take(valid_pixels, chosen)[:, None]
        own = jnp.take(counts, own_ids)
        own_safe = jnp.where(own_valid, own, 1)
        factor = jnp.sqrt(all_count.astype(jnp.float32) / (channels * own_safe.astype(jnp.float32)))
        conf = jnp.where(own_valid, col_num[step] / col_total[step] * factor, 0.0)
        confidences.append(conf)
    return (readout.reshape(fr_dev, pix_dev, channels), jnp.stack(confidences))


def solution(mesh):
    placed = (
        P("tm", "space", None),
        P("tm", "space", None),
        P("tm", "space", None),
        P(None, "space"),
        P(),
        P(),
    )
    return jax.shard_map(
        body,
        mesh=mesh,
        in_specs=placed,
        out_specs=(P("tm", "space", None), P(None, None, "space")),
        check_vma=False,
    )
```

```python
import math

import jax
import jax.numpy as jnp
from jax import lax
from jax.experimental import pallas as pl
from jax.experimental.pallas import tpu as pltpu
from jax.sharding import PartitionSpec as P

LOWEST = -1e30
NEAR_TM = 4


def broadcast_tm(value, owner, axis, inner):
    size = lax.axis_size(axis)
    me = lax.axis_index(axis)
    rounds = inner.bit_length() - 1
    assert (1 << rounds) == inner and size % inner == 0
    for r in range(rounds):
        bit = 1 << r
        pairs = [(i, i ^ bit) for i in range(size)]
        got = lax.ppermute(value, axis, pairs)
        take = ((me ^ owner) % inner >> r) == 1
        value = jnp.where(take[:, None], got, value)
    groups = size // inner
    rel = (me // inner - owner // inner) % groups
    ahead = [(i, (i + inner) % size) for i in range(size)]
    behind = [(i, (i - inner) % size) for i in range(size)]
    half = value.shape[0] // 2
    for k in range(1, groups // 2 + 1):
        if 2 * k == groups:
            got_a = lax.ppermute(value[:half], axis, ahead)
            got_b = lax.ppermute(value[half:], axis, behind)
            got = jnp.concatenate([got_a, got_b], axis=0)
            value = jnp.where((rel == k)[:, None], got, value)
        else:
            got_a = lax.ppermute(value, axis, ahead)
            got_b = lax.ppermute(value, axis, behind)
            value = jnp.where((rel == k)[:, None], got_a, value)
            value = jnp.where((rel == groups - k)[:, None], got_b, value)
    return value


def gather_all(value, axis):
    size = lax.axis_size(axis)
    spread = jnp.broadcast_to(value[None], (size,) + value.shape)
    return lax.all_to_all(spread, axis, 0, 0, tiled=True)


def merge_stats(col_max, col_total, col_num, axis):
    top = jnp.max(col_max, axis=axis, keepdims=True)
    keep = jnp.exp(col_max - top)
    total = jnp.sum(col_total * keep, axis=axis)
    num = jnp.sum(col_num * keep, axis=axis)
    return jnp.squeeze(top, axis), total, num


BLOCK_ROWS = 256


def step_kernel(q_ref, row_ok_ref, col_ok_ref, keys_ref, key_ok_ref, values_ref, aux_ref,
                *out_refs, scale, step, with_stats):
    scores = lax.dot_general(
        q_ref[...], keys_ref[...], (((1,), (1,)), ((), ())), preferred_element_type=jnp.float32
    ) * scale
    key_ok = key_ok_ref[...] != 0
    row_ok = row_ok_ref[...] != 0
    masked = jnp.where(key_ok, scores, LOWEST)
    row_max = jnp.max(masked, axis=1, keepdims=True)
    weights = jnp.where(key_ok, jnp.exp(scores - row_max), 0.0)
    total = jnp.sum(weights, axis=1, keepdims=True)
    mixed = jnp.dot(
        weights.astype(jnp.bfloat16), values_ref[...], preferred_element_type=jnp.float32
    ) / total
    out = jnp.where(row_ok, mixed, 0.0).astype(jnp.bfloat16)
    out_refs[0][...] = out
    if not with_stats:
        return
    cmax_ref, ctot_ref, cnum_ref, onehot_ref = out_refs[1:]

    @pl.when(pl.program_id(0) == 0)
    def _():
        cmax_ref[...] = jnp.full_like(cmax_ref, LOWEST)
        ctot_ref[...] = jnp.zeros_like(ctot_ref)
        cnum_ref[...] = jnp.zeros_like(cnum_ref)
        channels = values_ref.shape[1]
        ids = aux_ref[:, channels + step:channels + step + 1].astype(jnp.float32)
        classes = lax.broadcasted_iota(jnp.int32, (1, channels), 1).astype(jnp.float32)
        onehot = (ids == classes).astype(jnp.float32)
        onehot_ref[...] = jnp.transpose(onehot).astype(jnp.bfloat16)

    picked = jnp.dot(out, onehot_ref[...], preferred_element_type=jnp.float32)
    col_ok = col_ok_ref[...] != 0
    old_max = cmax_ref[...]
    local = jnp.max(jnp.where(col_ok, scores, LOWEST), axis=0, keepdims=True)
    new_max = jnp.maximum(old_max, local)
    keep = jnp.exp(old_max - new_max)
    expo = jnp.where(col_ok, jnp.exp(scores - new_max), 0.0)
    ctot_ref[...] = ctot_ref[...] * keep + jnp.sum(expo, axis=0, keepdims=True)
    cnum_ref[...] = cnum_ref[...] * keep + jnp.sum(expo * picked, axis=0, keepdims=True)
    cmax_ref[...] = new_max


def step_pass(q, row_ok, col_ok, gathered, step, key_ok, mem_values, scale, with_stats):
    rows, width = q.shape
    parts, mem, _ = gathered.shape
    channels = mem_values.shape[1]
    block = min(BLOCK_ROWS, rows)
    assert rows % block == 0
    blocks = rows // block
    whole = lambda shape: pl.BlockSpec(shape, lambda i: (0, 0))
    by_row = lambda cols: pl.BlockSpec((block, cols), lambda i: (i, 0))
    stat = jax.ShapeDtypeStruct((1, mem), jnp.float32)
    out_specs = [by_row(channels)]
    out_shape = [jax.ShapeDtypeStruct((rows, channels), jnp.bfloat16)]
    if with_stats:
        out_specs += [whole((1, mem))] * 3
        out_shape += [stat] * 3
    return pl.pallas_call(
        lambda *refs: step_kernel(*refs, scale=scale, step=step, with_stats=with_stats),
        grid=(blocks,),
        in_specs=[
            by_row(width), by_row(1), by_row(1),
            pl.BlockSpec((None, mem, width), lambda i: (step, 0, 0)),
            whole((1, mem)),
            whole((mem, channels)),
            pl.BlockSpec((None, mem, 128), lambda i: (parts - 1, 0, 0)),
        ],
        out_specs=out_specs,
        out_shape=out_shape,
        scratch_shapes=[pltpu.VMEM((channels, mem), jnp.bfloat16)] if with_stats else [],
        compiler_params=pltpu.CompilerParams(dimension_semantics=("arbitrary",)),
    )(q, row_ok, col_ok, gathered, key_ok, mem_values, gathered)


def body(queries, keys, label_values, class_ids, valid_pixels, keyframe_index):
    fr_dev, pix_dev, width = queries.shape
    channels = label_values.shape[2]
    total_steps, keyframes = keyframe_index.shape
    n_space = lax.axis_size("space")
    pix_all = pix_dev * n_space
    mem_width = keyframes * pix_all
    time_pos = lax.axis_index("tm")
    space_pos = lax.axis_index("space")
    rows = fr_dev * pix_dev
    scale = 3.0 / math.sqrt(width)
    class_range = jnp.arange(channels, dtype=jnp.int32)

    frame_valid = lax.dynamic_slice_in_dim(valid_pixels, time_pos * fr_dev, fr_dev)
    pixel_ids = space_pos * pix_dev + jnp.arange(pix_dev, dtype=jnp.int32)
    row_valid = (pixel_ids[None, :] < frame_valid[:, None]).reshape(rows)
    query_rows = queries.reshape(rows, width)

    flat_kf = keyframe_index.reshape(-1)
    owners = flat_kf // fr_dev
    slots = flat_kf % fr_dev
    later = keyframes * (total_steps - 1)

    kf_keys = jnp.take(keys, slots, axis=0)
    kf_values = jnp.take(label_values, slots[:keyframes], axis=0)
    kf_queries = jnp.take(queries, slots[keyframes:], axis=0)
    parts = [kf_keys, kf_queries, kf_values]
    part_owners = [owners, owners[keyframes:], owners[:keyframes]]
    flat = jnp.concatenate([p.reshape(-1, width) for p in parts], axis=0)
    row_owner = jnp.concatenate(
        [jnp.repeat(o, p[0].size // width) for p, o in zip(parts, part_owners)]
    )
    flat = broadcast_tm(flat, row_owner, "tm", NEAR_TM)
    sizes = [p.size // width for p in parts]
    kf_keys = flat[:sizes[0]].reshape(kf_keys.shape)
    kf_queries = flat[sizes[0]:sizes[0] + sizes[1]].reshape(kf_queries.shape)
    kf_values = flat[sizes[0] + sizes[1]:].reshape(kf_values.shape)

    kf_ids = jnp.take(class_ids, flat_kf, axis=0).astype(jnp.bfloat16)
    kf_ids = kf_ids.reshape(total_steps, keyframes, pix_dev).transpose(1, 2, 0)
    step_keys = kf_keys.reshape(total_steps, keyframes, pix_dev, width)
    aux = jnp.concatenate([kf_values, kf_ids], axis=2)
    aux = jnp.pad(aux, ((0, 0), (0, 0), (0, width - aux.shape[2])))
    packed = jnp.concatenate([step_keys, aux[None]], axis=0)
    gathered = lax.all_gather(packed, "space", axis=2, tiled=True)
    gathered = gathered.reshape(total_steps + 1, mem_width, width)
    mem_values = gathered[total_steps, :, :channels]
    mem_ids = [
        gathered[total_steps, :, channels + s].astype(jnp.int32) for s in range(total_steps)
    ]

    extra_queries = kf_queries.reshape(later, pix_dev, width)
    extra_valid = pixel_ids[None, :] < jnp.take(valid_pixels, flat_kf[keyframes:])[:, None]

    stats = []
    readout = None
    for step in range(total_steps):
        chosen = keyframe_index[step]
        key_valid = (
            jnp.arange(pix_all, dtype=jnp.int32)[None, :]
            < jnp.take(valid_pixels, chosen)[:, None]
        ).reshape(mem_width)
        key_ok = key_valid.astype(jnp.int32)[None, :]
        if step + 1 < total_steps:
            extra = extra_queries[step * keyframes:(step + 1) * keyframes].reshape(-1, width)
            extra_ok = extra_valid[step * keyframes:(step + 1) * keyframes].reshape(-1, 1)
            extra_ok = extra_ok.astype(jnp.int32)
            (part,) = step_pass(
                extra, extra_ok, extra_ok, gathered, step, key_ok, mem_values, scale, False
            )
            part = part.reshape(keyframes, pix_dev, channels)
            next_values = gather_all(part, "space").transpose(1, 0, 2, 3).reshape(
                mem_width, channels
            )
        ok = row_valid.astype(jnp.int32)[:, None]
        readout, col_max, col_total, col_num = step_pass(
            query_rows, ok, ok, gathered, step, key_ok, mem_values, scale, True
        )
        stats.append(jnp.stack([col_max[0], col_total[0], col_num[0]]))
        if step + 1 < total_steps:
            mem_values = next_values

    local = jnp.stack(stats).reshape(total_steps, 3, keyframes, n_space, pix_dev)
    local = local.transpose(3, 1, 0, 2, 4)
    spread = lax.all_to_all(local, "space", 0, 0, tiled=True)
    m, t, n = merge_stats(spread[:, 0], spread[:, 1], spread[:, 2], 0)
    joined = gather_all(jnp.stack([m, t, n]), "tm")
    m, col_total, col_num = merge_stats(joined[:, 0], joined[:, 1], joined[:, 2], 0)

    confidences = []
    for step in range(total_steps):
        chosen = keyframe_index[step]
        key_valid = (
            jnp.arange(pix_all, dtype=jnp.int32)[None, :]
            < jnp.take(valid_pixels, chosen)[:, None]
        ).reshape(mem_width)
        class_match = mem_ids[step][None, :] == class_range[:, None]
        hits = (class_match & key_valid[None, :]).astype(jnp.int32)
        counts = jnp.sum(hits, axis=1)
        all_count = jnp.sum(counts)
        own_ids = lax.dynamic_slice_in_dim(
            mem_ids[step].reshape(keyframes, pix_all), space_pos * pix_dev, pix_dev, 1
        )
        own_valid = pixel_ids[None, :] < jnp.take(valid_pixels, chosen)[:, None]
        own = jnp.take(counts, own_ids)
        own_safe = jnp.where(own_valid, own, 1)
        factor = jnp.sqrt(all_count.astype(jnp.float32) / (channels * own_safe.astype(jnp.float32)))
        conf = jnp.where(own_valid, col_num[step] / col_total[step] * factor, 0.0)
        confidences.append(conf)
    return (readout.reshape(fr_dev, pix_dev, channels), jnp.stack(confidences))


def solution(mesh):
    placed = (
        P("tm", "space", None),
        P("tm", "space", None),
        P("tm", "space", None),
        P(None, "space"),
        P(),
        P(),
    )
    return jax.shard_map(
        body,
        mesh=mesh,
        in_specs=placed,
        out_specs=(P("tm", "space", None), P(None, None, "space")),
        check_vma=False,
    )
```

```python
import functools
import math

import jax
import jax.numpy as jnp
from jax import lax
from jax.experimental import pallas as pl
from jax.experimental.pallas import tpu as pltpu
from jax.sharding import PartitionSpec as P

LOWEST = -1e30
NEAR_TM = 4


def broadcast_tm(value, owner, axis, inner):
    size = lax.axis_size(axis)
    me = lax.axis_index(axis)
    rounds = inner.bit_length() - 1
    assert (1 << rounds) == inner and size % inner == 0
    for r in range(rounds):
        bit = 1 << r
        pairs = [(i, i ^ bit) for i in range(size)]
        got = lax.ppermute(value, axis, pairs)
        take = ((me ^ owner) % inner >> r) == 1
        value = jnp.where(take[:, None], got, value)
    groups = size // inner
    rel = (me // inner - owner // inner) % groups
    ahead = [(i, (i + inner) % size) for i in range(size)]
    behind = [(i, (i - inner) % size) for i in range(size)]
    half = value.shape[0] // 2
    for k in range(1, groups // 2 + 1):
        if 2 * k == groups:
            got_a = lax.ppermute(value[:half], axis, ahead)
            got_b = lax.ppermute(value[half:], axis, behind)
            got = jnp.concatenate([got_a, got_b], axis=0)
            value = jnp.where((rel == k)[:, None], got, value)
        else:
            got_a = lax.ppermute(value, axis, ahead)
            got_b = lax.ppermute(value, axis, behind)
            value = jnp.where((rel == k)[:, None], got_a, value)
            value = jnp.where((rel == groups - k)[:, None], got_b, value)
    return value


def gather_all(value, axis):
    size = lax.axis_size(axis)
    spread = jnp.broadcast_to(value[None], (size,) + value.shape)
    return lax.all_to_all(spread, axis, 0, 0, tiled=True)


def merge_stats(col_max, col_total, col_num, axis):
    top = jnp.max(col_max, axis=axis, keepdims=True)
    keep = jnp.exp(col_max - top)
    total = jnp.sum(col_total * keep, axis=axis)
    num = jnp.sum(col_num * keep, axis=axis)
    return jnp.squeeze(top, axis), total, num


BLOCK_ROWS = 256


def step_kernel(q_ref, row_ok_ref, col_ok_ref, keys_ref, key_ok_ref, aux_ref, *refs,
                scale, step, with_stats, channels, values_from_aux):
    if values_from_aux:
        values = aux_ref[:, :channels]
        out_refs = refs
    else:
        values = refs[0][...]
        out_refs = refs[1:]
    scores = lax.dot_general(
        q_ref[...], keys_ref[...], (((1,), (1,)), ((), ())), preferred_element_type=jnp.float32
    ) * scale
    key_ok = key_ok_ref[...] != 0
    row_ok = row_ok_ref[...] != 0
    masked = jnp.where(key_ok, scores, LOWEST)
    row_max = jnp.max(masked, axis=1, keepdims=True)
    weights = jnp.where(key_ok, jnp.exp(scores - row_max), 0.0)
    total = jnp.sum(weights, axis=1, keepdims=True)
    mixed = jnp.dot(
        weights.astype(jnp.bfloat16), values, preferred_element_type=jnp.float32
    ) / total
    out = jnp.where(row_ok, mixed, 0.0).astype(jnp.bfloat16)
    out_refs[0][...] = out
    if not with_stats:
        return
    cmax_ref, ctot_ref, cnum_ref, onehot_ref = out_refs[1:]

    @pl.when(pl.program_id(0) == 0)
    def _():
        cmax_ref[...] = jnp.full_like(cmax_ref, LOWEST)
        ctot_ref[...] = jnp.zeros_like(ctot_ref)
        cnum_ref[...] = jnp.zeros_like(cnum_ref)
        ids = aux_ref[:, channels + step:channels + step + 1].astype(jnp.float32)
        classes = lax.broadcasted_iota(jnp.int32, (1, channels), 1).astype(jnp.float32)
        onehot = (ids == classes).astype(jnp.float32)
        onehot_ref[...] = jnp.transpose(onehot).astype(jnp.bfloat16)

    picked = jnp.dot(out, onehot_ref[...], preferred_element_type=jnp.float32)
    col_ok = col_ok_ref[...] != 0
    old_max = cmax_ref[...]
    local = jnp.max(jnp.where(col_ok, scores, LOWEST), axis=0, keepdims=True)
    new_max = jnp.maximum(old_max, local)
    keep = jnp.exp(old_max - new_max)
    expo = jnp.where(col_ok, jnp.exp(scores - new_max), 0.0)
    ctot_ref[...] = ctot_ref[...] * keep + jnp.sum(expo, axis=0, keepdims=True)
    cnum_ref[...] = cnum_ref[...] * keep + jnp.sum(expo * picked, axis=0, keepdims=True)
    cmax_ref[...] = new_max


def step_pass(q, row_ok, col_ok, gathered, step, key_ok, mem_values, channels, scale, with_stats):
    rows, width = q.shape
    parts, mem, _ = gathered.shape
    block = min(BLOCK_ROWS, rows)
    assert rows % block == 0
    blocks = rows // block
    whole = lambda shape: pl.BlockSpec(shape, lambda i: (0, 0))
    by_row = lambda cols: pl.BlockSpec((block, cols), lambda i: (i, 0))
    stat = jax.ShapeDtypeStruct((1, mem), jnp.float32)
    out_specs = [by_row(channels)]
    out_shape = [jax.ShapeDtypeStruct((rows, channels), jnp.bfloat16)]
    if with_stats:
        out_specs += [whole((1, mem))] * 3
        out_shape += [stat] * 3
    in_specs = [
        by_row(width), by_row(1), by_row(1),
        pl.BlockSpec((None, mem, width), lambda i: (step, 0, 0)),
        whole((1, mem)),
        pl.BlockSpec((None, mem, 128), lambda i: (parts - 1, 0, 0)),
    ]
    args = [q, row_ok, col_ok, gathered, key_ok, gathered]
    if mem_values is not None:
        in_specs.append(whole((mem, channels)))
        args.append(mem_values)
    kernel = functools.partial(
        step_kernel, scale=scale, step=step, with_stats=with_stats, channels=channels,
        values_from_aux=mem_values is None,
    )
    return pl.pallas_call(
        kernel,
        grid=(blocks,),
        in_specs=in_specs,
        out_specs=out_specs,
        out_shape=out_shape,
        scratch_shapes=[pltpu.VMEM((channels, mem), jnp.bfloat16)] if with_stats else [],
        compiler_params=pltpu.CompilerParams(dimension_semantics=("arbitrary",)),
    )(*args)


def body(queries, keys, label_values, class_ids, valid_pixels, keyframe_index):
    fr_dev, pix_dev, width = queries.shape
    channels = label_values.shape[2]
    total_steps, keyframes = keyframe_index.shape
    n_space = lax.axis_size("space")
    pix_all = pix_dev * n_space
    mem_width = keyframes * pix_all
    time_pos = lax.axis_index("tm")
    space_pos = lax.axis_index("space")
    rows = fr_dev * pix_dev
    scale = 3.0 / math.sqrt(width)
    class_range = jnp.arange(channels, dtype=jnp.int32)

    frame_valid = lax.dynamic_slice_in_dim(valid_pixels, time_pos * fr_dev, fr_dev)
    pixel_ids = space_pos * pix_dev + jnp.arange(pix_dev, dtype=jnp.int32)
    row_valid = (pixel_ids[None, :] < frame_valid[:, None]).reshape(rows)
    query_rows = queries.reshape(rows, width)

    flat_kf = keyframe_index.reshape(-1)
    owners = flat_kf // fr_dev
    slots = flat_kf % fr_dev
    later = keyframes * (total_steps - 1)

    kf_keys = jnp.take(keys, slots, axis=0)
    kf_values = jnp.take(label_values, slots[:keyframes], axis=0)
    kf_queries = jnp.take(queries, slots[keyframes:], axis=0)
    parts = [kf_keys, kf_queries, kf_values]
    part_owners = [owners, owners[keyframes:], owners[:keyframes]]
    flat = jnp.concatenate([p.reshape(-1, width) for p in parts], axis=0)
    row_owner = jnp.concatenate(
        [jnp.repeat(o, p[0].size // width) for p, o in zip(parts, part_owners)]
    )
    flat = broadcast_tm(flat, row_owner, "tm", NEAR_TM)
    sizes = [p.size // width for p in parts]
    kf_keys = flat[:sizes[0]].reshape(kf_keys.shape)
    kf_queries = flat[sizes[0]:sizes[0] + sizes[1]].reshape(kf_queries.shape)
    kf_values = flat[sizes[0] + sizes[1]:].reshape(kf_values.shape)

    kf_class = jnp.take(class_ids, flat_kf, axis=0)
    kf_ok = pixel_ids[None, :] < jnp.take(valid_pixels, flat_kf)[:, None]
    hits = (kf_class[:, :, None] == class_range[None, None, :]) & kf_ok[:, :, None]
    partial = jnp.sum(hits.astype(jnp.int32), axis=1).reshape(total_steps, keyframes, channels)
    partial = jnp.sum(partial, axis=1).astype(jnp.bfloat16)
    kf_ids = kf_class.astype(jnp.bfloat16)
    kf_ids = kf_ids.reshape(total_steps, keyframes, pix_dev).transpose(1, 2, 0)
    step_keys = kf_keys.reshape(total_steps, keyframes, pix_dev, width)
    aux = jnp.concatenate([kf_values, kf_ids], axis=2)
    aux = jnp.pad(aux, ((0, 0), (0, 0), (0, 128 - aux.shape[2])))
    tally = jnp.zeros((keyframes, pix_dev, width - 128), jnp.bfloat16)
    tally = tally.at[0, :total_steps, :channels].set(partial)
    aux = jnp.concatenate([aux, tally], axis=2)
    packed = jnp.concatenate([step_keys, aux[None]], axis=0)
    gathered = lax.all_gather(packed, "space", axis=2, tiled=True)
    gathered = gathered.reshape(total_steps + 1, mem_width, width)
    tallies = gathered[total_steps].reshape(keyframes, n_space, pix_dev, width)
    counts = jnp.sum(
        tallies[0, :, :total_steps, 128:128 + channels].astype(jnp.int32), axis=0
    )
    mem_values = None

    extra_queries = kf_queries.reshape(later, pix_dev, width)
    extra_valid = pixel_ids[None, :] < jnp.take(valid_pixels, flat_kf[keyframes:])[:, None]

    stats = []
    readout = None
    for step in range(total_steps):
        chosen = keyframe_index[step]
        key_valid = (
            jnp.arange(pix_all, dtype=jnp.int32)[None, :]
            < jnp.take(valid_pixels, chosen)[:, None]
        ).reshape(mem_width)
        key_ok = key_valid.astype(jnp.int32)[None, :]
        if step + 1 < total_steps:
            extra = extra_queries[step * keyframes:(step + 1) * keyframes].reshape(-1, width)
            extra_ok = extra_valid[step * keyframes:(step + 1) * keyframes].reshape(-1, 1)
            extra_ok = extra_ok.astype(jnp.int32)
            (part,) = step_pass(
                extra, extra_ok, extra_ok, gathered, step, key_ok, mem_values, channels, scale,
                False,
            )
            part = part.reshape(keyframes, pix_dev, channels)
            next_values = gather_all(part, "space").transpose(1, 0, 2, 3).reshape(
                mem_width, channels
            )
        ok = row_valid.astype(jnp.int32)[:, None]
        readout, col_max, col_total, col_num = step_pass(
            query_rows, ok, ok, gathered, step, key_ok, mem_values, channels, scale, True
        )
        stats.append(jnp.stack([col_max[0], col_total[0], col_num[0]]))
        if step + 1 < total_steps:
            mem_values = next_values

    local = jnp.stack(stats).reshape(total_steps, 3, keyframes, n_space, pix_dev)
    local = local.transpose(3, 1, 0, 2, 4)
    spread = lax.all_to_all(local, "space", 0, 0, tiled=True)
    m, t, n = merge_stats(spread[:, 0], spread[:, 1], spread[:, 2], 0)
    joined = gather_all(jnp.stack([m, t, n]), "tm")
    m, col_total, col_num = merge_stats(joined[:, 0], joined[:, 1], joined[:, 2], 0)

    all_count = jnp.sum(counts, axis=1)
    own_ids = kf_class.reshape(total_steps, keyframes, pix_dev)
    own = jnp.sum(
        jnp.where(own_ids[..., None] == class_range, counts[:, None, None, :], 0), axis=3
    )
    own_valid = kf_ok.reshape(total_steps, keyframes, pix_dev)
    own_safe = jnp.where(own_valid, own, 1)
    factor = jnp.sqrt(
        all_count[:, None, None].astype(jnp.float32) / (channels * own_safe.astype(jnp.float32))
    )
    confidences = jnp.where(own_valid, col_num / col_total * factor, 0.0)
    return (readout.reshape(fr_dev, pix_dev, channels), confidences)


def solution(mesh):
    placed = (
        P("tm", "space", None),
        P("tm", "space", None),
        P("tm", "space", None),
        P(None, "space"),
        P(),
        P(),
    )
    return jax.shard_map(
        body,
        mesh=mesh,
        in_specs=placed,
        out_specs=(P("tm", "space", None), P(None, None, "space")),
        check_vma=False,
    )
```

```python
import functools
import math

import jax
import jax.numpy as jnp
from jax import lax
from jax.experimental import pallas as pl
from jax.experimental.pallas import tpu as pltpu
from jax.sharding import PartitionSpec as P

LOWEST = -1e30
NEAR_TM = 4


def broadcast_tm(value, owner, axis, inner):
    size = lax.axis_size(axis)
    me = lax.axis_index(axis)
    rounds = inner.bit_length() - 1
    assert (1 << rounds) == inner and size % inner == 0
    for r in range(rounds):
        bit = 1 << r
        pairs = [(i, i ^ bit) for i in range(size)]
        got = lax.ppermute(value, axis, pairs)
        take = ((me ^ owner) % inner >> r) == 1
        value = jnp.where(take[:, None], got, value)
    groups = size // inner
    rel = (me // inner - owner // inner) % groups
    ahead = [(i, (i + inner) % size) for i in range(size)]
    behind = [(i, (i - inner) % size) for i in range(size)]
    half = value.shape[0] // 2
    for k in range(1, groups // 2 + 1):
        if 2 * k == groups:
            got_a = lax.ppermute(value[:half], axis, ahead)
            got_b = lax.ppermute(value[half:], axis, behind)
            got = jnp.concatenate([got_a, got_b], axis=0)
            value = jnp.where((rel == k)[:, None], got, value)
        else:
            got_a = lax.ppermute(value, axis, ahead)
            got_b = lax.ppermute(value, axis, behind)
            value = jnp.where((rel == k)[:, None], got_a, value)
            value = jnp.where((rel == groups - k)[:, None], got_b, value)
    return value


def gather_all(value, axis):
    size = lax.axis_size(axis)
    spread = jnp.broadcast_to(value[None], (size,) + value.shape)
    return lax.all_to_all(spread, axis, 0, 0, tiled=True)


def merge_stats(col_max, col_total, col_num, axis):
    top = jnp.max(col_max, axis=axis, keepdims=True)
    keep = jnp.exp(col_max - top)
    total = jnp.sum(col_total * keep, axis=axis)
    num = jnp.sum(col_num * keep, axis=axis)
    return jnp.squeeze(top, axis), total, num


BLOCK_ROWS = 256


def step_kernel(q_ref, row_ok_ref, col_ok_ref, keys_ref, key_ok_ref, aux_ref, *refs,
                scale, step, with_stats, channels, values_from_aux):
    if values_from_aux:
        values = aux_ref[:, :channels]
        out_refs = refs
    else:
        values = refs[0][...]
        out_refs = refs[1:]
    scores = lax.dot_general(
        q_ref[...], keys_ref[...], (((1,), (1,)), ((), ())), preferred_element_type=jnp.float32
    ) * scale
    key_ok = key_ok_ref[...] != 0
    row_ok = row_ok_ref[...] != 0
    masked = jnp.where(key_ok, scores, LOWEST)
    row_max = jnp.max(masked, axis=1, keepdims=True)
    weights = jnp.where(key_ok, jnp.exp(scores - row_max), 0.0)
    total = jnp.sum(weights, axis=1, keepdims=True)
    mixed = jnp.dot(
        weights.astype(jnp.bfloat16), values, preferred_element_type=jnp.float32
    ) / total
    out = jnp.where(row_ok, mixed, 0.0).astype(jnp.bfloat16)
    out_refs[0][...] = out
    if not with_stats:
        return
    cmax_ref, ctot_ref, cnum_ref, onehot_ref = out_refs[1:]

    @pl.when(pl.program_id(0) == 0)
    def _():
        cmax_ref[...] = jnp.full_like(cmax_ref, LOWEST)
        ctot_ref[...] = jnp.zeros_like(ctot_ref)
        cnum_ref[...] = jnp.zeros_like(cnum_ref)
        ids = aux_ref[:, channels + step:channels + step + 1].astype(jnp.float32)
        classes = lax.broadcasted_iota(jnp.int32, (1, channels), 1).astype(jnp.float32)
        onehot = (ids == classes).astype(jnp.float32)
        onehot_ref[...] = jnp.transpose(onehot).astype(jnp.bfloat16)

    out_t = jnp.transpose(out.astype(jnp.float32)).astype(jnp.bfloat16)
    col_ok = col_ok_ref[...] != 0
    old_max = cmax_ref[...]
    local = jnp.max(jnp.where(col_ok, scores, LOWEST), axis=0, keepdims=True)
    new_max = jnp.maximum(old_max, local)
    keep = jnp.exp(old_max - new_max)
    expo = jnp.where(col_ok, jnp.exp(scores - new_max), 0.0)
    ctot_ref[...] = ctot_ref[...] * keep + jnp.sum(expo, axis=0, keepdims=True)
    high = expo.astype(jnp.bfloat16)
    low = (expo - high.astype(jnp.float32)).astype(jnp.bfloat16)
    by_class = jnp.dot(out_t, high, preferred_element_type=jnp.float32) + jnp.dot(
        out_t, low, preferred_element_type=jnp.float32
    )
    num = jnp.sum(by_class * onehot_ref[...].astype(jnp.float32), axis=0, keepdims=True)
    cnum_ref[...] = cnum_ref[...] * keep + num
    cmax_ref[...] = new_max


def step_pass(q, row_ok, col_ok, gathered, step, key_ok, mem_values, channels, scale, with_stats):
    rows, width = q.shape
    parts, mem, _ = gathered.shape
    block = min(BLOCK_ROWS, rows)
    assert rows % block == 0
    blocks = rows // block
    whole = lambda shape: pl.BlockSpec(shape, lambda i: (0, 0))
    by_row = lambda cols: pl.BlockSpec((block, cols), lambda i: (i, 0))
    stat = jax.ShapeDtypeStruct((1, mem), jnp.float32)
    out_specs = [by_row(channels)]
    out_shape = [jax.ShapeDtypeStruct((rows, channels), jnp.bfloat16)]
    if with_stats:
        out_specs += [whole((1, mem))] * 3
        out_shape += [stat] * 3
    in_specs = [
        by_row(width), by_row(1), by_row(1),
        pl.BlockSpec((None, mem, width), lambda i: (step, 0, 0)),
        whole((1, mem)),
        pl.BlockSpec((None, mem, 128), lambda i: (parts - 1, 0, 0)),
    ]
    args = [q, row_ok, col_ok, gathered, key_ok, gathered]
    if mem_values is not None:
        in_specs.append(whole((mem, channels)))
        args.append(mem_values)
    kernel = functools.partial(
        step_kernel, scale=scale, step=step, with_stats=with_stats, channels=channels,
        values_from_aux=mem_values is None,
    )
    return pl.pallas_call(
        kernel,
        grid=(blocks,),
        in_specs=in_specs,
        out_specs=out_specs,
        out_shape=out_shape,
        scratch_shapes=[pltpu.VMEM((channels, mem), jnp.bfloat16)] if with_stats else [],
        compiler_params=pltpu.CompilerParams(dimension_semantics=("arbitrary",)),
    )(*args)


def body(queries, keys, label_values, class_ids, valid_pixels, keyframe_index):
    fr_dev, pix_dev, width = queries.shape
    channels = label_values.shape[2]
    total_steps, keyframes = keyframe_index.shape
    n_space = lax.axis_size("space")
    pix_all = pix_dev * n_space
    mem_width = keyframes * pix_all
    time_pos = lax.axis_index("tm")
    space_pos = lax.axis_index("space")
    rows = fr_dev * pix_dev
    scale = 3.0 / math.sqrt(width)
    class_range = jnp.arange(channels, dtype=jnp.int32)

    frame_valid = lax.dynamic_slice_in_dim(valid_pixels, time_pos * fr_dev, fr_dev)
    pixel_ids = space_pos * pix_dev + jnp.arange(pix_dev, dtype=jnp.int32)
    row_valid = (pixel_ids[None, :] < frame_valid[:, None]).reshape(rows)
    query_rows = queries.reshape(rows, width)

    flat_kf = keyframe_index.reshape(-1)
    owners = flat_kf // fr_dev
    slots = flat_kf % fr_dev
    later = keyframes * (total_steps - 1)

    kf_keys = jnp.take(keys, slots, axis=0)
    kf_values = jnp.take(label_values, slots[:keyframes], axis=0)
    kf_queries = jnp.take(queries, slots[keyframes:], axis=0)
    parts = [kf_keys, kf_queries, kf_values]
    part_owners = [owners, owners[keyframes:], owners[:keyframes]]
    flat = jnp.concatenate([p.reshape(-1, width) for p in parts], axis=0)
    row_owner = jnp.concatenate(
        [jnp.repeat(o, p[0].size // width) for p, o in zip(parts, part_owners)]
    )
    flat = broadcast_tm(flat, row_owner, "tm", NEAR_TM)
    sizes = [p.size // width for p in parts]
    kf_keys = flat[:sizes[0]].reshape(kf_keys.shape)
    kf_queries = flat[sizes[0]:sizes[0] + sizes[1]].reshape(kf_queries.shape)
    kf_values = flat[sizes[0] + sizes[1]:].reshape(kf_values.shape)

    kf_class = jnp.take(class_ids, flat_kf, axis=0)
    kf_ok = pixel_ids[None, :] < jnp.take(valid_pixels, flat_kf)[:, None]
    hits = (kf_class[:, :, None] == class_range[None, None, :]) & kf_ok[:, :, None]
    partial = jnp.sum(hits.astype(jnp.int32), axis=1).reshape(total_steps, keyframes, channels)
    partial = jnp.sum(partial, axis=1).astype(jnp.bfloat16)
    kf_ids = kf_class.astype(jnp.bfloat16)
    kf_ids = kf_ids.reshape(total_steps, keyframes, pix_dev).transpose(1, 2, 0)
    step_keys = kf_keys.reshape(total_steps, keyframes, pix_dev, width)
    aux = jnp.concatenate([kf_values, kf_ids], axis=2)
    aux = jnp.pad(aux, ((0, 0), (0, 0), (0, 128 - aux.shape[2])))
    tally = jnp.zeros((keyframes, pix_dev, width - 128), jnp.bfloat16)
    tally = tally.at[0, :total_steps, :channels].set(partial)
    aux = jnp.concatenate([aux, tally], axis=2)
    packed = jnp.concatenate([step_keys, aux[None]], axis=0)
    gathered = lax.all_gather(packed, "space", axis=2, tiled=True)
    gathered = gathered.reshape(total_steps + 1, mem_width, width)
    tallies = gathered[total_steps].reshape(keyframes, n_space, pix_dev, width)
    counts = jnp.sum(
        tallies[0, :, :total_steps, 128:128 + channels].astype(jnp.int32), axis=0
    )
    mem_values = None

    extra_queries = kf_queries.reshape(later, pix_dev, width)
    extra_valid = pixel_ids[None, :] < jnp.take(valid_pixels, flat_kf[keyframes:])[:, None]

    stats = []
    readout = None
    for step in range(total_steps):
        chosen = keyframe_index[step]
        key_valid = (
            jnp.arange(pix_all, dtype=jnp.int32)[None, :]
            < jnp.take(valid_pixels, chosen)[:, None]
        ).reshape(mem_width)
        key_ok = key_valid.astype(jnp.int32)[None, :]
        if step + 1 < total_steps:
            extra = extra_queries[step * keyframes:(step + 1) * keyframes].reshape(-1, width)
            extra_ok = extra_valid[step * keyframes:(step + 1) * keyframes].reshape(-1, 1)
            extra_ok = extra_ok.astype(jnp.int32)
            (part,) = step_pass(
                extra, extra_ok, extra_ok, gathered, step, key_ok, mem_values, channels, scale,
                False,
            )
            part = part.reshape(keyframes, pix_dev, channels)
            next_values = gather_all(part, "space").transpose(1, 0, 2, 3).reshape(
                mem_width, channels
            )
        ok = row_valid.astype(jnp.int32)[:, None]
        readout, col_max, col_total, col_num = step_pass(
            query_rows, ok, ok, gathered, step, key_ok, mem_values, channels, scale, True
        )
        stats.append(jnp.stack([col_max[0], col_total[0], col_num[0]]))
        if step + 1 < total_steps:
            mem_values = next_values

    local = jnp.stack(stats).reshape(total_steps, 3, keyframes, n_space, pix_dev)
    local = local.transpose(3, 1, 0, 2, 4)
    spread = lax.all_to_all(local, "space", 0, 0, tiled=True)
    m, t, n = merge_stats(spread[:, 0], spread[:, 1], spread[:, 2], 0)
    joined = gather_all(jnp.stack([m, t, n]), "tm")
    m, col_total, col_num = merge_stats(joined[:, 0], joined[:, 1], joined[:, 2], 0)

    all_count = jnp.sum(counts, axis=1)
    own_ids = kf_class.reshape(total_steps, keyframes, pix_dev)
    own = jnp.sum(
        jnp.where(own_ids[..., None] == class_range, counts[:, None, None, :], 0), axis=3
    )
    own_valid = kf_ok.reshape(total_steps, keyframes, pix_dev)
    own_safe = jnp.where(own_valid, own, 1)
    factor = jnp.sqrt(
        all_count[:, None, None].astype(jnp.float32) / (channels * own_safe.astype(jnp.float32))
    )
    confidences = jnp.where(own_valid, col_num / col_total * factor, 0.0)
    return (readout.reshape(fr_dev, pix_dev, channels), confidences)


def solution(mesh):
    placed = (
        P("tm", "space", None),
        P("tm", "space", None),
        P("tm", "space", None),
        P(None, "space"),
        P(),
        P(),
    )
    return jax.shard_map(
        body,
        mesh=mesh,
        in_specs=placed,
        out_specs=(P("tm", "space", None), P(None, None, "space")),
        check_vma=False,
    )
```

```python
import functools
import math

import jax
import jax.numpy as jnp
from jax import lax
from jax.experimental import pallas as pl
from jax.experimental.pallas import tpu as pltpu
from jax.sharding import PartitionSpec as P

LOWEST = -1e30
NEAR_TM = 4


def broadcast_tm(value, owner, axis, inner):
    size = lax.axis_size(axis)
    me = lax.axis_index(axis)
    rounds = inner.bit_length() - 1
    assert (1 << rounds) == inner and size % inner == 0
    for r in range(rounds):
        bit = 1 << r
        pairs = [(i, i ^ bit) for i in range(size)]
        got = lax.ppermute(value, axis, pairs)
        take = ((me ^ owner) % inner >> r) == 1
        value = jnp.where(take[:, None], got, value)
    groups = size // inner
    rel = (me // inner - owner // inner) % groups
    ahead = [(i, (i + inner) % size) for i in range(size)]
    behind = [(i, (i - inner) % size) for i in range(size)]
    half = value.shape[0] // 2
    for k in range(1, groups // 2 + 1):
        if 2 * k == groups:
            got_a = lax.ppermute(value[:half], axis, ahead)
            got_b = lax.ppermute(value[half:], axis, behind)
            got = jnp.concatenate([got_a, got_b], axis=0)
            value = jnp.where((rel == k)[:, None], got, value)
        else:
            got_a = lax.ppermute(value, axis, ahead)
            got_b = lax.ppermute(value, axis, behind)
            value = jnp.where((rel == k)[:, None], got_a, value)
            value = jnp.where((rel == groups - k)[:, None], got_b, value)
    return value


def gather_all(value, axis):
    size = lax.axis_size(axis)
    spread = jnp.broadcast_to(value[None], (size,) + value.shape)
    return lax.all_to_all(spread, axis, 0, 0, tiled=True)


def merge_stats(col_max, col_total, col_num, axis):
    top = jnp.max(col_max, axis=axis, keepdims=True)
    keep = jnp.exp(col_max - top)
    total = jnp.sum(col_total * keep, axis=axis)
    num = jnp.sum(col_num * keep, axis=axis)
    return jnp.squeeze(top, axis), total, num


BLOCK_ROWS = 256


def step_kernel(q_ref, row_ok_ref, col_ok_ref, keys_ref, key_ok_ref, aux_ref, *refs,
                scale, step, with_stats, channels, values_from_aux):
    if values_from_aux:
        values = aux_ref[:, :channels]
        out_refs = refs
    else:
        values = refs[0][...]
        out_refs = refs[1:]
    scores = lax.dot_general(
        q_ref[...], keys_ref[...], (((1,), (1,)), ((), ())), preferred_element_type=jnp.float32
    ) * scale
    key_ok = key_ok_ref[...] != 0
    row_ok = row_ok_ref[...] != 0
    masked = jnp.where(key_ok, scores, LOWEST)
    row_max = jnp.max(masked, axis=1, keepdims=True)
    weights = jnp.exp(masked - row_max)
    total = jnp.sum(weights, axis=1, keepdims=True)
    mixed = jnp.dot(
        weights.astype(jnp.bfloat16), values, preferred_element_type=jnp.float32
    ) / total
    out = jnp.where(row_ok, mixed, 0.0).astype(jnp.bfloat16)
    out_refs[0][...] = out
    if not with_stats:
        return
    cmax_ref, ctot_ref, cnum_ref, onehot_ref = out_refs[1:]

    @pl.when(pl.program_id(0) == 0)
    def _():
        cmax_ref[...] = jnp.full_like(cmax_ref, LOWEST)
        ctot_ref[...] = jnp.zeros_like(ctot_ref)
        cnum_ref[...] = jnp.zeros_like(cnum_ref)
        ids = aux_ref[:, channels + step:channels + step + 1].astype(jnp.float32)
        classes = lax.broadcasted_iota(jnp.int32, (1, channels), 1).astype(jnp.float32)
        onehot = (ids == classes).astype(jnp.float32)
        onehot_ref[...] = jnp.transpose(onehot).astype(jnp.bfloat16)

    picked = jnp.dot(out, onehot_ref[...], preferred_element_type=jnp.float32)
    col_ok = col_ok_ref[...] != 0
    old_max = cmax_ref[...]
    col_scores = jnp.where(col_ok, scores, LOWEST)
    local = jnp.max(col_scores, axis=0, keepdims=True)
    new_max = jnp.maximum(old_max, local)
    keep = jnp.exp(old_max - new_max)
    expo = jnp.exp(col_scores - new_max)
    ctot_ref[...] = ctot_ref[...] * keep + jnp.sum(expo, axis=0, keepdims=True)
    cnum_ref[...] = cnum_ref[...] * keep + jnp.sum(expo * picked, axis=0, keepdims=True)
    cmax_ref[...] = new_max


def step_pass(q, row_ok, col_ok, gathered, step, key_ok, mem_values, channels, scale, with_stats):
    rows, width = q.shape
    parts, mem, _ = gathered.shape
    block = min(BLOCK_ROWS, rows)
    assert rows % block == 0
    blocks = rows // block
    whole = lambda shape: pl.BlockSpec(shape, lambda i: (0, 0))
    by_row = lambda cols: pl.BlockSpec((block, cols), lambda i: (i, 0))
    stat = jax.ShapeDtypeStruct((1, mem), jnp.float32)
    out_specs = [by_row(channels)]
    out_shape = [jax.ShapeDtypeStruct((rows, channels), jnp.bfloat16)]
    if with_stats:
        out_specs += [whole((1, mem))] * 3
        out_shape += [stat] * 3
    in_specs = [
        by_row(width), by_row(1), by_row(1),
        pl.BlockSpec((None, mem, width), lambda i: (step, 0, 0)),
        whole((1, mem)),
        pl.BlockSpec((None, mem, 128), lambda i: (parts - 1, 0, 0)),
    ]
    args = [q, row_ok, col_ok, gathered, key_ok, gathered]
    if mem_values is not None:
        in_specs.append(whole((mem, channels)))
        args.append(mem_values)
    kernel = functools.partial(
        step_kernel, scale=scale, step=step, with_stats=with_stats, channels=channels,
        values_from_aux=mem_values is None,
    )
    return pl.pallas_call(
        kernel,
        grid=(blocks,),
        in_specs=in_specs,
        out_specs=out_specs,
        out_shape=out_shape,
        scratch_shapes=[pltpu.VMEM((channels, mem), jnp.bfloat16)] if with_stats else [],
        compiler_params=pltpu.CompilerParams(dimension_semantics=("arbitrary",)),
    )(*args)


def body(queries, keys, label_values, class_ids, valid_pixels, keyframe_index):
    fr_dev, pix_dev, width = queries.shape
    channels = label_values.shape[2]
    total_steps, keyframes = keyframe_index.shape
    n_space = lax.axis_size("space")
    pix_all = pix_dev * n_space
    mem_width = keyframes * pix_all
    time_pos = lax.axis_index("tm")
    space_pos = lax.axis_index("space")
    rows = fr_dev * pix_dev
    scale = 3.0 / math.sqrt(width)
    class_range = jnp.arange(channels, dtype=jnp.int32)

    frame_valid = lax.dynamic_slice_in_dim(valid_pixels, time_pos * fr_dev, fr_dev)
    pixel_ids = space_pos * pix_dev + jnp.arange(pix_dev, dtype=jnp.int32)
    row_valid = (pixel_ids[None, :] < frame_valid[:, None]).reshape(rows)
    query_rows = queries.reshape(rows, width)

    flat_kf = keyframe_index.reshape(-1)
    owners = flat_kf // fr_dev
    slots = flat_kf % fr_dev
    later = keyframes * (total_steps - 1)

    kf_keys = jnp.take(keys, slots, axis=0)
    kf_values = jnp.take(label_values, slots[:keyframes], axis=0)
    kf_queries = jnp.take(queries, slots[keyframes:], axis=0)
    parts = [kf_keys, kf_queries, kf_values]
    part_owners = [owners, owners[keyframes:], owners[:keyframes]]
    flat = jnp.concatenate([p.reshape(-1, width) for p in parts], axis=0)
    row_owner = jnp.concatenate(
        [jnp.repeat(o, p[0].size // width) for p, o in zip(parts, part_owners)]
    )
    flat = broadcast_tm(flat, row_owner, "tm", NEAR_TM)
    sizes = [p.size // width for p in parts]
    kf_keys = flat[:sizes[0]].reshape(kf_keys.shape)
    kf_queries = flat[sizes[0]:sizes[0] + sizes[1]].reshape(kf_queries.shape)
    kf_values = flat[sizes[0] + sizes[1]:].reshape(kf_values.shape)

    kf_class = jnp.take(class_ids, flat_kf, axis=0)
    kf_ok = pixel_ids[None, :] < jnp.take(valid_pixels, flat_kf)[:, None]
    hits = (kf_class[:, :, None] == class_range[None, None, :]) & kf_ok[:, :, None]
    partial = jnp.sum(hits.astype(jnp.int32), axis=1).reshape(total_steps, keyframes, channels)
    partial = jnp.sum(partial, axis=1).astype(jnp.bfloat16)
    kf_ids = kf_class.astype(jnp.bfloat16)
    kf_ids = kf_ids.reshape(total_steps, keyframes, pix_dev).transpose(1, 2, 0)
    step_keys = kf_keys.reshape(total_steps, keyframes, pix_dev, width)
    aux = jnp.concatenate([kf_values, kf_ids], axis=2)
    aux = jnp.pad(aux, ((0, 0), (0, 0), (0, 128 - aux.shape[2])))
    tally = jnp.zeros((keyframes, pix_dev, width - 128), jnp.bfloat16)
    tally = tally.at[0, :total_steps, :channels].set(partial)
    aux = jnp.concatenate([aux, tally], axis=2)
    packed = jnp.concatenate([step_keys, aux[None]], axis=0)
    gathered = lax.all_gather(packed, "space", axis=2, tiled=True)
    gathered = gathered.reshape(total_steps + 1, mem_width, width)
    tallies = gathered[total_steps].reshape(keyframes, n_space, pix_dev, width)
    counts = jnp.sum(
        tallies[0, :, :total_steps, 128:128 + channels].astype(jnp.int32), axis=0
    )
    mem_values = None

    extra_queries = kf_queries.reshape(later, pix_dev, width)
    extra_valid = pixel_ids[None, :] < jnp.take(valid_pixels, flat_kf[keyframes:])[:, None]

    stats = []
    readout = None
    for step in range(total_steps):
        chosen = keyframe_index[step]
        key_valid = (
            jnp.arange(pix_all, dtype=jnp.int32)[None, :]
            < jnp.take(valid_pixels, chosen)[:, None]
        ).reshape(mem_width)
        key_ok = key_valid.astype(jnp.int32)[None, :]
        if step + 1 < total_steps:
            extra = extra_queries[step * keyframes:(step + 1) * keyframes].reshape(-1, width)
            extra_ok = extra_valid[step * keyframes:(step + 1) * keyframes].reshape(-1, 1)
            extra_ok = extra_ok.astype(jnp.int32)
            (part,) = step_pass(
                extra, extra_ok, extra_ok, gathered, step, key_ok, mem_values, channels, scale,
                False,
            )
            part = part.reshape(keyframes, pix_dev, channels)
            next_values = gather_all(part, "space").transpose(1, 0, 2, 3).reshape(
                mem_width, channels
            )
        ok = row_valid.astype(jnp.int32)[:, None]
        readout, col_max, col_total, col_num = step_pass(
            query_rows, ok, ok, gathered, step, key_ok, mem_values, channels, scale, True
        )
        stats.append(jnp.stack([col_max[0], col_total[0], col_num[0]]))
        if step + 1 < total_steps:
            mem_values = next_values

    local = jnp.stack(stats).reshape(total_steps, 3, keyframes, n_space, pix_dev)
    local = local.transpose(3, 1, 0, 2, 4)
    spread = lax.all_to_all(local, "space", 0, 0, tiled=True)
    m, t, n = merge_stats(spread[:, 0], spread[:, 1], spread[:, 2], 0)
    joined = gather_all(jnp.stack([m, t, n]), "tm")
    m, col_total, col_num = merge_stats(joined[:, 0], joined[:, 1], joined[:, 2], 0)

    all_count = jnp.sum(counts, axis=1)
    own_ids = kf_class.reshape(total_steps, keyframes, pix_dev)
    own = jnp.sum(
        jnp.where(own_ids[..., None] == class_range, counts[:, None, None, :], 0), axis=3
    )
    own_valid = kf_ok.reshape(total_steps, keyframes, pix_dev)
    own_safe = jnp.where(own_valid, own, 1)
    factor = jnp.sqrt(
        all_count[:, None, None].astype(jnp.float32) / (channels * own_safe.astype(jnp.float32))
    )
    confidences = jnp.where(own_valid, col_num / col_total * factor, 0.0)
    return (readout.reshape(fr_dev, pix_dev, channels), confidences)


def solution(mesh):
    placed = (
        P("tm", "space", None),
        P("tm", "space", None),
        P("tm", "space", None),
        P(None, "space"),
        P(),
        P(),
    )
    return jax.shard_map(
        body,
        mesh=mesh,
        in_specs=placed,
        out_specs=(P("tm", "space", None), P(None, None, "space")),
        check_vma=False,
    )
```

```python
import functools
import math

import jax
import jax.numpy as jnp
from jax import lax
from jax.experimental import pallas as pl
from jax.experimental.pallas import tpu as pltpu
from jax.sharding import PartitionSpec as P

LOWEST = -1e30
NEAR_TM = 4


def broadcast_tm(value, owner, axis, inner):
    size = lax.axis_size(axis)
    me = lax.axis_index(axis)
    rounds = inner.bit_length() - 1
    assert (1 << rounds) == inner and size % inner == 0
    for r in range(rounds):
        bit = 1 << r
        pairs = [(i, i ^ bit) for i in range(size)]
        got = lax.ppermute(value, axis, pairs)
        take = ((me ^ owner) % inner >> r) == 1
        value = jnp.where(take[:, None], got, value)
    groups = size // inner
    rel = (me // inner - owner // inner) % groups
    ahead = [(i, (i + inner) % size) for i in range(size)]
    behind = [(i, (i - inner) % size) for i in range(size)]
    half = value.shape[0] // 2
    for k in range(1, groups // 2 + 1):
        if 2 * k == groups:
            got_a = lax.ppermute(value[:half], axis, ahead)
            got_b = lax.ppermute(value[half:], axis, behind)
            got = jnp.concatenate([got_a, got_b], axis=0)
            value = jnp.where((rel == k)[:, None], got, value)
        else:
            got_a = lax.ppermute(value, axis, ahead)
            got_b = lax.ppermute(value, axis, behind)
            value = jnp.where((rel == k)[:, None], got_a, value)
            value = jnp.where((rel == groups - k)[:, None], got_b, value)
    return value


def gather_all(value, axis):
    size = lax.axis_size(axis)
    spread = jnp.broadcast_to(value[None], (size,) + value.shape)
    return lax.all_to_all(spread, axis, 0, 0, tiled=True)


def merge_stats(col_max, col_total, col_num, axis):
    top = jnp.max(col_max, axis=axis, keepdims=True)
    keep = jnp.exp(col_max - top)
    total = jnp.sum(col_total * keep, axis=axis)
    num = jnp.sum(col_num * keep, axis=axis)
    return jnp.squeeze(top, axis), total, num


def reduce_tm(m, t, n, axis):
    size = lax.axis_size(axis)
    rounds = size.bit_length() - 1
    assert (1 << rounds) == size
    for r in range(rounds):
        bit = 1 << r
        pairs = [(i, i ^ bit) for i in range(size)]
        gm, gt, gn = lax.ppermute(jnp.stack([m, t, n]), axis, pairs)
        top = jnp.maximum(m, gm)
        keep, got_keep = jnp.exp(m - top), jnp.exp(gm - top)
        t = t * keep + gt * got_keep
        n = n * keep + gn * got_keep
        m = top
    return m, t, n


BLOCK_ROWS = 256


def step_kernel(q_ref, row_ok_ref, col_ok_ref, keys_ref, key_ok_ref, aux_ref, *refs,
                scale, step, with_stats, channels, values_from_aux):
    if values_from_aux:
        values = aux_ref[:, :channels]
        out_refs = refs
    else:
        values = refs[0][...]
        out_refs = refs[1:]
    scores = lax.dot_general(
        q_ref[...], keys_ref[...], (((1,), (1,)), ((), ())), preferred_element_type=jnp.float32
    ) * scale
    key_ok = key_ok_ref[...] != 0
    row_ok = row_ok_ref[...] != 0
    masked = jnp.where(key_ok, scores, LOWEST)
    row_max = jnp.max(masked, axis=1, keepdims=True)
    weights = jnp.exp(masked - row_max)
    total = jnp.sum(weights, axis=1, keepdims=True)
    mixed = jnp.dot(
        weights.astype(jnp.bfloat16), values, preferred_element_type=jnp.float32
    ) / total
    out = jnp.where(row_ok, mixed, 0.0).astype(jnp.bfloat16)
    out_refs[0][...] = out
    if not with_stats:
        return
    cmax_ref, ctot_ref, cnum_ref, onehot_ref = out_refs[1:]

    @pl.when(pl.program_id(0) == 0)
    def _():
        cmax_ref[...] = jnp.full_like(cmax_ref, LOWEST)
        ctot_ref[...] = jnp.zeros_like(ctot_ref)
        cnum_ref[...] = jnp.zeros_like(cnum_ref)
        ids = aux_ref[:, channels + step:channels + step + 1].astype(jnp.float32)
        classes = lax.broadcasted_iota(jnp.int32, (1, channels), 1).astype(jnp.float32)
        onehot = (ids == classes).astype(jnp.float32)
        onehot_ref[...] = jnp.transpose(onehot).astype(jnp.bfloat16)

    picked = jnp.dot(out, onehot_ref[...], preferred_element_type=jnp.float32)
    col_ok = col_ok_ref[...] != 0
    old_max = cmax_ref[...]
    col_scores = jnp.where(col_ok, scores, LOWEST)
    local = jnp.max(col_scores, axis=0, keepdims=True)
    new_max = jnp.maximum(old_max, local)
    keep = jnp.exp(old_max - new_max)
    expo = jnp.exp(col_scores - new_max)
    ctot_ref[...] = ctot_ref[...] * keep + jnp.sum(expo, axis=0, keepdims=True)
    cnum_ref[...] = cnum_ref[...] * keep + jnp.sum(expo * picked, axis=0, keepdims=True)
    cmax_ref[...] = new_max


def step_pass(q, row_ok, col_ok, gathered, step, key_ok, mem_values, channels, scale, with_stats):
    rows, width = q.shape
    parts, mem, _ = gathered.shape
    block = min(BLOCK_ROWS, rows)
    assert rows % block == 0
    blocks = rows // block
    whole = lambda shape: pl.BlockSpec(shape, lambda i: (0, 0))
    by_row = lambda cols: pl.BlockSpec((block, cols), lambda i: (i, 0))
    stat = jax.ShapeDtypeStruct((1, mem), jnp.float32)
    out_specs = [by_row(channels)]
    out_shape = [jax.ShapeDtypeStruct((rows, channels), jnp.bfloat16)]
    if with_stats:
        out_specs += [whole((1, mem))] * 3
        out_shape += [stat] * 3
    in_specs = [
        by_row(width), by_row(1), by_row(1),
        pl.BlockSpec((None, mem, width), lambda i: (step, 0, 0)),
        whole((1, mem)),
        pl.BlockSpec((None, mem, 128), lambda i: (parts - 1, 0, 0)),
    ]
    args = [q, row_ok, col_ok, gathered, key_ok, gathered]
    if mem_values is not None:
        in_specs.append(whole((mem, channels)))
        args.append(mem_values)
    kernel = functools.partial(
        step_kernel, scale=scale, step=step, with_stats=with_stats, channels=channels,
        values_from_aux=mem_values is None,
    )
    return pl.pallas_call(
        kernel,
        grid=(blocks,),
        in_specs=in_specs,
        out_specs=out_specs,
        out_shape=out_shape,
        scratch_shapes=[pltpu.VMEM((channels, mem), jnp.bfloat16)] if with_stats else [],
        compiler_params=pltpu.CompilerParams(dimension_semantics=("arbitrary",)),
    )(*args)


def body(queries, keys, label_values, class_ids, valid_pixels, keyframe_index):
    fr_dev, pix_dev, width = queries.shape
    channels = label_values.shape[2]
    total_steps, keyframes = keyframe_index.shape
    n_space = lax.axis_size("space")
    pix_all = pix_dev * n_space
    mem_width = keyframes * pix_all
    time_pos = lax.axis_index("tm")
    space_pos = lax.axis_index("space")
    rows = fr_dev * pix_dev
    scale = 3.0 / math.sqrt(width)
    class_range = jnp.arange(channels, dtype=jnp.int32)

    frame_valid = lax.dynamic_slice_in_dim(valid_pixels, time_pos * fr_dev, fr_dev)
    pixel_ids = space_pos * pix_dev + jnp.arange(pix_dev, dtype=jnp.int32)
    row_valid = (pixel_ids[None, :] < frame_valid[:, None]).reshape(rows)
    query_rows = queries.reshape(rows, width)

    flat_kf = keyframe_index.reshape(-1)
    owners = flat_kf // fr_dev
    slots = flat_kf % fr_dev
    later = keyframes * (total_steps - 1)

    kf_keys = jnp.take(keys, slots, axis=0)
    kf_values = jnp.take(label_values, slots[:keyframes], axis=0)
    kf_queries = jnp.take(queries, slots[keyframes:], axis=0)
    parts = [kf_keys, kf_queries, kf_values]
    part_owners = [owners, owners[keyframes:], owners[:keyframes]]
    flat = jnp.concatenate([p.reshape(-1, width) for p in parts], axis=0)
    row_owner = jnp.concatenate(
        [jnp.repeat(o, p[0].size // width) for p, o in zip(parts, part_owners)]
    )
    flat = broadcast_tm(flat, row_owner, "tm", NEAR_TM)
    sizes = [p.size // width for p in parts]
    kf_keys = flat[:sizes[0]].reshape(kf_keys.shape)
    kf_queries = flat[sizes[0]:sizes[0] + sizes[1]].reshape(kf_queries.shape)
    kf_values = flat[sizes[0] + sizes[1]:].reshape(kf_values.shape)

    kf_class = jnp.take(class_ids, flat_kf, axis=0)
    kf_ok = pixel_ids[None, :] < jnp.take(valid_pixels, flat_kf)[:, None]
    hits = (kf_class[:, :, None] == class_range[None, None, :]) & kf_ok[:, :, None]
    partial = jnp.sum(hits.astype(jnp.int32), axis=1).reshape(total_steps, keyframes, channels)
    partial = jnp.sum(partial, axis=1).astype(jnp.bfloat16)
    kf_ids = kf_class.astype(jnp.bfloat16)
    kf_ids = kf_ids.reshape(total_steps, keyframes, pix_dev).transpose(1, 2, 0)
    step_keys = kf_keys.reshape(total_steps, keyframes, pix_dev, width)
    aux = jnp.concatenate([kf_values, kf_ids], axis=2)
    aux = jnp.pad(aux, ((0, 0), (0, 0), (0, 128 - aux.shape[2])))
    tally = jnp.zeros((keyframes, pix_dev, width - 128), jnp.bfloat16)
    tally = tally.at[0, :total_steps, :channels].set(partial)
    aux = jnp.concatenate([aux, tally], axis=2)
    packed = jnp.concatenate([step_keys, aux[None]], axis=0)
    gathered = lax.all_gather(packed, "space", axis=2, tiled=True)
    gathered = gathered.reshape(total_steps + 1, mem_width, width)
    tallies = gathered[total_steps].reshape(keyframes, n_space, pix_dev, width)
    counts = jnp.sum(
        tallies[0, :, :total_steps, 128:128 + channels].astype(jnp.int32), axis=0
    )
    mem_values = None

    extra_queries = kf_queries.reshape(later, pix_dev, width)
    extra_valid = pixel_ids[None, :] < jnp.take(valid_pixels, flat_kf[keyframes:])[:, None]

    stats = []
    readout = None
    for step in range(total_steps):
        chosen = keyframe_index[step]
        key_valid = (
            jnp.arange(pix_all, dtype=jnp.int32)[None, :]
            < jnp.take(valid_pixels, chosen)[:, None]
        ).reshape(mem_width)
        key_ok = key_valid.astype(jnp.int32)[None, :]
        if step + 1 < total_steps:
            extra = extra_queries[step * keyframes:(step + 1) * keyframes].reshape(-1, width)
            extra_ok = extra_valid[step * keyframes:(step + 1) * keyframes].reshape(-1, 1)
            extra_ok = extra_ok.astype(jnp.int32)
            (part,) = step_pass(
                extra, extra_ok, extra_ok, gathered, step, key_ok, mem_values, channels, scale,
                False,
            )
            part = part.reshape(keyframes, pix_dev, channels)
            next_values = gather_all(part, "space").transpose(1, 0, 2, 3).reshape(
                mem_width, channels
            )
        ok = row_valid.astype(jnp.int32)[:, None]
        readout, col_max, col_total, col_num = step_pass(
            query_rows, ok, ok, gathered, step, key_ok, mem_values, channels, scale, True
        )
        stats.append(jnp.stack([col_max[0], col_total[0], col_num[0]]))
        if step + 1 < total_steps:
            mem_values = next_values

    local = jnp.stack(stats).reshape(total_steps, 3, keyframes, n_space, pix_dev)
    local = local.transpose(3, 1, 0, 2, 4)
    spread = lax.all_to_all(local, "space", 0, 0, tiled=True)
    m, t, n = merge_stats(spread[:, 0], spread[:, 1], spread[:, 2], 0)
    m, col_total, col_num = reduce_tm(m, t, n, "tm")

    all_count = jnp.sum(counts, axis=1)
    own_ids = kf_class.reshape(total_steps, keyframes, pix_dev)
    own = jnp.sum(
        jnp.where(own_ids[..., None] == class_range, counts[:, None, None, :], 0), axis=3
    )
    own_valid = kf_ok.reshape(total_steps, keyframes, pix_dev)
    own_safe = jnp.where(own_valid, own, 1)
    factor = jnp.sqrt(
        all_count[:, None, None].astype(jnp.float32) / (channels * own_safe.astype(jnp.float32))
    )
    confidences = jnp.where(own_valid, col_num / col_total * factor, 0.0)
    return (readout.reshape(fr_dev, pix_dev, channels), confidences)


def solution(mesh):
    placed = (
        P("tm", "space", None),
        P("tm", "space", None),
        P("tm", "space", None),
        P(None, "space"),
        P(),
        P(),
    )
    return jax.shard_map(
        body,
        mesh=mesh,
        in_specs=placed,
        out_specs=(P("tm", "space", None), P(None, None, "space")),
        check_vma=False,
    )
```

```python
import functools
import math

import jax
import jax.numpy as jnp
from jax import lax
from jax.experimental import pallas as pl
from jax.experimental.pallas import tpu as pltpu
from jax.sharding import PartitionSpec as P

LOWEST = -1e30
NEAR_TM = 4


def broadcast_tm(value, owner, axis, inner):
    size = lax.axis_size(axis)
    me = lax.axis_index(axis)
    rounds = inner.bit_length() - 1
    assert (1 << rounds) == inner and size % inner == 0
    for r in range(rounds):
        bit = 1 << r
        pairs = [(i, i ^ bit) for i in range(size)]
        got = lax.ppermute(value, axis, pairs)
        take = ((me ^ owner) % inner >> r) == 1
        value = jnp.where(take[:, None], got, value)
    groups = size // inner
    rel = (me // inner - owner // inner) % groups
    ahead = [(i, (i + inner) % size) for i in range(size)]
    behind = [(i, (i - inner) % size) for i in range(size)]
    half = value.shape[0] // 2
    for k in range(1, groups // 2 + 1):
        if 2 * k == groups:
            got_a = lax.ppermute(value[:half], axis, ahead)
            got_b = lax.ppermute(value[half:], axis, behind)
            got = jnp.concatenate([got_a, got_b], axis=0)
            value = jnp.where((rel == k)[:, None], got, value)
        else:
            got_a = lax.ppermute(value, axis, ahead)
            got_b = lax.ppermute(value, axis, behind)
            value = jnp.where((rel == k)[:, None], got_a, value)
            value = jnp.where((rel == groups - k)[:, None], got_b, value)
    return value


def gather_all(value, axis):
    size = lax.axis_size(axis)
    spread = jnp.broadcast_to(value[None], (size,) + value.shape)
    return lax.all_to_all(spread, axis, 0, 0, tiled=True)


def merge_stats(col_max, col_total, col_num, axis):
    top = jnp.max(col_max, axis=axis, keepdims=True)
    keep = jnp.exp(col_max - top)
    total = jnp.sum(col_total * keep, axis=axis)
    num = jnp.sum(col_num * keep, axis=axis)
    return jnp.squeeze(top, axis), total, num


BLOCK_ROWS = 512


def step_kernel(q_ref, row_ok_ref, col_ok_ref, keys_ref, key_ok_ref, aux_ref, *refs,
                scale, step, with_stats, channels, values_from_aux):
    if values_from_aux:
        values = aux_ref[:, :channels]
        out_refs = refs
    else:
        values = refs[0][...]
        out_refs = refs[1:]
    scores = lax.dot_general(
        q_ref[...], keys_ref[...], (((1,), (1,)), ((), ())), preferred_element_type=jnp.float32
    ) * scale
    key_ok = key_ok_ref[...] != 0
    row_ok = row_ok_ref[...] != 0
    masked = jnp.where(key_ok, scores, LOWEST)
    row_max = jnp.max(masked, axis=1, keepdims=True)
    weights = jnp.exp(masked - row_max)
    total = jnp.sum(weights, axis=1, keepdims=True)
    mixed = jnp.dot(
        weights.astype(jnp.bfloat16), values, preferred_element_type=jnp.float32
    ) / total
    out = jnp.where(row_ok, mixed, 0.0).astype(jnp.bfloat16)
    out_refs[0][...] = out
    if not with_stats:
        return
    cmax_ref, ctot_ref, cnum_ref, onehot_ref = out_refs[1:]

    @pl.when(pl.program_id(0) == 0)
    def _():
        cmax_ref[...] = jnp.full_like(cmax_ref, LOWEST)
        ctot_ref[...] = jnp.zeros_like(ctot_ref)
        cnum_ref[...] = jnp.zeros_like(cnum_ref)
        ids = aux_ref[:, channels + step:channels + step + 1].astype(jnp.float32)
        classes = lax.broadcasted_iota(jnp.int32, (1, channels), 1).astype(jnp.float32)
        onehot = (ids == classes).astype(jnp.float32)
        onehot_ref[...] = jnp.transpose(onehot).astype(jnp.bfloat16)

    picked = jnp.dot(out, onehot_ref[...], preferred_element_type=jnp.float32)
    col_ok = col_ok_ref[...] != 0
    old_max = cmax_ref[...]
    col_scores = jnp.where(col_ok, scores, LOWEST)
    local = jnp.max(col_scores, axis=0, keepdims=True)
    new_max = jnp.maximum(old_max, local)
    keep = jnp.exp(old_max - new_max)
    expo = jnp.exp(col_scores - new_max)
    ctot_ref[...] = ctot_ref[...] * keep + jnp.sum(expo, axis=0, keepdims=True)
    cnum_ref[...] = cnum_ref[...] * keep + jnp.sum(expo * picked, axis=0, keepdims=True)
    cmax_ref[...] = new_max


def step_pass(q, row_ok, col_ok, gathered, step, key_ok, mem_values, channels, scale, with_stats):
    rows, width = q.shape
    parts, mem, _ = gathered.shape
    block = min(BLOCK_ROWS, rows)
    assert rows % block == 0
    blocks = rows // block
    whole = lambda shape: pl.BlockSpec(shape, lambda i: (0, 0))
    by_row = lambda cols: pl.BlockSpec((block, cols), lambda i: (i, 0))
    stat = jax.ShapeDtypeStruct((1, mem), jnp.float32)
    out_specs = [by_row(channels)]
    out_shape = [jax.ShapeDtypeStruct((rows, channels), jnp.bfloat16)]
    if with_stats:
        out_specs += [whole((1, mem))] * 3
        out_shape += [stat] * 3
    in_specs = [
        by_row(width), by_row(1), by_row(1),
        pl.BlockSpec((None, mem, width), lambda i: (step, 0, 0)),
        whole((1, mem)),
        pl.BlockSpec((None, mem, 128), lambda i: (parts - 1, 0, 0)),
    ]
    args = [q, row_ok, col_ok, gathered, key_ok, gathered]
    if mem_values is not None:
        in_specs.append(whole((mem, channels)))
        args.append(mem_values)
    kernel = functools.partial(
        step_kernel, scale=scale, step=step, with_stats=with_stats, channels=channels,
        values_from_aux=mem_values is None,
    )
    return pl.pallas_call(
        kernel,
        grid=(blocks,),
        in_specs=in_specs,
        out_specs=out_specs,
        out_shape=out_shape,
        scratch_shapes=[pltpu.VMEM((channels, mem), jnp.bfloat16)] if with_stats else [],
        compiler_params=pltpu.CompilerParams(dimension_semantics=("arbitrary",)),
    )(*args)


def body(queries, keys, label_values, class_ids, valid_pixels, keyframe_index):
    fr_dev, pix_dev, width = queries.shape
    channels = label_values.shape[2]
    total_steps, keyframes = keyframe_index.shape
    n_space = lax.axis_size("space")
    pix_all = pix_dev * n_space
    mem_width = keyframes * pix_all
    time_pos = lax.axis_index("tm")
    space_pos = lax.axis_index("space")
    rows = fr_dev * pix_dev
    scale = 3.0 / math.sqrt(width)
    class_range = jnp.arange(channels, dtype=jnp.int32)

    frame_valid = lax.dynamic_slice_in_dim(valid_pixels, time_pos * fr_dev, fr_dev)
    pixel_ids = space_pos * pix_dev + jnp.arange(pix_dev, dtype=jnp.int32)
    row_valid = (pixel_ids[None, :] < frame_valid[:, None]).reshape(rows)
    query_rows = queries.reshape(rows, width)

    flat_kf = keyframe_index.reshape(-1)
    owners = flat_kf // fr_dev
    slots = flat_kf % fr_dev
    later = keyframes * (total_steps - 1)

    kf_keys = jnp.take(keys, slots, axis=0)
    kf_values = jnp.take(label_values, slots[:keyframes], axis=0)
    kf_queries = jnp.take(queries, slots[keyframes:], axis=0)
    parts = [kf_keys, kf_queries, kf_values]
    part_owners = [owners, owners[keyframes:], owners[:keyframes]]
    flat = jnp.concatenate([p.reshape(-1, width) for p in parts], axis=0)
    row_owner = jnp.concatenate(
        [jnp.repeat(o, p[0].size // width) for p, o in zip(parts, part_owners)]
    )
    flat = broadcast_tm(flat, row_owner, "tm", NEAR_TM)
    sizes = [p.size // width for p in parts]
    kf_keys = flat[:sizes[0]].reshape(kf_keys.shape)
    kf_queries = flat[sizes[0]:sizes[0] + sizes[1]].reshape(kf_queries.shape)
    kf_values = flat[sizes[0] + sizes[1]:].reshape(kf_values.shape)

    kf_class = jnp.take(class_ids, flat_kf, axis=0)
    kf_ok = pixel_ids[None, :] < jnp.take(valid_pixels, flat_kf)[:, None]
    hits = (kf_class[:, :, None] == class_range[None, None, :]) & kf_ok[:, :, None]
    partial = jnp.sum(hits.astype(jnp.int32), axis=1).reshape(total_steps, keyframes, channels)
    partial = jnp.sum(partial, axis=1).astype(jnp.bfloat16)
    kf_ids = kf_class.astype(jnp.bfloat16)
    kf_ids = kf_ids.reshape(total_steps, keyframes, pix_dev).transpose(1, 2, 0)
    step_keys = kf_keys.reshape(total_steps, keyframes, pix_dev, width)
    aux = jnp.concatenate([kf_values, kf_ids], axis=2)
    aux = jnp.pad(aux, ((0, 0), (0, 0), (0, 128 - aux.shape[2])))
    tally = jnp.zeros((keyframes, pix_dev, width - 128), jnp.bfloat16)
    tally = tally.at[0, :total_steps, :channels].set(partial)
    aux = jnp.concatenate([aux, tally], axis=2)
    packed = jnp.concatenate([step_keys, aux[None]], axis=0)
    gathered = lax.all_gather(packed, "space", axis=2, tiled=True)
    gathered = gathered.reshape(total_steps + 1, mem_width, width)
    tallies = gathered[total_steps].reshape(keyframes, n_space, pix_dev, width)
    counts = jnp.sum(
        tallies[0, :, :total_steps, 128:128 + channels].astype(jnp.int32), axis=0
    )
    mem_values = None

    extra_queries = kf_queries.reshape(later, pix_dev, width)
    extra_valid = pixel_ids[None, :] < jnp.take(valid_pixels, flat_kf[keyframes:])[:, None]

    stats = []
    readout = None
    for step in range(total_steps):
        chosen = keyframe_index[step]
        key_valid = (
            jnp.arange(pix_all, dtype=jnp.int32)[None, :]
            < jnp.take(valid_pixels, chosen)[:, None]
        ).reshape(mem_width)
        key_ok = key_valid.astype(jnp.int32)[None, :]
        if step + 1 < total_steps:
            extra = extra_queries[step * keyframes:(step + 1) * keyframes].reshape(-1, width)
            extra_ok = extra_valid[step * keyframes:(step + 1) * keyframes].reshape(-1, 1)
            extra_ok = extra_ok.astype(jnp.int32)
            (part,) = step_pass(
                extra, extra_ok, extra_ok, gathered, step, key_ok, mem_values, channels, scale,
                False,
            )
            part = part.reshape(keyframes, pix_dev, channels)
            next_values = gather_all(part, "space").transpose(1, 0, 2, 3).reshape(
                mem_width, channels
            )
        ok = row_valid.astype(jnp.int32)[:, None]
        readout, col_max, col_total, col_num = step_pass(
            query_rows, ok, ok, gathered, step, key_ok, mem_values, channels, scale, True
        )
        stats.append(jnp.stack([col_max[0], col_total[0], col_num[0]]))
        if step + 1 < total_steps:
            mem_values = next_values

    local = jnp.stack(stats).reshape(total_steps, 3, keyframes, n_space, pix_dev)
    local = local.transpose(3, 1, 0, 2, 4)
    spread = lax.all_to_all(local, "space", 0, 0, tiled=True)
    m, t, n = merge_stats(spread[:, 0], spread[:, 1], spread[:, 2], 0)
    joined = gather_all(jnp.stack([m, t, n]), "tm")
    m, col_total, col_num = merge_stats(joined[:, 0], joined[:, 1], joined[:, 2], 0)

    all_count = jnp.sum(counts, axis=1)
    own_ids = kf_class.reshape(total_steps, keyframes, pix_dev)
    own = jnp.sum(
        jnp.where(own_ids[..., None] == class_range, counts[:, None, None, :], 0), axis=3
    )
    own_valid = kf_ok.reshape(total_steps, keyframes, pix_dev)
    own_safe = jnp.where(own_valid, own, 1)
    factor = jnp.sqrt(
        all_count[:, None, None].astype(jnp.float32) / (channels * own_safe.astype(jnp.float32))
    )
    confidences = jnp.where(own_valid, col_num / col_total * factor, 0.0)
    return (readout.reshape(fr_dev, pix_dev, channels), confidences)


def solution(mesh):
    placed = (
        P("tm", "space", None),
        P("tm", "space", None),
        P("tm", "space", None),
        P(None, "space"),
        P(),
        P(),
    )
    return jax.shard_map(
        body,
        mesh=mesh,
        in_specs=placed,
        out_specs=(P("tm", "space", None), P(None, None, "space")),
        check_vma=False,
    )
```

```python
import functools
import math

import jax
import jax.numpy as jnp
from jax import lax
from jax.experimental import pallas as pl
from jax.experimental.pallas import tpu as pltpu
from jax.sharding import PartitionSpec as P

LOWEST = -1e30
NEAR_TM = 4


def broadcast_tm(value, owner, axis, inner):
    size = lax.axis_size(axis)
    me = lax.axis_index(axis)
    rounds = inner.bit_length() - 1
    assert (1 << rounds) == inner and size % inner == 0
    for r in range(rounds):
        bit = 1 << r
        pairs = [(i, i ^ bit) for i in range(size)]
        got = lax.ppermute(value, axis, pairs)
        take = ((me ^ owner) % inner >> r) == 1
        value = jnp.where(take[:, None], got, value)
    groups = size // inner
    rel = (me // inner - owner // inner) % groups
    ahead = [(i, (i + inner) % size) for i in range(size)]
    behind = [(i, (i - inner) % size) for i in range(size)]
    half = value.shape[0] // 2
    for k in range(1, groups // 2 + 1):
        if 2 * k == groups:
            got_a = lax.ppermute(value[:half], axis, ahead)
            got_b = lax.ppermute(value[half:], axis, behind)
            got = jnp.concatenate([got_a, got_b], axis=0)
            value = jnp.where((rel == k)[:, None], got, value)
        else:
            got_a = lax.ppermute(value, axis, ahead)
            got_b = lax.ppermute(value, axis, behind)
            value = jnp.where((rel == k)[:, None], got_a, value)
            value = jnp.where((rel == groups - k)[:, None], got_b, value)
    return value


def gather_all(value, axis):
    size = lax.axis_size(axis)
    spread = jnp.broadcast_to(value[None], (size,) + value.shape)
    return lax.all_to_all(spread, axis, 0, 0, tiled=True)


def merge_stats(col_max, col_total, col_num, axis):
    top = jnp.max(col_max, axis=axis, keepdims=True)
    keep = jnp.exp(col_max - top)
    total = jnp.sum(col_total * keep, axis=axis)
    num = jnp.sum(col_num * keep, axis=axis)
    return jnp.squeeze(top, axis), total, num


BLOCK_ROWS = 512


def step_kernel(q_ref, row_ok_ref, col_ok_ref, keys_ref, key_ok_ref, aux_ref, *refs,
                scale, step, with_stats, channels, values_from_aux):
    if values_from_aux:
        values = aux_ref[:, :channels]
        out_refs = refs
    else:
        values = refs[0][...]
        out_refs = refs[1:]
    scores = lax.dot_general(
        q_ref[...], keys_ref[...], (((1,), (1,)), ((), ())), preferred_element_type=jnp.float32
    ) * scale
    key_ok = key_ok_ref[...] != 0
    row_ok = row_ok_ref[...] != 0
    masked = jnp.where(key_ok, scores, LOWEST)
    row_max = jnp.max(masked, axis=1, keepdims=True)
    weights = jnp.exp(masked - row_max)
    total = jnp.sum(weights, axis=1, keepdims=True)
    mixed = jnp.dot(
        weights.astype(jnp.bfloat16), values, preferred_element_type=jnp.float32
    ) / total
    out = jnp.where(row_ok, mixed, 0.0).astype(jnp.bfloat16)
    out_refs[0][...] = out
    if not with_stats:
        return
    cmax_ref, ctot_ref, cnum_ref, onehot_ref = out_refs[1:]

    @pl.when(pl.program_id(0) == 0)
    def _():
        cmax_ref[...] = jnp.full_like(cmax_ref, LOWEST)
        ctot_ref[...] = jnp.zeros_like(ctot_ref)
        cnum_ref[...] = jnp.zeros_like(cnum_ref)
        ids = aux_ref[:, channels + step:channels + step + 1].astype(jnp.float32)
        classes = lax.broadcasted_iota(jnp.int32, (1, channels), 1).astype(jnp.float32)
        onehot = (ids == classes).astype(jnp.float32)
        onehot_ref[...] = jnp.transpose(onehot).astype(jnp.bfloat16)

    picked = jnp.dot(out, onehot_ref[...], preferred_element_type=jnp.float32)
    col_ok = col_ok_ref[...] != 0
    old_max = cmax_ref[...]
    col_scores = jnp.where(col_ok, scores, LOWEST)
    local = jnp.max(col_scores, axis=0, keepdims=True)
    new_max = jnp.maximum(old_max, local)
    keep = jnp.exp(old_max - new_max)
    expo = jnp.exp(col_scores - new_max)
    ctot_ref[...] = ctot_ref[...] * keep + jnp.sum(expo, axis=0, keepdims=True)
    cnum_ref[...] = cnum_ref[...] * keep + jnp.sum(expo * picked, axis=0, keepdims=True)
    cmax_ref[...] = new_max


def step_pass(q, row_ok, col_ok, gathered, step, key_ok, mem_values, channels, scale, with_stats):
    rows, width = q.shape
    parts, mem, _ = gathered.shape
    block = min(BLOCK_ROWS, rows)
    assert rows % block == 0
    blocks = rows // block
    whole = lambda shape: pl.BlockSpec(shape, lambda i: (0, 0))
    by_row = lambda cols: pl.BlockSpec((block, cols), lambda i: (i, 0))
    stat = jax.ShapeDtypeStruct((1, mem), jnp.float32)
    out_specs = [by_row(channels)]
    out_shape = [jax.ShapeDtypeStruct((rows, channels), jnp.bfloat16)]
    if with_stats:
        out_specs += [whole((1, mem))] * 3
        out_shape += [stat] * 3
    in_specs = [
        by_row(width), by_row(1), by_row(1),
        pl.BlockSpec((None, mem, width), lambda i: (step, 0, 0)),
        whole((1, mem)),
        pl.BlockSpec((None, mem, 128), lambda i: (parts - 1, 0, 0)),
    ]
    args = [q, row_ok, col_ok, gathered, key_ok, gathered]
    if mem_values is not None:
        in_specs.append(whole((mem, channels)))
        args.append(mem_values)
    kernel = functools.partial(
        step_kernel, scale=scale, step=step, with_stats=with_stats, channels=channels,
        values_from_aux=mem_values is None,
    )
    return pl.pallas_call(
        kernel,
        grid=(blocks,),
        in_specs=in_specs,
        out_specs=out_specs,
        out_shape=out_shape,
        scratch_shapes=[pltpu.VMEM((channels, mem), jnp.bfloat16)] if with_stats else [],
        compiler_params=pltpu.CompilerParams(dimension_semantics=("arbitrary",)),
    )(*args)


def body(queries, keys, label_values, class_ids, valid_pixels, keyframe_index):
    fr_dev, pix_dev, width = queries.shape
    channels = label_values.shape[2]
    total_steps, keyframes = keyframe_index.shape
    n_space = lax.axis_size("space")
    pix_all = pix_dev * n_space
    mem_width = keyframes * pix_all
    time_pos = lax.axis_index("tm")
    space_pos = lax.axis_index("space")
    rows = fr_dev * pix_dev
    scale = 3.0 / math.sqrt(width)
    class_range = jnp.arange(channels, dtype=jnp.int32)

    frame_valid = lax.dynamic_slice_in_dim(valid_pixels, time_pos * fr_dev, fr_dev)
    pixel_ids = space_pos * pix_dev + jnp.arange(pix_dev, dtype=jnp.int32)
    row_valid = (pixel_ids[None, :] < frame_valid[:, None]).reshape(rows)
    query_rows = queries.reshape(rows, width)

    flat_kf = keyframe_index.reshape(-1)
    owners = flat_kf // fr_dev
    slots = flat_kf % fr_dev
    later = keyframes * (total_steps - 1)

    kf_keys = jnp.take(keys, slots, axis=0)
    kf_values = jnp.take(label_values, slots[:keyframes], axis=0)
    kf_queries = jnp.take(queries, slots[keyframes:], axis=0)
    parts = [kf_keys, kf_queries, kf_values]
    part_owners = [owners, owners[keyframes:], owners[:keyframes]]
    flat = jnp.concatenate([p.reshape(-1, width) for p in parts], axis=0)
    row_owner = jnp.concatenate(
        [jnp.repeat(o, p[0].size // width) for p, o in zip(parts, part_owners)]
    )
    flat = broadcast_tm(flat, row_owner, "tm", NEAR_TM)
    sizes = [p.size // width for p in parts]
    kf_keys = flat[:sizes[0]].reshape(kf_keys.shape)
    kf_queries = flat[sizes[0]:sizes[0] + sizes[1]].reshape(kf_queries.shape)
    kf_values = flat[sizes[0] + sizes[1]:].reshape(kf_values.shape)

    kf_class = jnp.take(class_ids, flat_kf, axis=0)
    kf_ok = pixel_ids[None, :] < jnp.take(valid_pixels, flat_kf)[:, None]
    hits = (kf_class[:, :, None] == class_range[None, None, :]) & kf_ok[:, :, None]
    partial = jnp.sum(hits.astype(jnp.int32), axis=1).reshape(total_steps, keyframes, channels)
    partial = jnp.sum(partial, axis=1).astype(jnp.bfloat16)
    kf_ids = kf_class.astype(jnp.bfloat16)
    kf_ids = kf_ids.reshape(total_steps, keyframes, pix_dev).transpose(1, 2, 0)
    step_keys = kf_keys.reshape(total_steps, keyframes, pix_dev, width)
    aux = jnp.concatenate([kf_values, kf_ids], axis=2)
    aux = jnp.pad(aux, ((0, 0), (0, 0), (0, 128 - aux.shape[2])))
    tally = jnp.zeros((keyframes, pix_dev, width - 128), jnp.bfloat16)
    tally = tally.at[0, :total_steps, :channels].set(partial)
    aux = jnp.concatenate([aux, tally], axis=2)
    packed = jnp.concatenate([step_keys, aux[None]], axis=0)
    gathered = lax.all_gather(packed, "space", axis=2, tiled=True)
    gathered = gathered.reshape(total_steps + 1, mem_width, width)
    tallies = gathered[total_steps].reshape(keyframes, n_space, pix_dev, width)
    counts = jnp.sum(
        tallies[0, :, :total_steps, 128:128 + channels].astype(jnp.int32), axis=0
    )
    mem_values = None

    extra_queries = kf_queries.reshape(later, pix_dev, width)
    extra_valid = pixel_ids[None, :] < jnp.take(valid_pixels, flat_kf[keyframes:])[:, None]

    stats = []
    readout = None
    for step in range(total_steps):
        chosen = keyframe_index[step]
        key_valid = (
            jnp.arange(pix_all, dtype=jnp.int32)[None, :]
            < jnp.take(valid_pixels, chosen)[:, None]
        ).reshape(mem_width)
        key_ok = key_valid.astype(jnp.int32)[None, :]
        if step + 1 < total_steps:
            extra = extra_queries[step * keyframes:(step + 1) * keyframes].reshape(-1, width)
            extra_ok = extra_valid[step * keyframes:(step + 1) * keyframes].reshape(-1, 1)
            extra_ok = extra_ok.astype(jnp.int32)
            (part,) = step_pass(
                extra, extra_ok, extra_ok, gathered, step, key_ok, mem_values, channels, scale,
                False,
            )
            part = part.reshape(keyframes, pix_dev * channels)
            next_values = gather_all(part, "space").reshape(
                n_space, keyframes, pix_dev, channels
            ).transpose(1, 0, 2, 3).reshape(mem_width, channels)
        ok = row_valid.astype(jnp.int32)[:, None]
        readout, col_max, col_total, col_num = step_pass(
            query_rows, ok, ok, gathered, step, key_ok, mem_values, channels, scale, True
        )
        stats.append(jnp.stack([col_max[0], col_total[0], col_num[0]]))
        if step + 1 < total_steps:
            mem_values = next_values

    local = jnp.stack(stats).reshape(total_steps, 3, keyframes, n_space, pix_dev)
    local = local.transpose(3, 1, 0, 2, 4)
    spread = lax.all_to_all(local, "space", 0, 0, tiled=True)
    m, t, n = merge_stats(spread[:, 0], spread[:, 1], spread[:, 2], 0)
    joined = gather_all(jnp.stack([m, t, n]), "tm")
    m, col_total, col_num = merge_stats(joined[:, 0], joined[:, 1], joined[:, 2], 0)

    all_count = jnp.sum(counts, axis=1)
    own_ids = kf_class.reshape(total_steps, keyframes, pix_dev)
    own = jnp.sum(
        jnp.where(own_ids[..., None] == class_range, counts[:, None, None, :], 0), axis=3
    )
    own_valid = kf_ok.reshape(total_steps, keyframes, pix_dev)
    own_safe = jnp.where(own_valid, own, 1)
    factor = jnp.sqrt(
        all_count[:, None, None].astype(jnp.float32) / (channels * own_safe.astype(jnp.float32))
    )
    confidences = jnp.where(own_valid, col_num / col_total * factor, 0.0)
    return (readout.reshape(fr_dev, pix_dev, channels), confidences)


def solution(mesh):
    placed = (
        P("tm", "space", None),
        P("tm", "space", None),
        P("tm", "space", None),
        P(None, "space"),
        P(),
        P(),
    )
    return jax.shard_map(
        body,
        mesh=mesh,
        in_specs=placed,
        out_specs=(P("tm", "space", None), P(None, None, "space")),
        check_vma=False,
    )
```

```python
import functools
import math

import jax
import jax.numpy as jnp
from jax import lax
from jax.experimental import pallas as pl
from jax.experimental.pallas import tpu as pltpu
from jax.sharding import PartitionSpec as P

LOWEST = -1e30
NEAR_TM = 4


def broadcast_tm(value, owner, axis, inner):
    size = lax.axis_size(axis)
    me = lax.axis_index(axis)
    rounds = inner.bit_length() - 1
    assert (1 << rounds) == inner and size % inner == 0
    for r in range(rounds):
        bit = 1 << r
        pairs = [(i, i ^ bit) for i in range(size)]
        got = lax.ppermute(value, axis, pairs)
        take = ((me ^ owner) % inner >> r) == 1
        value = jnp.where(take[:, None], got, value)
    groups = size // inner
    rel = (me // inner - owner // inner) % groups
    ahead = [(i, (i + inner) % size) for i in range(size)]
    behind = [(i, (i - inner) % size) for i in range(size)]
    half = value.shape[0] // 2
    for k in range(1, groups // 2 + 1):
        if 2 * k == groups:
            got_a = lax.ppermute(value[:half], axis, ahead)
            got_b = lax.ppermute(value[half:], axis, behind)
            got = jnp.concatenate([got_a, got_b], axis=0)
            value = jnp.where((rel == k)[:, None], got, value)
        else:
            got_a = lax.ppermute(value, axis, ahead)
            got_b = lax.ppermute(value, axis, behind)
            value = jnp.where((rel == k)[:, None], got_a, value)
            value = jnp.where((rel == groups - k)[:, None], got_b, value)
    return value


def gather_all(value, axis):
    size = lax.axis_size(axis)
    spread = jnp.broadcast_to(value[None], (size,) + value.shape)
    return lax.all_to_all(spread, axis, 0, 0, tiled=True)


def merge_stats(col_max, col_total, col_num, axis):
    top = jnp.max(col_max, axis=axis, keepdims=True)
    keep = jnp.exp(col_max - top)
    total = jnp.sum(col_total * keep, axis=axis)
    num = jnp.sum(col_num * keep, axis=axis)
    return jnp.squeeze(top, axis), total, num


BLOCK_ROWS = 512


def step_kernel(q_ref, row_ok_ref, col_ok_ref, keys_ref, key_ok_ref, aux_ref, *refs,
                scale, step, with_stats, channels, values_from_aux):
    if values_from_aux:
        values = aux_ref[:, :channels]
        out_refs = refs
    else:
        values = refs[0][...]
        out_refs = refs[1:]
    scores = lax.dot_general(
        q_ref[...], keys_ref[...], (((1,), (1,)), ((), ())), preferred_element_type=jnp.float32
    ) * scale
    key_ok = key_ok_ref[...] != 0
    row_ok = row_ok_ref[...] != 0
    masked = jnp.where(key_ok, scores, LOWEST)
    row_max = jnp.max(masked, axis=1, keepdims=True)
    weights = jnp.exp(masked - row_max)
    total = jnp.sum(weights, axis=1, keepdims=True)
    mixed = jnp.dot(
        weights.astype(jnp.bfloat16), values, preferred_element_type=jnp.float32
    ) / total
    out = jnp.where(row_ok, mixed, 0.0).astype(jnp.bfloat16)
    out_refs[0][...] = out
    if not with_stats:
        return
    cmax_ref, ctot_ref, cnum_ref, onehot_ref = out_refs[1:]

    @pl.when(pl.program_id(0) == 0)
    def _():
        cmax_ref[...] = jnp.full_like(cmax_ref, LOWEST)
        ctot_ref[...] = jnp.zeros_like(ctot_ref)
        cnum_ref[...] = jnp.zeros_like(cnum_ref)
        ids = aux_ref[:, channels + step:channels + step + 1].astype(jnp.float32)
        classes = lax.broadcasted_iota(jnp.int32, (1, channels), 1).astype(jnp.float32)
        onehot = (ids == classes).astype(jnp.float32)
        onehot_ref[...] = jnp.transpose(onehot).astype(jnp.bfloat16)

    picked = jnp.dot(out, onehot_ref[...], preferred_element_type=jnp.float32)
    col_ok = col_ok_ref[...] != 0
    old_max = cmax_ref[...]
    col_scores = jnp.where(col_ok, scores, LOWEST)
    local = jnp.max(col_scores, axis=0, keepdims=True)
    new_max = jnp.maximum(old_max, local)
    keep = jnp.exp(old_max - new_max)
    expo = jnp.exp(col_scores - new_max)
    ctot_ref[...] = ctot_ref[...] * keep + jnp.sum(expo, axis=0, keepdims=True)
    cnum_ref[...] = cnum_ref[...] * keep + jnp.sum(expo * picked, axis=0, keepdims=True)
    cmax_ref[...] = new_max


def step_pass(q, row_ok, col_ok, gathered, step, key_ok, mem_values, channels, scale, with_stats):
    rows, width = q.shape
    parts, mem, _ = gathered.shape
    block = min(BLOCK_ROWS, rows)
    assert rows % block == 0
    blocks = rows // block
    whole = lambda shape: pl.BlockSpec(shape, lambda i: (0, 0))
    by_row = lambda cols: pl.BlockSpec((block, cols), lambda i: (i, 0))
    stat = jax.ShapeDtypeStruct((1, mem), jnp.float32)
    out_specs = [by_row(channels)]
    out_shape = [jax.ShapeDtypeStruct((rows, channels), jnp.bfloat16)]
    if with_stats:
        out_specs += [whole((1, mem))] * 3
        out_shape += [stat] * 3
    in_specs = [
        by_row(width), by_row(1), by_row(1),
        pl.BlockSpec((None, mem, width), lambda i: (step, 0, 0)),
        whole((1, mem)),
        pl.BlockSpec((None, mem, 128), lambda i: (parts - 1, 0, 0)),
    ]
    args = [q, row_ok, col_ok, gathered, key_ok, gathered]
    if mem_values is not None:
        in_specs.append(whole((mem, channels)))
        args.append(mem_values)
    kernel = functools.partial(
        step_kernel, scale=scale, step=step, with_stats=with_stats, channels=channels,
        values_from_aux=mem_values is None,
    )
    return pl.pallas_call(
        kernel,
        grid=(blocks,),
        in_specs=in_specs,
        out_specs=out_specs,
        out_shape=out_shape,
        scratch_shapes=[pltpu.VMEM((channels, mem), jnp.bfloat16)] if with_stats else [],
        compiler_params=pltpu.CompilerParams(dimension_semantics=("arbitrary",)),
    )(*args)


def body(queries, keys, label_values, class_ids, valid_pixels, keyframe_index):
    fr_dev, pix_dev, width = queries.shape
    channels = label_values.shape[2]
    total_steps, keyframes = keyframe_index.shape
    n_space = lax.axis_size("space")
    pix_all = pix_dev * n_space
    mem_width = keyframes * pix_all
    time_pos = lax.axis_index("tm")
    space_pos = lax.axis_index("space")
    rows = fr_dev * pix_dev
    scale = 3.0 / math.sqrt(width)
    class_range = jnp.arange(channels, dtype=jnp.int32)

    frame_valid = lax.dynamic_slice_in_dim(valid_pixels, time_pos * fr_dev, fr_dev)
    pixel_ids = space_pos * pix_dev + jnp.arange(pix_dev, dtype=jnp.int32)
    row_valid = (pixel_ids[None, :] < frame_valid[:, None]).reshape(rows)
    query_rows = queries.reshape(rows, width)

    flat_kf = keyframe_index.reshape(-1)
    owners = flat_kf // fr_dev
    slots = flat_kf % fr_dev
    later = keyframes * (total_steps - 1)

    pick = lambda array, which: jnp.stack(
        [lax.dynamic_index_in_dim(array, w, 0, keepdims=False) for w in which]
    )
    kf_keys = pick(keys, [slots[i] for i in range(total_steps * keyframes)])
    kf_values = pick(label_values, [slots[i] for i in range(keyframes)])
    kf_queries = pick(queries, [slots[i] for i in range(keyframes, total_steps * keyframes)])
    parts = [kf_keys, kf_queries, kf_values]
    part_owners = [owners, owners[keyframes:], owners[:keyframes]]
    flat = jnp.concatenate([p.reshape(-1, width) for p in parts], axis=0)
    row_owner = jnp.concatenate(
        [jnp.repeat(o, p[0].size // width) for p, o in zip(parts, part_owners)]
    )
    flat = broadcast_tm(flat, row_owner, "tm", NEAR_TM)
    sizes = [p.size // width for p in parts]
    kf_keys = flat[:sizes[0]].reshape(kf_keys.shape)
    kf_queries = flat[sizes[0]:sizes[0] + sizes[1]].reshape(kf_queries.shape)
    kf_values = flat[sizes[0] + sizes[1]:].reshape(kf_values.shape)

    kf_class = jnp.take(class_ids, flat_kf, axis=0)
    kf_ok = pixel_ids[None, :] < jnp.take(valid_pixels, flat_kf)[:, None]
    hits = (kf_class[:, :, None] == class_range[None, None, :]) & kf_ok[:, :, None]
    partial = jnp.sum(hits.astype(jnp.int32), axis=1).reshape(total_steps, keyframes, channels)
    partial = jnp.sum(partial, axis=1).astype(jnp.bfloat16)
    kf_ids = kf_class.astype(jnp.bfloat16)
    kf_ids = kf_ids.reshape(total_steps, keyframes, pix_dev).transpose(1, 2, 0)
    step_keys = kf_keys.reshape(total_steps, keyframes, pix_dev, width)
    aux = jnp.concatenate([kf_values, kf_ids], axis=2)
    aux = jnp.pad(aux, ((0, 0), (0, 0), (0, 128 - aux.shape[2])))
    tally = jnp.zeros((keyframes, pix_dev, width - 128), jnp.bfloat16)
    tally = tally.at[0, :total_steps, :channels].set(partial)
    aux = jnp.concatenate([aux, tally], axis=2)
    packed = jnp.concatenate([step_keys, aux[None]], axis=0)
    gathered = lax.all_gather(packed, "space", axis=2, tiled=True)
    gathered = gathered.reshape(total_steps + 1, mem_width, width)
    tallies = gathered[total_steps].reshape(keyframes, n_space, pix_dev, width)
    counts = jnp.sum(
        tallies[0, :, :total_steps, 128:128 + channels].astype(jnp.int32), axis=0
    )
    mem_values = None

    extra_queries = kf_queries.reshape(later, pix_dev, width)
    extra_valid = pixel_ids[None, :] < jnp.take(valid_pixels, flat_kf[keyframes:])[:, None]

    stats = []
    readout = None
    for step in range(total_steps):
        chosen = keyframe_index[step]
        key_valid = (
            jnp.arange(pix_all, dtype=jnp.int32)[None, :]
            < jnp.take(valid_pixels, chosen)[:, None]
        ).reshape(mem_width)
        key_ok = key_valid.astype(jnp.int32)[None, :]
        if step + 1 < total_steps:
            extra = extra_queries[step * keyframes:(step + 1) * keyframes].reshape(-1, width)
            extra_ok = extra_valid[step * keyframes:(step + 1) * keyframes].reshape(-1, 1)
            extra_ok = extra_ok.astype(jnp.int32)
            (part,) = step_pass(
                extra, extra_ok, extra_ok, gathered, step, key_ok, mem_values, channels, scale,
                False,
            )
            part = part.reshape(keyframes, pix_dev, channels)
            next_values = gather_all(part, "space").transpose(1, 0, 2, 3).reshape(
                mem_width, channels
            )
        ok = row_valid.astype(jnp.int32)[:, None]
        readout, col_max, col_total, col_num = step_pass(
            query_rows, ok, ok, gathered, step, key_ok, mem_values, channels, scale, True
        )
        stats.append(jnp.stack([col_max[0], col_total[0], col_num[0]]))
        if step + 1 < total_steps:
            mem_values = next_values

    local = jnp.stack(stats).reshape(total_steps, 3, keyframes, n_space, pix_dev)
    local = local.transpose(3, 1, 0, 2, 4)
    spread = lax.all_to_all(local, "space", 0, 0, tiled=True)
    m, t, n = merge_stats(spread[:, 0], spread[:, 1], spread[:, 2], 0)
    joined = gather_all(jnp.stack([m, t, n]), "tm")
    m, col_total, col_num = merge_stats(joined[:, 0], joined[:, 1], joined[:, 2], 0)

    all_count = jnp.sum(counts, axis=1)
    own_ids = kf_class.reshape(total_steps, keyframes, pix_dev)
    own = jnp.sum(
        jnp.where(own_ids[..., None] == class_range, counts[:, None, None, :], 0), axis=3
    )
    own_valid = kf_ok.reshape(total_steps, keyframes, pix_dev)
    own_safe = jnp.where(own_valid, own, 1)
    factor = jnp.sqrt(
        all_count[:, None, None].astype(jnp.float32) / (channels * own_safe.astype(jnp.float32))
    )
    confidences = jnp.where(own_valid, col_num / col_total * factor, 0.0)
    return (readout.reshape(fr_dev, pix_dev, channels), confidences)


def solution(mesh):
    placed = (
        P("tm", "space", None),
        P("tm", "space", None),
        P("tm", "space", None),
        P(None, "space"),
        P(),
        P(),
    )
    return jax.shard_map(
        body,
        mesh=mesh,
        in_specs=placed,
        out_specs=(P("tm", "space", None), P(None, None, "space")),
        check_vma=False,
    )
```

```python
import functools
import math

import jax
import jax.numpy as jnp
from jax import lax
from jax.experimental import pallas as pl
from jax.experimental.pallas import tpu as pltpu
from jax.sharding import PartitionSpec as P

LOWEST = -1e30
NEAR_TM = 4


def broadcast_tm(value, owner, axis, inner):
    size = lax.axis_size(axis)
    me = lax.axis_index(axis)
    rounds = inner.bit_length() - 1
    assert (1 << rounds) == inner and size % inner == 0
    for r in range(rounds):
        bit = 1 << r
        pairs = [(i, i ^ bit) for i in range(size)]
        got = lax.ppermute(value, axis, pairs)
        take = ((me ^ owner) % inner >> r) == 1
        value = jnp.where(take[:, None], got, value)
    groups = size // inner
    rel = (me // inner - owner // inner) % groups
    ahead = [(i, (i + inner) % size) for i in range(size)]
    behind = [(i, (i - inner) % size) for i in range(size)]
    half = value.shape[0] // 2
    for k in range(1, groups // 2 + 1):
        if 2 * k == groups:
            got_a = lax.ppermute(value[:half], axis, ahead)
            got_b = lax.ppermute(value[half:], axis, behind)
            got = jnp.concatenate([got_a, got_b], axis=0)
            value = jnp.where((rel == k)[:, None], got, value)
        else:
            got_a = lax.ppermute(value, axis, ahead)
            got_b = lax.ppermute(value, axis, behind)
            value = jnp.where((rel == k)[:, None], got_a, value)
            value = jnp.where((rel == groups - k)[:, None], got_b, value)
    return value


def gather_all(value, axis):
    size = lax.axis_size(axis)
    spread = jnp.broadcast_to(value[None], (size,) + value.shape)
    return lax.all_to_all(spread, axis, 0, 0, tiled=True)


def merge_stats(col_max, col_total, col_num, axis):
    top = jnp.max(col_max, axis=axis, keepdims=True)
    keep = jnp.exp(col_max - top)
    total = jnp.sum(col_total * keep, axis=axis)
    num = jnp.sum(col_num * keep, axis=axis)
    return jnp.squeeze(top, axis), total, num


BLOCK_ROWS = 512


def step_kernel(q_ref, row_ok_ref, keys_ref, key_ok_ref, aux_ref, *refs,
                scale, step, with_stats, channels, values_from_aux):
    if values_from_aux:
        values = aux_ref[:, :channels]
        out_refs = refs
    else:
        values = refs[0][...]
        out_refs = refs[1:]
    scores = lax.dot_general(
        q_ref[...], keys_ref[...], (((1,), (1,)), ((), ())), preferred_element_type=jnp.float32
    ) * scale
    key_ok = key_ok_ref[...] != 0
    row_ok = row_ok_ref[...] != 0
    masked = jnp.where(key_ok, scores, LOWEST)
    row_max = jnp.max(masked, axis=1, keepdims=True)
    weights = jnp.exp(masked - row_max)
    total = jnp.sum(weights, axis=1, keepdims=True)
    mixed = jnp.dot(
        weights.astype(jnp.bfloat16), values, preferred_element_type=jnp.float32
    ) / total
    out = jnp.where(row_ok, mixed, 0.0).astype(jnp.bfloat16)
    out_refs[0][...] = out
    if not with_stats:
        return
    cmax_ref, ctot_ref, cnum_ref, onehot_ref = out_refs[1:]

    @pl.when(pl.program_id(0) == 0)
    def _():
        cmax_ref[...] = jnp.full_like(cmax_ref, LOWEST)
        ctot_ref[...] = jnp.zeros_like(ctot_ref)
        cnum_ref[...] = jnp.zeros_like(cnum_ref)
        ids = aux_ref[:, channels + step:channels + step + 1].astype(jnp.float32)
        classes = lax.broadcasted_iota(jnp.int32, (1, channels), 1).astype(jnp.float32)
        onehot = (ids == classes).astype(jnp.float32)
        onehot_ref[...] = jnp.transpose(onehot).astype(jnp.bfloat16)

    picked = jnp.dot(out, onehot_ref[...], preferred_element_type=jnp.float32)
    col_ok = row_ok
    old_max = cmax_ref[...]
    col_scores = jnp.where(col_ok, scores, LOWEST)
    local = jnp.max(col_scores, axis=0, keepdims=True)
    new_max = jnp.maximum(old_max, local)
    keep = jnp.exp(old_max - new_max)
    expo = jnp.exp(col_scores - new_max)
    ctot_ref[...] = ctot_ref[...] * keep + jnp.sum(expo, axis=0, keepdims=True)
    cnum_ref[...] = cnum_ref[...] * keep + jnp.sum(expo * picked, axis=0, keepdims=True)
    cmax_ref[...] = new_max


def step_pass(q, row_ok, gathered, step, key_ok, mem_values, channels, scale, with_stats):
    rows, width = q.shape
    parts, mem, _ = gathered.shape
    block = min(BLOCK_ROWS, rows)
    assert rows % block == 0
    blocks = rows // block
    whole = lambda shape: pl.BlockSpec(shape, lambda i: (0, 0))
    by_row = lambda cols: pl.BlockSpec((block, cols), lambda i: (i, 0))
    stat = jax.ShapeDtypeStruct((1, mem), jnp.float32)
    out_specs = [by_row(channels)]
    out_shape = [jax.ShapeDtypeStruct((rows, channels), jnp.bfloat16)]
    if with_stats:
        out_specs += [whole((1, mem))] * 3
        out_shape += [stat] * 3
    in_specs = [
        by_row(width), by_row(1),
        pl.BlockSpec((None, mem, width), lambda i: (step, 0, 0)),
        whole((1, mem)),
        pl.BlockSpec((None, mem, 128), lambda i: (parts - 1, 0, 0)),
    ]
    args = [q, row_ok, gathered, key_ok, gathered]
    if mem_values is not None:
        in_specs.append(whole((mem, channels)))
        args.append(mem_values)
    kernel = functools.partial(
        step_kernel, scale=scale, step=step, with_stats=with_stats, channels=channels,
        values_from_aux=mem_values is None,
    )
    return pl.pallas_call(
        kernel,
        grid=(blocks,),
        in_specs=in_specs,
        out_specs=out_specs,
        out_shape=out_shape,
        scratch_shapes=[pltpu.VMEM((channels, mem), jnp.bfloat16)] if with_stats else [],
        compiler_params=pltpu.CompilerParams(dimension_semantics=("arbitrary",)),
    )(*args)


def body(queries, keys, label_values, class_ids, valid_pixels, keyframe_index):
    fr_dev, pix_dev, width = queries.shape
    channels = label_values.shape[2]
    total_steps, keyframes = keyframe_index.shape
    n_space = lax.axis_size("space")
    pix_all = pix_dev * n_space
    mem_width = keyframes * pix_all
    time_pos = lax.axis_index("tm")
    space_pos = lax.axis_index("space")
    rows = fr_dev * pix_dev
    scale = 3.0 / math.sqrt(width)
    class_range = jnp.arange(channels, dtype=jnp.int32)

    frame_valid = lax.dynamic_slice_in_dim(valid_pixels, time_pos * fr_dev, fr_dev)
    pixel_ids = space_pos * pix_dev + jnp.arange(pix_dev, dtype=jnp.int32)
    row_valid = (pixel_ids[None, :] < frame_valid[:, None]).reshape(rows)
    query_rows = queries.reshape(rows, width)

    flat_kf = keyframe_index.reshape(-1)
    owners = flat_kf // fr_dev
    slots = flat_kf % fr_dev
    later = keyframes * (total_steps - 1)

    kf_keys = jnp.take(keys, slots, axis=0)
    kf_values = jnp.take(label_values, slots[:keyframes], axis=0)
    kf_queries = jnp.take(queries, slots[keyframes:], axis=0)
    parts = [kf_keys, kf_queries, kf_values]
    part_owners = [owners, owners[keyframes:], owners[:keyframes]]
    flat = jnp.concatenate([p.reshape(-1, width) for p in parts], axis=0)
    row_owner = jnp.concatenate(
        [jnp.repeat(o, p[0].size // width) for p, o in zip(parts, part_owners)]
    )
    flat = broadcast_tm(flat, row_owner, "tm", NEAR_TM)
    sizes = [p.size // width for p in parts]
    kf_keys = flat[:sizes[0]].reshape(kf_keys.shape)
    kf_queries = flat[sizes[0]:sizes[0] + sizes[1]].reshape(kf_queries.shape)
    kf_values = flat[sizes[0] + sizes[1]:].reshape(kf_values.shape)

    kf_class = jnp.take(class_ids, flat_kf, axis=0)
    kf_ok = pixel_ids[None, :] < jnp.take(valid_pixels, flat_kf)[:, None]
    hits = (kf_class[:, :, None] == class_range[None, None, :]) & kf_ok[:, :, None]
    partial = jnp.sum(hits.astype(jnp.int32), axis=1).reshape(total_steps, keyframes, channels)
    partial = jnp.sum(partial, axis=1).astype(jnp.bfloat16)
    kf_ids = kf_class.astype(jnp.bfloat16)
    kf_ids = kf_ids.reshape(total_steps, keyframes, pix_dev).transpose(1, 2, 0)
    step_keys = kf_keys.reshape(total_steps, keyframes, pix_dev, width)
    aux = jnp.concatenate([kf_values, kf_ids], axis=2)
    aux = jnp.pad(aux, ((0, 0), (0, 0), (0, 128 - aux.shape[2])))
    tally = jnp.zeros((keyframes, pix_dev, width - 128), jnp.bfloat16)
    tally = tally.at[0, :total_steps, :channels].set(partial)
    aux = jnp.concatenate([aux, tally], axis=2)
    packed = jnp.concatenate([step_keys, aux[None]], axis=0)
    gathered = lax.all_gather(packed, "space", axis=2, tiled=True)
    gathered = gathered.reshape(total_steps + 1, mem_width, width)
    tallies = gathered[total_steps].reshape(keyframes, n_space, pix_dev, width)
    counts = jnp.sum(
        tallies[0, :, :total_steps, 128:128 + channels].astype(jnp.int32), axis=0
    )
    mem_values = None

    extra_queries = kf_queries.reshape(later, pix_dev, width)
    extra_valid = pixel_ids[None, :] < jnp.take(valid_pixels, flat_kf[keyframes:])[:, None]

    stats = []
    readout = None
    for step in range(total_steps):
        chosen = keyframe_index[step]
        key_valid = (
            jnp.arange(pix_all, dtype=jnp.int32)[None, :]
            < jnp.take(valid_pixels, chosen)[:, None]
        ).reshape(mem_width)
        key_ok = key_valid.astype(jnp.int32)[None, :]
        if step + 1 < total_steps:
            extra = extra_queries[step * keyframes:(step + 1) * keyframes].reshape(-1, width)
            extra_ok = extra_valid[step * keyframes:(step + 1) * keyframes].reshape(-1, 1)
            extra_ok = extra_ok.astype(jnp.int32)
            (part,) = step_pass(
                extra, extra_ok, gathered, step, key_ok, mem_values, channels, scale,
                False,
            )
            part = part.reshape(keyframes, pix_dev, channels)
            next_values = gather_all(part, "space").transpose(1, 0, 2, 3).reshape(
                mem_width, channels
            )
        ok = row_valid.astype(jnp.int32)[:, None]
        readout, col_max, col_total, col_num = step_pass(
            query_rows, ok, gathered, step, key_ok, mem_values, channels, scale, True
        )
        stats.append(jnp.stack([col_max[0], col_total[0], col_num[0]]))
        if step + 1 < total_steps:
            mem_values = next_values

    local = jnp.stack(stats).reshape(total_steps, 3, keyframes, n_space, pix_dev)
    local = local.transpose(3, 1, 0, 2, 4)
    spread = lax.all_to_all(local, "space", 0, 0, tiled=True)
    m, t, n = merge_stats(spread[:, 0], spread[:, 1], spread[:, 2], 0)
    joined = gather_all(jnp.stack([m, t, n]), "tm")
    m, col_total, col_num = merge_stats(joined[:, 0], joined[:, 1], joined[:, 2], 0)

    all_count = jnp.sum(counts, axis=1)
    own_ids = kf_class.reshape(total_steps, keyframes, pix_dev)
    own = jnp.sum(
        jnp.where(own_ids[..., None] == class_range, counts[:, None, None, :], 0), axis=3
    )
    own_valid = kf_ok.reshape(total_steps, keyframes, pix_dev)
    own_safe = jnp.where(own_valid, own, 1)
    factor = jnp.sqrt(
        all_count[:, None, None].astype(jnp.float32) / (channels * own_safe.astype(jnp.float32))
    )
    confidences = jnp.where(own_valid, col_num / col_total * factor, 0.0)
    return (readout.reshape(fr_dev, pix_dev, channels), confidences)


def solution(mesh):
    placed = (
        P("tm", "space", None),
        P("tm", "space", None),
        P("tm", "space", None),
        P(None, "space"),
        P(),
        P(),
    )
    return jax.shard_map(
        body,
        mesh=mesh,
        in_specs=placed,
        out_specs=(P("tm", "space", None), P(None, None, "space")),
        check_vma=False,
    )
```
